32 devices in a mesh: fsdp: 4 (over x, core), replica: 8 (over z, y).
Axes of the slice: x: 2, y: 2, z: 4, core: 2. Of those that a mesh axis runs over, the one named last changes fastest.
Arguments:
- hidden_in: bfloat16 [16384, 768], P(('fsdp', 'replica')), may hold values from -6 to 6
- encoder_states: bfloat16 [16384, 768], P(('fsdp', 'replica')), may hold values from -6 to 6
- output_grad: bfloat16 [16384, 768], P(('fsdp', 'replica')), may hold values from -6 to 6
- piece_starts: int32 [32, 3], P(('fsdp', 'replica')), may hold values from 0 to 384, as said below
- selfquery: bfloat16 [768, 768], P('fsdp'), may hold values from -0.0546875 to 0.0546875
- selfkey: bfloat16 [768, 768], P('fsdp'), may hold values from -0.21875 to 0.21875
- selfvalue: bfloat16 [768, 768], P('fsdp'), may hold values from -0.21875 to 0.21875
- selfproj: bfloat16 [768, 768], P('fsdp'), may hold values from -0.875 to 0.875
- crossquery: bfloat16 [768, 768], P('fsdp'), may hold values from -0.0546875 to 0.0546875
- crosskey: bfloat16 [768, 768], P('fsdp'), may hold values from -0.21875 to 0.21875
- crossvalue: bfloat16 [768, 768], P('fsdp'), may hold values from -0.21875 to 0.21875
- crossproj: bfloat16 [768, 768], P('fsdp'), may hold values from -0.875 to 0.875
- gateproj: bfloat16 [768, 2048], P('fsdp'), may hold values from -0.21875 to 0.21875
- upproj: bfloat16 [768, 2048], P('fsdp'), may hold values from -0.21875 to 0.21875
- downproj: bfloat16 [2048, 768], P('fsdp'), may hold values from -0.125 to 0.125
- gainself: bfloat16 [768], P('fsdp'), may hold values from 0.5 to 1.5
- gaincross: bfloat16 [768], P('fsdp'), may hold values from 0.5 to 1.5
- gainffn: bfloat16 [768], P('fsdp'), may hold values from 0.5 to 1.5
- reltable: bfloat16 [32, 12], P('fsdp'), may hold values from -4 to 4
Outputs:
- layer_out: bfloat16 [16384, 768], P(('fsdp', 'replica'))
- hidden_grad: float32 [16384, 768], P(('fsdp', 'replica'))
- encoder_grad: float32 [16384, 768], P(('fsdp', 'replica'))
- selfquery_grad: float32 [768, 768], P('fsdp')
- selfkey_grad: float32 [768, 768], P('fsdp')
- selfvalue_grad: float32 [768, 768], P('fsdp')
- selfproj_grad: float32 [768, 768], P('fsdp')
- crossquery_grad: float32 [768, 768], P('fsdp')
- crosskey_grad: float32 [768, 768], P('fsdp')
- crossvalue_grad: float32 [768, 768], P('fsdp')
- crossproj_grad: float32 [768, 768], P('fsdp')
- gateproj_grad: float32 [768, 2048], P('fsdp')
- upproj_grad: float32 [768, 2048], P('fsdp')
- downproj_grad: float32 [2048, 768], P('fsdp')
- gainself_grad: float32 [768], P('fsdp')
- gaincross_grad: float32 [768], P('fsdp')
- gainffn_grad: float32 [768], P('fsdp')
- reltable_grad: float32 [32, 12], P('fsdp')
The draws below stay inside these ranges and needn't reach their ends.
Inputs may be any that keep to these rules, and one draw needn't show every extreme that they name: `piece_starts`: each row holds the 3 increasing starts of one sequence's pieces, the first 0 and the last exactly 384; no piece has more than 256 tokens, and each sequence has one piece of exactly 256.
All inputs are finite; a program needn't handle non-finite values.
Results may differ from the reference program's by a relative error of at most 0.028.
The reference program's roundings to bfloat16 on the way count: a program that leaves them out, or rounds other values in their place, can miss the bound.
Values may be sent and summed in bfloat16 or wider, within the bound.
No kernel may reach another device: no remote copies, remote signals or barrier semaphores. Data moves between devices by JAX's collectives and lax.ppermute only.
A program may use at most 256 MiB of HBM per device.

```python
import jax
import jax.numpy as jnp
from jax import lax

D = 768
FF = 2048
HEADS = 12
HEAD_DIM = 64
BUCKETS = 32
PIECE = 256
SEQ = 512
ENC = 512
NSEQ = 32
TOKENS = 16384
ENC_TOK = 16384


def draw_piece_starts(key, part):
    halves = 2 * SEQ // PIECE
    half_len = PIECE // 2
    shift_reach = half_len // 4
    key_drop, key_shift = jax.random.split(jax.random.fold_in(key, 11))
    dropped = jax.random.randint(key_drop, (NSEQ, 1), 1, halves - 1)
    shifts = jax.random.randint(key_shift, (NSEQ, halves), -shift_reach, shift_reach + 1)
    column = jnp.arange(halves, dtype=jnp.int32)[None, :]
    pinned = (column == 0) | (column == halves - 1) | (column == dropped - 1) | (column == dropped + 1)
    shifts = jnp.where(pinned, 0, shifts)
    full_starts = column * half_len + shifts
    slot_index = jnp.arange(halves - 1, dtype=jnp.int32)[None, :]
    source = slot_index + (slot_index >= dropped).astype(jnp.int32)
    return jnp.take_along_axis(full_starts, source, axis=1).astype(jnp.int32)


def block_scale(stream_key, dims, pieces, low, high):
    loudness = 1.0
    for dim, shards_of in pieces:
        heights = jax.random.uniform(jax.random.fold_in(jax.random.fold_in(stream_key, 6), dim), (shards_of,), jnp.float32, low / len(pieces), high / len(pieces))
        loudness = loudness * jnp.repeat(jnp.exp(heights), dims[dim] // shards_of).reshape((-1,) + (1,) * (len(dims) - 1 - dim))
    return loudness


def gaussian(own_key, dims, deviation, most, cuts=(), kind=jnp.bfloat16):
    factor_of = block_scale(own_key, dims, cuts, -0.22, 0.18) if cuts else 1.0
    array = jax.random.normal(own_key, dims, jnp.float32) * deviation * factor_of
    return jnp.minimum(jnp.maximum(array, -most), most).astype(kind)


def setup_inputs(seed: int = 0) -> dict:
    keys = jax.random.split(jax.random.key(seed), 20)
    return {
        "hidden_in": gaussian(keys[0], (TOKENS, D), 1.0, 6.0, ((0, 32),)),
        "encoder_states": gaussian(keys[1], (ENC_TOK, D), 1.0, 6.0, ((0, 32),)),
        "output_grad": gaussian(keys[2], (TOKENS, D), 1.0, 6.0, ((0, 32),)),
        "piece_starts": draw_piece_starts(jax.random.fold_in(keys[19], 71), 0),
        "selfquery": gaussian(keys[4], (D, D), (D * 16) ** -0.5, 0.0546875, ((0, 4),)),
        "selfkey": gaussian(keys[5], (D, D), D ** -0.5, 0.21875, ((0, 4),)),
        "selfvalue": gaussian(keys[6], (D, D), D ** -0.5, 0.21875, ((0, 4),)),
        "selfproj": gaussian(keys[7], (D, D), (D // 16) ** -0.5, 0.875, ((0, 4),)),
        "crossquery": gaussian(keys[8], (D, D), (D * 16) ** -0.5, 0.0546875, ((0, 4),)),
        "crosskey": gaussian(keys[9], (D, D), D ** -0.5, 0.21875, ((0, 4),)),
        "crossvalue": gaussian(keys[10], (D, D), D ** -0.5, 0.21875, ((0, 4),)),
        "crossproj": gaussian(keys[11], (D, D), (D // 16) ** -0.5, 0.875, ((0, 4),)),
        "gateproj": gaussian(keys[12], (D, FF), D ** -0.5, 0.21875, ((0, 4),)),
        "upproj": gaussian(keys[13], (D, FF), D ** -0.5, 0.21875, ((0, 4),)),
        "downproj": gaussian(keys[14], (FF, D), FF ** -0.5, 0.125, ((0, 4),)),
        "gainself": jnp.clip(1.0 + 0.1 * jax.random.normal(keys[15], (D,), jnp.float32), 0.5, 1.5).astype(jnp.bfloat16),
        "gaincross": jnp.clip(1.0 + 0.1 * jax.random.normal(keys[16], (D,), jnp.float32), 0.5, 1.5).astype(jnp.bfloat16),
        "gainffn": jnp.clip(1.0 + 0.1 * jax.random.normal(keys[17], (D,), jnp.float32), 0.5, 1.5).astype(jnp.bfloat16),
        "reltable": gaussian(keys[18], (BUCKETS, HEADS), 0.8, 4.0, ((0, 4),)),
    }


@jax.custom_vjp
def low(v):
    return lax.optimization_barrier(v.astype(jnp.bfloat16)).astype(jnp.float32)

@jax.custom_vjp
def low_back(v):
    return v

def low_keep(v):
    return (low(v), None)

def low_pass(kept, grad):
    return (grad,)

def back_keep(v):
    return (v, None)

def back_low(kept, grad):
    return (low(grad),)
low.defvjp(low_keep, low_pass)
low_back.defvjp(back_keep, back_low)
EPS = 1e-06
NEG = -1000000000.0
EDGES = (1, 2, 3, 4, 5, 6, 7, 8, 12, 16, 23, 32, 46, 64, 91)
HIGH = lax.Precision.HIGHEST

def rms_scale(hidden, gain):
    return hidden * lax.rsqrt(lax.optimization_barrier(jnp.mean(hidden * hidden, axis=-1, keepdims=True)) + EPS) * gain

def gated(gate, upper):
    return jax.nn.gelu(gate, approximate=True) * upper

def product(left, right):
    return jnp.dot(left, right, precision=HIGH, preferred_element_type=jnp.float32)

def onehot_of(length):
    position = jnp.arange(length, dtype=jnp.int32)
    relative = position[None, :] - position[:, None]
    distance = jnp.abs(relative)
    bucket = 16 * (relative > 0).astype(jnp.int32)
    for edge_len in EDGES:
        bucket = bucket + (distance >= edge_len).astype(jnp.int32)
    return (bucket[:, :, None] == jnp.arange(BUCKETS, dtype=jnp.int32)[None, None, :]).astype(jnp.float32)

def attend(queries, key_rows, value_rows, bias_full, allowed):
    row_count = queries.shape[0]
    query_heads = queries.reshape(row_count, HEADS, HEAD_DIM)
    key_heads = key_rows.reshape(key_rows.shape[0], HEADS, HEAD_DIM)
    value_heads = value_rows.reshape(value_rows.shape[0], HEADS, HEAD_DIM)
    scores = jnp.einsum('qhd,khd->hqk', query_heads, key_heads, precision=HIGH)
    if bias_full is not None:
        scores = jnp.where(allowed[None], scores + bias_full, NEG)
    scores = low_back(scores)
    row_max = lax.optimization_barrier(jnp.max(scores, axis=-1, keepdims=True))
    raised = jnp.exp(scores - row_max)
    probs = low(raised / lax.optimization_barrier(jnp.sum(raised, axis=-1, keepdims=True)))
    mixed = jnp.einsum('hqk,khd->qhd', probs, value_heads, precision=HIGH).reshape(row_count, HEADS * HEAD_DIM)
    return low(low_back(mixed))

def layer(hidden, encoder, onehot, allowed, selfquery, selfkey, selfvalue, selfproj, crossquery, crosskey, crossvalue, crossproj, gateproj, upproj, downproj, gainself, gaincross, gainffn, reltable):
    normed_one = low(rms_scale(hidden, gainself))
    query_one = low(low_back(product(normed_one, selfquery)))
    key_one = low(low_back(product(normed_one, selfkey)))
    value_one = low(low_back(product(normed_one, selfvalue)))
    bias_full = jnp.einsum('qkb,bh->hqk', onehot, reltable, precision=HIGH)
    mixed_one = attend(query_one, key_one, value_one, bias_full, allowed)
    after_self = hidden + low_back(product(mixed_one, selfproj))
    normed_two = low(rms_scale(after_self, gaincross))
    query_two = low(low_back(product(normed_two, crossquery)))
    key_two = low(low_back(product(encoder, crosskey)))
    value_two = low(low_back(product(encoder, crossvalue)))
    mixed_two = attend(query_two, key_two, value_two, None, None)
    after_cross = after_self + low_back(product(mixed_two, crossproj))
    normed_three = low(rms_scale(after_cross, gainffn))
    gate_pre = low_back(product(normed_three, gateproj))
    upper_pre = low_back(product(normed_three, upproj))
    inner = low(gated(gate_pre, upper_pre))
    return after_cross + low_back(product(inner, downproj))

def reference(hidden_in, encoder_states, output_grad, piece_starts, selfquery, selfkey, selfvalue, selfproj, crossquery, crosskey, crossvalue, crossproj, gateproj, upproj, downproj, gainself, gaincross, gainffn, reltable):
    params = tuple((weight.astype(jnp.float32) for weight in (selfquery, selfkey, selfvalue, selfproj, crossquery, crosskey, crossvalue, crossproj, gateproj, upproj, downproj, gainself, gaincross, gainffn, reltable)))
    onehot = onehot_of(SEQ)
    position = jnp.arange(SEQ, dtype=jnp.int32)
    hidden_seq = hidden_in.reshape(NSEQ, SEQ, D)
    encoder_seq = encoder_states.reshape(NSEQ, ENC, D)
    grad_seq = output_grad.reshape(NSEQ, SEQ, D)

    def one_sequence(totals, inputs):
        hidden, encoder, cotangent, starts = inputs
        piece_ids = lax.optimization_barrier(jnp.sum((starts[None, :] <= position[:, None]).astype(jnp.int32), axis=1)) - 1
        allowed = (position[None, :] <= position[:, None]) | (piece_ids[None, :] == piece_ids[:, None])

        def forward(hidden_f, encoder_f, *weights):
            return layer(hidden_f, encoder_f, onehot, allowed, *weights)
        output, pullback = jax.vjp(forward, hidden.astype(jnp.float32), encoder.astype(jnp.float32), *params)
        grads = pullback(cotangent.astype(jnp.float32))
        totals = tuple((running + fresh for running, fresh in zip(totals, grads[2:])))
        return (totals, (output.astype(jnp.bfloat16), grads[0], grads[1]))
    zeros = tuple((jnp.zeros(weight.shape, jnp.float32) for weight in params))
    totals, outputs = lax.scan(one_sequence, zeros, (hidden_seq, encoder_seq, grad_seq, piece_starts))
    return (outputs[0].reshape(TOKENS, D), outputs[1].reshape(TOKENS, D), outputs[2].reshape(ENC_TOK, D), totals[0], totals[1], totals[2], totals[3], totals[4], totals[5], totals[6], totals[7], totals[8], totals[9], totals[10], totals[11], totals[12], totals[13], totals[14])
```

```python
import jax
import jax.numpy as jnp
from jax import lax
from jax.sharding import PartitionSpec as P

HEADS = 12
HEAD_DIM = 64
BUCKETS = 32
QBLOCK = 512


EPS = 1e-06
NEG = -1000000000.0
EDGES = (1, 2, 3, 4, 5, 6, 7, 8, 12, 16, 23, 32, 46, 64, 91)


def rms_scale(hidden, gain):
    return hidden * lax.rsqrt(jnp.mean(hidden * hidden, axis=-1, keepdims=True) + EPS) * gain


def gated(gate, upper):
    return jax.nn.gelu(gate, approximate=True) * upper


def product(left, right):
    return jnp.dot(left, right, preferred_element_type=jnp.float32)


def left_product(left, right):
    return lax.dot_general(
        left, right, (((0,), (0,)), ((), ())), preferred_element_type=jnp.float32
    )


def right_product(left, right):
    return lax.dot_general(
        left, right, (((1,), (1,)), ((), ())), preferred_element_type=jnp.float32
    )


def split_heads(matrix):
    return matrix.reshape(matrix.shape[0], HEADS, HEAD_DIM)


def block_terms(context, block_rows, key_count):
    if context is None:
        return (None, None, None)
    rel_table, piece_ids = context
    query_pos = jnp.arange(block_rows, dtype=jnp.int32)
    key_pos = jnp.arange(key_count, dtype=jnp.int32)
    relative = key_pos[None, :] - query_pos[:, None]
    distance = jnp.abs(relative)
    bucket = 16 * (relative > 0).astype(jnp.int32)
    for edge_len in EDGES:
        bucket = bucket + (distance >= edge_len).astype(jnp.int32)
    onehot = (bucket[:, :, None] == jnp.arange(BUCKETS, dtype=jnp.int32)[None, None, :]).astype(
        jnp.bfloat16
    )
    bias_block = jnp.einsum("qkb,bh->hqk", onehot, rel_table, preferred_element_type=jnp.float32)
    allowed = (key_pos[None, :] <= query_pos[:, None]) | (piece_ids[None, :] == piece_ids[:, None])
    return (onehot, bias_block, allowed)


def block_scores(query_block, key_heads, bias_block, allowed):
    scores = jnp.einsum("qhd,khd->hqk", query_block, key_heads, preferred_element_type=jnp.float32)
    if bias_block is not None:
        scores = jnp.where(allowed[None], scores + bias_block, NEG)
    return scores


def attend_forward(queries, key_rows, value_rows, context):
    key_heads = split_heads(key_rows)
    value_heads = split_heads(value_rows)
    query_block = split_heads(queries)
    onehot, bias_block, allowed = block_terms(context, QBLOCK, key_rows.shape[0])
    scores = block_scores(query_block, key_heads, bias_block, allowed)
    row_max = jnp.max(scores, axis=-1, keepdims=True)
    raised = jnp.exp(scores - row_max)
    row_sum = jnp.sum(raised, axis=-1, keepdims=True)
    prob_low = (raised / row_sum).astype(jnp.bfloat16)
    mixed_block = jnp.einsum(
        "hqk,khd->qhd", prob_low, value_heads, preferred_element_type=jnp.float32
    )
    mixed_parts = mixed_block.reshape(QBLOCK, HEADS * HEAD_DIM).astype(jnp.bfloat16)
    lse_parts = row_max + jnp.log(row_sum)
    return (mixed_parts, lse_parts)


def attend_backward(queries, key_rows, value_rows, grad_mixed, lse_rows, context):
    key_count = key_rows.shape[0]
    key_heads = split_heads(key_rows)
    value_heads = split_heads(value_rows)
    table_grad = jnp.zeros((BUCKETS, HEADS), jnp.float32)
    query_block = split_heads(queries)
    grad_block = split_heads(grad_mixed)
    onehot, bias_block, allowed = block_terms(context, QBLOCK, key_count)
    scores = block_scores(query_block, key_heads, bias_block, allowed)
    probs = jnp.exp(scores - lse_rows)
    prob_low = probs.astype(jnp.bfloat16)
    grad_probs = jnp.einsum(
        "qhd,khd->hqk", grad_block, value_heads, preferred_element_type=jnp.float32
    )
    inner_sum = jnp.sum(probs * grad_probs, axis=-1, keepdims=True)
    grad_scores = (probs * (grad_probs - inner_sum)).astype(jnp.bfloat16)
    query_grad = jnp.einsum(
        "hqk,khd->qhd", grad_scores, key_heads, preferred_element_type=jnp.float32
    )
    query_parts = query_grad.reshape(QBLOCK, HEADS * HEAD_DIM).astype(jnp.bfloat16)
    key_grad = jnp.einsum(
        "hqk,qhd->khd", grad_scores, query_block, preferred_element_type=jnp.float32
    )
    value_grad = jnp.einsum(
        "hqk,qhd->khd", prob_low, grad_block, preferred_element_type=jnp.float32
    )
    if onehot is not None:
        table_grad = jnp.einsum(
            "hqk,qkb->bh", grad_scores, onehot, preferred_element_type=jnp.float32
        )
    key_low = key_grad.reshape(key_count, HEADS * HEAD_DIM).astype(jnp.bfloat16)
    value_low = value_grad.reshape(key_count, HEADS * HEAD_DIM).astype(jnp.bfloat16)
    return (query_parts, key_low, value_low, table_grad)


def make_on_device(fsdp_size, replica_size):
    def on_device(
        hidden_in,
        encoder_states,
        output_grad,
        piece_starts,
        selfquery,
        selfkey,
        selfvalue,
        selfproj,
        crossquery,
        crosskey,
        crossvalue,
        crossproj,
        gateproj,
        upproj,
        downproj,
        gainself,
        gaincross,
        gainffn,
        reltable,
    ):
        shard_rows, width = selfquery.shape
        ff_width = gateproj.shape[1]
        table_rows = reltable.shape[0]
        self_packed = jnp.concatenate([selfquery, selfkey, selfvalue], axis=1)
        small_packed = jnp.concatenate(
            [gainself, gaincross, gainffn, reltable.reshape(-1)]
        )
        mid_packed = jnp.concatenate(
            [selfproj, crossquery, crosskey, crossvalue, crossproj], axis=1
        )
        ffn_packed = jnp.concatenate(
            [gateproj, upproj, downproj.reshape(shard_rows, -1)], axis=1
        )
        self_full = lax.all_gather(self_packed, "fsdp", axis=0, tiled=True)
        small_full = lax.all_gather(small_packed, "fsdp", axis=0, tiled=False)
        mid_full = lax.all_gather(mid_packed, "fsdp", axis=0, tiled=True)
        ffn_full = lax.all_gather(ffn_packed, "fsdp", axis=0, tiled=True)

        gain_one = small_full[:, 0:shard_rows].reshape(-1)
        gain_two = small_full[:, shard_rows : 2 * shard_rows].reshape(-1)
        gain_three = small_full[:, 2 * shard_rows : 3 * shard_rows].reshape(-1)
        table_full = small_full[:, 3 * shard_rows :].reshape(-1, HEADS)
        self_proj = mid_full[:, 0:width]
        cross_query = mid_full[:, width : 2 * width]
        cross_kv = mid_full[:, 2 * width : 4 * width]
        cross_key = cross_kv[:, :width]
        cross_value = cross_kv[:, width:]
        cross_proj = mid_full[:, 4 * width : 5 * width]
        gate_up = ffn_full[:, : 2 * ff_width]
        down_full = (
            ffn_full[:, 2 * ff_width :]
            .reshape(fsdp_size, shard_rows, ff_width)
            .reshape(ff_width, width)
        )

        length = hidden_in.shape[0]
        position = jnp.arange(length, dtype=jnp.int32)
        piece_ids = (
            jnp.sum((piece_starts[0][None, :] <= position[:, None]).astype(jnp.int32), axis=1) - 1
        )
        context = (table_full, piece_ids)
        resid_in = hidden_in.astype(jnp.float32)
        normed_one = rms_scale(resid_in, gain_one.astype(jnp.float32)).astype(jnp.bfloat16)
        qkv_one = product(normed_one, self_full).astype(jnp.bfloat16)
        query_one = qkv_one[:, :width]
        key_one = qkv_one[:, width : 2 * width]
        value_one = qkv_one[:, 2 * width :]
        mixed_one, lse_one = attend_forward(query_one, key_one, value_one, context)
        after_self = resid_in + product(mixed_one, self_proj)
        normed_two = rms_scale(after_self, gain_two.astype(jnp.float32)).astype(jnp.bfloat16)
        query_two = product(normed_two, cross_query).astype(jnp.bfloat16)
        kv_two = product(encoder_states, cross_kv).astype(jnp.bfloat16)
        key_two = kv_two[:, :width]
        value_two = kv_two[:, width:]
        mixed_two, lse_two = attend_forward(query_two, key_two, value_two, None)
        after_cross = after_self + product(mixed_two, cross_proj)
        normed_three = rms_scale(after_cross, gain_three.astype(jnp.float32)).astype(jnp.bfloat16)
        gate_upper = product(normed_three, gate_up)
        gate_pre = gate_upper[:, :ff_width]
        upper_pre = gate_upper[:, ff_width:]
        inner = gated(gate_pre, upper_pre).astype(jnp.bfloat16)
        layer_out = (after_cross + product(inner, down_full)).astype(jnp.bfloat16)

        def reduce_rows(packed):
            owned = lax.psum_scatter(
                packed.astype(jnp.bfloat16), ("fsdp", "replica"), scatter_dimension=0, tiled=True
            )
            return lax.all_gather(owned, "replica", axis=0, tiled=True)

        downproj_grad = left_product(inner, output_grad)
        inner_grad = right_product(output_grad, down_full)
        gated_value, pull_gate = jax.vjp(gated, gate_pre, upper_pre)
        gate_grad, upper_grad = pull_gate(inner_grad)
        gate_upper_low = jnp.concatenate(
            [gate_grad.astype(jnp.bfloat16), upper_grad.astype(jnp.bfloat16)], axis=1
        )
        gate_up_grad = left_product(normed_three, gate_upper_low)
        ffn_owned = reduce_rows(
            jnp.concatenate([gate_up_grad, downproj_grad.reshape(width, ff_width)], axis=1)
        )
        normed_grad = right_product(gate_upper_low, gate_up)
        norm_value, pull_norm = jax.vjp(rms_scale, after_cross, gain_three.astype(jnp.float32))
        back_resid, gainffn_grad = pull_norm(normed_grad)
        resid_grad = output_grad.astype(jnp.float32) + back_resid
        branch_low = resid_grad.astype(jnp.bfloat16)
        crossproj_grad = left_product(mixed_two, branch_low)
        mixed_grad = right_product(branch_low, cross_proj).astype(jnp.bfloat16)
        query_back, key_back, value_back, unused_table = attend_backward(
            query_two, key_two, value_two, mixed_grad, lse_two, None
        )
        crossquery_grad = left_product(normed_two, query_back)
        kv_back = jnp.concatenate([key_back, value_back], axis=1)
        crosskv_grad = left_product(encoder_states, kv_back)
        cross_owned = reduce_rows(
            jnp.concatenate([crossproj_grad, crossquery_grad, crosskv_grad], axis=1)
        )
        encoder_grad = right_product(kv_back, cross_kv)
        normed_grad = right_product(query_back, cross_query)
        norm_value, pull_norm = jax.vjp(rms_scale, after_self, gain_two.astype(jnp.float32))
        back_resid, gaincross_grad = pull_norm(normed_grad)
        resid_grad = resid_grad + back_resid
        branch_low = resid_grad.astype(jnp.bfloat16)
        selfproj_grad = left_product(mixed_one, branch_low)
        mixed_grad = right_product(branch_low, self_proj).astype(jnp.bfloat16)
        query_back, key_back, value_back, reltable_grad = attend_backward(
            query_one, key_one, value_one, mixed_grad, lse_one, context
        )
        qkv_back = jnp.concatenate([query_back, key_back, value_back], axis=1)
        selfqkv_grad = left_product(normed_one, qkv_back)
        self_owned = reduce_rows(jnp.concatenate([selfproj_grad, selfqkv_grad], axis=1))
        normed_grad = right_product(qkv_back, self_full)
        norm_value, pull_norm = jax.vjp(rms_scale, resid_in, gain_one.astype(jnp.float32))
        back_resid, gainself_grad = pull_norm(normed_grad)
        hidden_grad = resid_grad + back_resid

        small_sum = lax.psum(
            jnp.concatenate(
                [gainself_grad, gaincross_grad, gainffn_grad, reltable_grad.reshape(-1)]
            ),
            ("fsdp", "replica"),
        )
        me = lax.axis_index("fsdp")
        gain_block = lambda i: lax.dynamic_slice_in_dim(
            small_sum, i * width + me * shard_rows, shard_rows
        )
        table_block = lax.dynamic_slice_in_dim(
            small_sum[3 * width :].reshape(-1, HEADS), me * table_rows, table_rows
        )

        as_f32 = lambda v: v.astype(jnp.float32)
        return (
            layer_out,
            hidden_grad,
            encoder_grad,
            as_f32(self_owned[:, width : 2 * width]),
            as_f32(self_owned[:, 2 * width : 3 * width]),
            as_f32(self_owned[:, 3 * width : 4 * width]),
            as_f32(self_owned[:, 0:width]),
            as_f32(cross_owned[:, width : 2 * width]),
            as_f32(cross_owned[:, 2 * width : 3 * width]),
            as_f32(cross_owned[:, 3 * width : 4 * width]),
            as_f32(cross_owned[:, 0:width]),
            as_f32(ffn_owned[:, 0:ff_width]),
            as_f32(ffn_owned[:, ff_width : 2 * ff_width]),
            as_f32(ffn_owned[:, 2 * ff_width :].reshape(-1, width)),
            gain_block(0),
            gain_block(1),
            gain_block(2),
            table_block,
        )

    return on_device


def solution(mesh):
    placed = (
        P(("fsdp", "replica"), None),
        P(("fsdp", "replica"), None),
        P(("fsdp", "replica"), None),
        P(("fsdp", "replica"), None),
        P("fsdp", None),
        P("fsdp", None),
        P("fsdp", None),
        P("fsdp", None),
        P("fsdp", None),
        P("fsdp", None),
        P("fsdp", None),
        P("fsdp", None),
        P("fsdp", None),
        P("fsdp", None),
        P("fsdp", None),
        P("fsdp"),
        P("fsdp"),
        P("fsdp"),
        P("fsdp", None),
    )
    return jax.shard_map(
        make_on_device(mesh.shape["fsdp"], mesh.shape["replica"]),
        mesh=mesh,
        in_specs=placed,
        out_specs=(
            P(("fsdp", "replica"), None),
            P(("fsdp", "replica"), None),
            P(("fsdp", "replica"), None),
            P("fsdp", None),
            P("fsdp", None),
            P("fsdp", None),
            P("fsdp", None),
            P("fsdp", None),
            P("fsdp", None),
            P("fsdp", None),
            P("fsdp", None),
            P("fsdp", None),
            P("fsdp", None),
            P("fsdp", None),
            P("fsdp"),
            P("fsdp"),
            P("fsdp"),
            P("fsdp", None),
        ),
        check_vma=False,
    )
```

```python
import jax
import jax.numpy as jnp
from jax import lax
from jax.sharding import PartitionSpec as P

HEADS = 12
HEAD_DIM = 64
BUCKETS = 32
QBLOCK = 512


EPS = 1e-06
NEG = -1000000000.0
EDGES = (1, 2, 3, 4, 5, 6, 7, 8, 12, 16, 23, 32, 46, 64, 91)


def rms_scale(hidden, gain):
    return hidden * lax.rsqrt(jnp.mean(hidden * hidden, axis=-1, keepdims=True) + EPS) * gain


def gated(gate, upper):
    return jax.nn.gelu(gate, approximate=True) * upper


def product(left, right):
    return jnp.dot(left, right, preferred_element_type=jnp.float32)


def left_product(left, right):
    return lax.dot_general(
        left, right, (((0,), (0,)), ((), ())), preferred_element_type=jnp.float32
    )


def right_product(left, right):
    return lax.dot_general(
        left, right, (((1,), (1,)), ((), ())), preferred_element_type=jnp.float32
    )


def split_heads(matrix):
    return matrix.reshape(matrix.shape[0], HEADS, HEAD_DIM)


def block_terms(context, block_rows, key_count):
    if context is None:
        return (None, None, None)
    rel_table, piece_ids = context
    query_pos = jnp.arange(block_rows, dtype=jnp.int32)
    key_pos = jnp.arange(key_count, dtype=jnp.int32)
    relative = key_pos[None, :] - query_pos[:, None]
    distance = jnp.abs(relative)
    bucket = 16 * (relative > 0).astype(jnp.int32)
    for edge_len in EDGES:
        bucket = bucket + (distance >= edge_len).astype(jnp.int32)
    onehot = (
        bucket.reshape(1, -1) == jnp.arange(BUCKETS, dtype=jnp.int32)[:, None]
    ).astype(jnp.bfloat16)
    bias_block = lax.dot_general(
        rel_table, onehot, (((0,), (0,)), ((), ())), preferred_element_type=jnp.float32
    ).reshape(HEADS, block_rows, key_count)
    allowed = (key_pos[None, :] <= query_pos[:, None]) | (piece_ids[None, :] == piece_ids[:, None])
    return (onehot, bias_block, allowed)


def block_scores(query_block, key_heads, bias_block, allowed):
    scores = jnp.einsum("qhd,khd->hqk", query_block, key_heads, preferred_element_type=jnp.float32)
    if bias_block is not None:
        scores = jnp.where(allowed[None], scores + bias_block, NEG)
    return scores


def attend_forward(queries, key_rows, value_rows, context):
    key_heads = split_heads(key_rows)
    value_heads = split_heads(value_rows)
    query_block = split_heads(queries)
    onehot, bias_block, allowed = block_terms(context, QBLOCK, key_rows.shape[0])
    scores = block_scores(query_block, key_heads, bias_block, allowed)
    row_max = jnp.max(scores, axis=-1, keepdims=True)
    raised = jnp.exp(scores - row_max)
    row_sum = jnp.sum(raised, axis=-1, keepdims=True)
    prob_low = (raised / row_sum).astype(jnp.bfloat16)
    mixed_block = jnp.einsum(
        "hqk,khd->qhd", prob_low, value_heads, preferred_element_type=jnp.float32
    )
    mixed_parts = mixed_block.reshape(QBLOCK, HEADS * HEAD_DIM).astype(jnp.bfloat16)
    lse_parts = row_max + jnp.log(row_sum)
    return (mixed_parts, lse_parts)


def attend_backward(queries, key_rows, value_rows, grad_mixed, lse_rows, context):
    key_count = key_rows.shape[0]
    key_heads = split_heads(key_rows)
    value_heads = split_heads(value_rows)
    table_grad = jnp.zeros((BUCKETS, HEADS), jnp.float32)
    query_block = split_heads(queries)
    grad_block = split_heads(grad_mixed)
    onehot, bias_block, allowed = block_terms(context, QBLOCK, key_count)
    scores = block_scores(query_block, key_heads, bias_block, allowed)
    probs = jnp.exp(scores - lse_rows)
    prob_low = probs.astype(jnp.bfloat16)
    grad_probs = jnp.einsum(
        "qhd,khd->hqk", grad_block, value_heads, preferred_element_type=jnp.float32
    )
    inner_sum = jnp.sum(probs * grad_probs, axis=-1, keepdims=True)
    grad_scores = (probs * (grad_probs - inner_sum)).astype(jnp.bfloat16)
    query_grad = jnp.einsum(
        "hqk,khd->qhd", grad_scores, key_heads, preferred_element_type=jnp.float32
    )
    query_parts = query_grad.reshape(QBLOCK, HEADS * HEAD_DIM).astype(jnp.bfloat16)
    key_grad = jnp.einsum(
        "hqk,qhd->khd", grad_scores, query_block, preferred_element_type=jnp.float32
    )
    value_grad = jnp.einsum(
        "hqk,qhd->khd", prob_low, grad_block, preferred_element_type=jnp.float32
    )
    if onehot is not None:
        table_grad = lax.dot_general(
            onehot,
            grad_scores.reshape(HEADS, -1),
            (((1,), (1,)), ((), ())),
            preferred_element_type=jnp.float32,
        )
    key_low = key_grad.reshape(key_count, HEADS * HEAD_DIM).astype(jnp.bfloat16)
    value_low = value_grad.reshape(key_count, HEADS * HEAD_DIM).astype(jnp.bfloat16)
    return (query_parts, key_low, value_low, table_grad)


def make_on_device(fsdp_size, replica_size):
    def on_device(
        hidden_in,
        encoder_states,
        output_grad,
        piece_starts,
        selfquery,
        selfkey,
        selfvalue,
        selfproj,
        crossquery,
        crosskey,
        crossvalue,
        crossproj,
        gateproj,
        upproj,
        downproj,
        gainself,
        gaincross,
        gainffn,
        reltable,
    ):
        shard_rows, width = selfquery.shape
        ff_width = gateproj.shape[1]
        table_rows = reltable.shape[0]
        self_packed = jnp.concatenate([selfquery, selfkey, selfvalue], axis=1)
        small_packed = jnp.concatenate(
            [gainself, gaincross, gainffn, reltable.reshape(-1)]
        )
        mid_packed = jnp.concatenate(
            [selfproj, crossquery, crosskey, crossvalue, crossproj], axis=1
        )
        ffn_packed = jnp.concatenate(
            [gateproj, upproj, downproj.reshape(shard_rows, -1)], axis=1
        )
        self_full = lax.all_gather(self_packed, "fsdp", axis=0, tiled=True)
        small_full = lax.all_gather(small_packed, "fsdp", axis=0, tiled=False)
        mid_full = lax.all_gather(mid_packed, "fsdp", axis=0, tiled=True)
        ffn_full = lax.all_gather(ffn_packed, "fsdp", axis=0, tiled=True)

        gain_one = small_full[:, 0:shard_rows].reshape(-1)
        gain_two = small_full[:, shard_rows : 2 * shard_rows].reshape(-1)
        gain_three = small_full[:, 2 * shard_rows : 3 * shard_rows].reshape(-1)
        table_full = small_full[:, 3 * shard_rows :].reshape(-1, HEADS)
        self_proj = mid_full[:, 0:width]
        cross_query = mid_full[:, width : 2 * width]
        cross_kv = mid_full[:, 2 * width : 4 * width]
        cross_key = cross_kv[:, :width]
        cross_value = cross_kv[:, width:]
        cross_proj = mid_full[:, 4 * width : 5 * width]
        gate_up = ffn_full[:, : 2 * ff_width]
        down_full = (
            ffn_full[:, 2 * ff_width :]
            .reshape(fsdp_size, shard_rows, ff_width)
            .reshape(ff_width, width)
        )

        length = hidden_in.shape[0]
        position = jnp.arange(length, dtype=jnp.int32)
        piece_ids = (
            jnp.sum((piece_starts[0][None, :] <= position[:, None]).astype(jnp.int32), axis=1) - 1
        )
        context = (table_full, piece_ids)
        resid_in = hidden_in.astype(jnp.float32)
        normed_one = rms_scale(resid_in, gain_one.astype(jnp.float32)).astype(jnp.bfloat16)
        qkv_one = product(normed_one, self_full).astype(jnp.bfloat16)
        query_one = qkv_one[:, :width]
        key_one = qkv_one[:, width : 2 * width]
        value_one = qkv_one[:, 2 * width :]
        mixed_one, lse_one = attend_forward(query_one, key_one, value_one, context)
        after_self = resid_in + product(mixed_one, self_proj)
        normed_two = rms_scale(after_self, gain_two.astype(jnp.float32)).astype(jnp.bfloat16)
        query_two = product(normed_two, cross_query).astype(jnp.bfloat16)
        kv_two = product(encoder_states, cross_kv).astype(jnp.bfloat16)
        key_two = kv_two[:, :width]
        value_two = kv_two[:, width:]
        mixed_two, lse_two = attend_forward(query_two, key_two, value_two, None)
        after_cross = after_self + product(mixed_two, cross_proj)
        normed_three = rms_scale(after_cross, gain_three.astype(jnp.float32)).astype(jnp.bfloat16)
        gate_upper = product(normed_three, gate_up)
        gate_pre = gate_upper[:, :ff_width]
        upper_pre = gate_upper[:, ff_width:]
        inner = gated(gate_pre, upper_pre).astype(jnp.bfloat16)
        layer_out = (after_cross + product(inner, down_full)).astype(jnp.bfloat16)

        def reduce_rows(packed):
            return lax.psum_scatter(
                packed.astype(jnp.bfloat16), ("fsdp", "replica"), scatter_dimension=0, tiled=True
            )

        downproj_grad = left_product(inner, output_grad)
        inner_grad = right_product(output_grad, down_full)
        gated_value, pull_gate = jax.vjp(gated, gate_pre, upper_pre)
        gate_grad, upper_grad = pull_gate(inner_grad)
        gate_upper_low = jnp.concatenate(
            [gate_grad.astype(jnp.bfloat16), upper_grad.astype(jnp.bfloat16)], axis=1
        )
        gate_up_grad = left_product(normed_three, gate_upper_low)
        ffn_part = reduce_rows(
            jnp.concatenate([gate_up_grad, downproj_grad.reshape(width, ff_width)], axis=1)
        )
        normed_grad = right_product(gate_upper_low, gate_up)
        norm_value, pull_norm = jax.vjp(rms_scale, after_cross, gain_three.astype(jnp.float32))
        back_resid, gainffn_grad = pull_norm(normed_grad)
        resid_grad = output_grad.astype(jnp.float32) + back_resid
        branch_low = resid_grad.astype(jnp.bfloat16)
        crossproj_grad = left_product(mixed_two, branch_low)
        mixed_grad = right_product(branch_low, cross_proj).astype(jnp.bfloat16)
        query_back, key_back, value_back, unused_table = attend_backward(
            query_two, key_two, value_two, mixed_grad, lse_two, None
        )
        crossquery_grad = left_product(normed_two, query_back)
        kv_back = jnp.concatenate([key_back, value_back], axis=1)
        crosskv_grad = left_product(encoder_states, kv_back)
        encoder_grad = right_product(kv_back, cross_kv)
        normed_grad = right_product(query_back, cross_query)
        norm_value, pull_norm = jax.vjp(rms_scale, after_self, gain_two.astype(jnp.float32))
        back_resid, gaincross_grad = pull_norm(normed_grad)
        resid_grad = resid_grad + back_resid
        branch_low = resid_grad.astype(jnp.bfloat16)
        selfproj_grad = left_product(mixed_one, branch_low)
        mixed_grad = right_product(branch_low, self_proj).astype(jnp.bfloat16)
        query_back, key_back, value_back, reltable_grad = attend_backward(
            query_one, key_one, value_one, mixed_grad, lse_one, context
        )
        qkv_back = jnp.concatenate([query_back, key_back, value_back], axis=1)
        selfqkv_grad = left_product(normed_one, qkv_back)
        normed_grad = right_product(qkv_back, self_full)
        norm_value, pull_norm = jax.vjp(rms_scale, resid_in, gain_one.astype(jnp.float32))
        back_resid, gainself_grad = pull_norm(normed_grad)
        hidden_grad = resid_grad + back_resid

        table_block_rows = table_rows
        table_cols = jnp.pad(
            reltable_grad.reshape(fsdp_size, table_block_rows, HEADS),
            ((0, 0), (0, shard_rows - table_block_rows), (0, 0)),
        ).reshape(width, HEADS)
        extra = jnp.concatenate(
            [
                gainffn_grad[:, None],
                gaincross_grad[:, None],
                gainself_grad[:, None],
                table_cols,
                jnp.zeros((width, 128 - 3 - HEADS), jnp.float32),
            ],
            axis=1,
        )
        attn_part = reduce_rows(
            jnp.concatenate(
                [
                    crossproj_grad,
                    crossquery_grad,
                    crosskv_grad,
                    selfproj_grad,
                    selfqkv_grad,
                    extra,
                ],
                axis=1,
            )
        )
        owned = lax.all_gather(
            jnp.concatenate([ffn_part, attn_part], axis=1), "replica", axis=0, tiled=True
        )
        ffn_owned = owned[:, : 3 * ff_width]
        cross_owned = owned[:, 3 * ff_width : 3 * ff_width + 4 * width]
        self_owned = owned[:, 3 * ff_width + 4 * width : 3 * ff_width + 8 * width]
        extra_owned = owned[:, 3 * ff_width + 8 * width :].astype(jnp.float32)

        as_f32 = lambda v: v.astype(jnp.float32)
        return (
            layer_out,
            hidden_grad,
            encoder_grad,
            as_f32(self_owned[:, width : 2 * width]),
            as_f32(self_owned[:, 2 * width : 3 * width]),
            as_f32(self_owned[:, 3 * width : 4 * width]),
            as_f32(self_owned[:, 0:width]),
            as_f32(cross_owned[:, width : 2 * width]),
            as_f32(cross_owned[:, 2 * width : 3 * width]),
            as_f32(cross_owned[:, 3 * width : 4 * width]),
            as_f32(cross_owned[:, 0:width]),
            as_f32(ffn_owned[:, 0:ff_width]),
            as_f32(ffn_owned[:, ff_width : 2 * ff_width]),
            as_f32(ffn_owned[:, 2 * ff_width :].reshape(-1, width)),
            extra_owned[:, 2],
            extra_owned[:, 1],
            extra_owned[:, 0],
            extra_owned[:table_block_rows, 3 : 3 + HEADS],
        )

    return on_device


def solution(mesh):
    placed = (
        P(("fsdp", "replica"), None),
        P(("fsdp", "replica"), None),
        P(("fsdp", "replica"), None),
        P(("fsdp", "replica"), None),
        P("fsdp", None),
        P("fsdp", None),
        P("fsdp", None),
        P("fsdp", None),
        P("fsdp", None),
        P("fsdp", None),
        P("fsdp", None),
        P("fsdp", None),
        P("fsdp", None),
        P("fsdp", None),
        P("fsdp", None),
        P("fsdp"),
        P("fsdp"),
        P("fsdp"),
        P("fsdp", None),
    )
    return jax.shard_map(
        make_on_device(mesh.shape["fsdp"], mesh.shape["replica"]),
        mesh=mesh,
        in_specs=placed,
        out_specs=(
            P(("fsdp", "replica"), None),
            P(("fsdp", "replica"), None),
            P(("fsdp", "replica"), None),
            P("fsdp", None),
            P("fsdp", None),
            P("fsdp", None),
            P("fsdp", None),
            P("fsdp", None),
            P("fsdp", None),
            P("fsdp", None),
            P("fsdp", None),
            P("fsdp", None),
            P("fsdp", None),
            P("fsdp", None),
            P("fsdp"),
            P("fsdp"),
            P("fsdp"),
            P("fsdp", None),
        ),
        check_vma=False,
    )
```

```python
import jax
import jax.numpy as jnp
from jax import lax
from jax.sharding import PartitionSpec as P

HEADS = 12
HEAD_DIM = 64
BUCKETS = 32
QBLOCK = 512


EPS = 1e-06
NEG = -1000000000.0
EDGES = (1, 2, 3, 4, 5, 6, 7, 8, 12, 16, 23, 32, 46, 64, 91)


def rms_scale(hidden, gain):
    return hidden * lax.rsqrt(jnp.mean(hidden * hidden, axis=-1, keepdims=True) + EPS) * gain


def gated(gate, upper):
    return jax.nn.gelu(gate, approximate=True) * upper


def product(left, right):
    return jnp.dot(left, right, preferred_element_type=jnp.float32)


def left_product(left, right):
    return lax.dot_general(
        left, right, (((0,), (0,)), ((), ())), preferred_element_type=jnp.float32
    )


def right_product(left, right):
    return lax.dot_general(
        left, right, (((1,), (1,)), ((), ())), preferred_element_type=jnp.float32
    )


def split_heads(matrix):
    return matrix.reshape(matrix.shape[0], HEADS, HEAD_DIM)


def block_terms(context, block_rows, key_count):
    if context is None:
        return (None, None, None)
    rel_table, piece_ids = context
    query_pos = jnp.arange(block_rows, dtype=jnp.int32)
    key_pos = jnp.arange(key_count, dtype=jnp.int32)
    relative = key_pos[None, :] - query_pos[:, None]
    distance = jnp.abs(relative)
    bucket = 16 * (relative > 0).astype(jnp.int32)
    for edge_len in EDGES:
        bucket = bucket + (distance >= edge_len).astype(jnp.int32)
    onehot = (
        bucket.reshape(1, -1) == jnp.arange(BUCKETS, dtype=jnp.int32)[:, None]
    ).astype(jnp.bfloat16)
    bias_block = lax.dot_general(
        rel_table, onehot, (((0,), (0,)), ((), ())), preferred_element_type=jnp.float32
    ).reshape(HEADS, block_rows, key_count)
    allowed = (key_pos[None, :] <= query_pos[:, None]) | (piece_ids[None, :] == piece_ids[:, None])
    return (onehot, bias_block, allowed)


def block_scores(query_block, key_heads, bias_block, allowed):
    scores = jnp.einsum("qhd,khd->hqk", query_block, key_heads, preferred_element_type=jnp.float32)
    if bias_block is not None:
        scores = jnp.where(allowed[None], scores + bias_block, NEG)
    return scores


def attend_forward(queries, key_rows, value_rows, context):
    key_heads = split_heads(key_rows)
    value_heads = split_heads(value_rows)
    query_block = split_heads(queries)
    onehot, bias_block, allowed = block_terms(context, QBLOCK, key_rows.shape[0])
    scores = block_scores(query_block, key_heads, bias_block, allowed)
    row_max = jnp.max(scores, axis=-1, keepdims=True)
    raised = jnp.exp(scores - row_max)
    row_sum = jnp.sum(raised, axis=-1, keepdims=True)
    prob_low = (raised / row_sum).astype(jnp.bfloat16)
    mixed_block = jnp.einsum(
        "hqk,khd->qhd", prob_low, value_heads, preferred_element_type=jnp.float32
    )
    mixed_parts = mixed_block.reshape(QBLOCK, HEADS * HEAD_DIM).astype(jnp.bfloat16)
    lse_parts = row_max + jnp.log(row_sum)
    return (mixed_parts, lse_parts)


def attend_backward(queries, key_rows, value_rows, grad_mixed, lse_rows, context):
    key_count = key_rows.shape[0]
    key_heads = split_heads(key_rows)
    value_heads = split_heads(value_rows)
    table_grad = jnp.zeros((BUCKETS, HEADS), jnp.float32)
    query_block = split_heads(queries)
    grad_block = split_heads(grad_mixed)
    onehot, bias_block, allowed = block_terms(context, QBLOCK, key_count)
    scores = block_scores(query_block, key_heads, bias_block, allowed)
    probs = jnp.exp(scores - lse_rows)
    prob_low = probs.astype(jnp.bfloat16)
    grad_probs = jnp.einsum(
        "qhd,khd->hqk", grad_block, value_heads, preferred_element_type=jnp.float32
    )
    inner_sum = jnp.sum(probs * grad_probs, axis=-1, keepdims=True)
    grad_scores = (probs * (grad_probs - inner_sum)).astype(jnp.bfloat16)
    query_grad = jnp.einsum(
        "hqk,khd->qhd", grad_scores, key_heads, preferred_element_type=jnp.float32
    )
    query_parts = query_grad.reshape(QBLOCK, HEADS * HEAD_DIM).astype(jnp.bfloat16)
    key_grad = jnp.einsum(
        "hqk,qhd->khd", grad_scores, query_block, preferred_element_type=jnp.float32
    )
    value_grad = jnp.einsum(
        "hqk,qhd->khd", prob_low, grad_block, preferred_element_type=jnp.float32
    )
    if onehot is not None:
        table_grad = lax.dot_general(
            onehot,
            grad_scores.reshape(HEADS, -1),
            (((1,), (1,)), ((), ())),
            preferred_element_type=jnp.float32,
        )
    key_low = key_grad.reshape(key_count, HEADS * HEAD_DIM).astype(jnp.bfloat16)
    value_low = value_grad.reshape(key_count, HEADS * HEAD_DIM).astype(jnp.bfloat16)
    return (query_parts, key_low, value_low, table_grad)


def make_on_device(fsdp_size, replica_size):
    def on_device(
        hidden_in,
        encoder_states,
        output_grad,
        piece_starts,
        selfquery,
        selfkey,
        selfvalue,
        selfproj,
        crossquery,
        crosskey,
        crossvalue,
        crossproj,
        gateproj,
        upproj,
        downproj,
        gainself,
        gaincross,
        gainffn,
        reltable,
    ):
        shard_rows, width = selfquery.shape
        ff_width = gateproj.shape[1]
        table_rows = reltable.shape[0]
        self_packed = jnp.concatenate([selfquery, selfkey, selfvalue], axis=1)
        small_packed = jnp.concatenate(
            [gainself, gaincross, gainffn, reltable.reshape(-1)]
        )
        mid_packed = jnp.concatenate(
            [selfproj, crossquery, crosskey, crossvalue, crossproj], axis=1
        )
        ffn_packed = jnp.concatenate(
            [gateproj, upproj, downproj.reshape(shard_rows, -1)], axis=1
        )
        core = lax.axis_index("core")
        swap = [(0, 1), (1, 0)]

        def gather_rows(packed):
            pair = lax.all_gather(packed, "fx", axis=0, tiled=False)
            other = lax.ppermute(pair, "core", swap)
            first = jnp.where(core == 0, pair, other)
            second = jnp.where(core == 0, other, pair)
            return jnp.stack([first, second], axis=1).reshape(-1, packed.shape[1])

        self_full = gather_rows(self_packed)
        small_full = lax.all_gather(small_packed, ("fx", "core"), axis=0, tiled=False)
        mid_full = gather_rows(mid_packed)
        ffn_full = gather_rows(ffn_packed)

        gain_one = small_full[:, 0:shard_rows].reshape(-1)
        gain_two = small_full[:, shard_rows : 2 * shard_rows].reshape(-1)
        gain_three = small_full[:, 2 * shard_rows : 3 * shard_rows].reshape(-1)
        table_full = small_full[:, 3 * shard_rows :].reshape(-1, HEADS)
        self_proj = mid_full[:, 0:width]
        cross_query = mid_full[:, width : 2 * width]
        cross_kv = mid_full[:, 2 * width : 4 * width]
        cross_key = cross_kv[:, :width]
        cross_value = cross_kv[:, width:]
        cross_proj = mid_full[:, 4 * width : 5 * width]
        gate_up = ffn_full[:, : 2 * ff_width]
        down_full = (
            ffn_full[:, 2 * ff_width :]
            .reshape(fsdp_size, shard_rows, ff_width)
            .reshape(ff_width, width)
        )

        length = hidden_in.shape[0]
        position = jnp.arange(length, dtype=jnp.int32)
        piece_ids = (
            jnp.sum((piece_starts[0][None, :] <= position[:, None]).astype(jnp.int32), axis=1) - 1
        )
        context = (table_full, piece_ids)
        resid_in = hidden_in.astype(jnp.float32)
        normed_one = rms_scale(resid_in, gain_one.astype(jnp.float32)).astype(jnp.bfloat16)
        qkv_one = product(normed_one, self_full).astype(jnp.bfloat16)
        query_one = qkv_one[:, :width]
        key_one = qkv_one[:, width : 2 * width]
        value_one = qkv_one[:, 2 * width :]
        mixed_one, lse_one = attend_forward(query_one, key_one, value_one, context)
        after_self = resid_in + product(mixed_one, self_proj)
        normed_two = rms_scale(after_self, gain_two.astype(jnp.float32)).astype(jnp.bfloat16)
        query_two = product(normed_two, cross_query).astype(jnp.bfloat16)
        kv_two = product(encoder_states, cross_kv).astype(jnp.bfloat16)
        key_two = kv_two[:, :width]
        value_two = kv_two[:, width:]
        mixed_two, lse_two = attend_forward(query_two, key_two, value_two, None)
        after_cross = after_self + product(mixed_two, cross_proj)
        normed_three = rms_scale(after_cross, gain_three.astype(jnp.float32)).astype(jnp.bfloat16)
        gate_upper = product(normed_three, gate_up)
        gate_pre = gate_upper[:, :ff_width]
        upper_pre = gate_upper[:, ff_width:]
        inner = gated(gate_pre, upper_pre).astype(jnp.bfloat16)
        layer_out = (after_cross + product(inner, down_full)).astype(jnp.bfloat16)

        def core_sum(packed):
            blocks = packed.reshape(fsdp_size // 2, 2, shard_rows, packed.shape[1])
            send = lax.dynamic_index_in_dim(blocks, 1 - core, axis=1, keepdims=False)
            keep = lax.dynamic_index_in_dim(blocks, core, axis=1, keepdims=False)
            recv = lax.ppermute(send.astype(jnp.bfloat16), "core", swap)
            summed = (keep + recv.astype(jnp.float32)).astype(jnp.bfloat16)
            return summed.reshape(-1, packed.shape[1])

        def reduce_rows(summed):
            return lax.psum_scatter(summed, ("fx", "replica"), scatter_dimension=0, tiled=True)

        downproj_grad = left_product(inner, output_grad)
        inner_grad = right_product(output_grad, down_full)
        gated_value, pull_gate = jax.vjp(gated, gate_pre, upper_pre)
        gate_grad, upper_grad = pull_gate(inner_grad)
        gate_upper_low = jnp.concatenate(
            [gate_grad.astype(jnp.bfloat16), upper_grad.astype(jnp.bfloat16)], axis=1
        )
        gate_up_grad = left_product(normed_three, gate_upper_low)
        ffn_summed = core_sum(
            jnp.concatenate([gate_up_grad, downproj_grad.reshape(width, ff_width)], axis=1)
        )
        normed_grad = right_product(gate_upper_low, gate_up)
        norm_value, pull_norm = jax.vjp(rms_scale, after_cross, gain_three.astype(jnp.float32))
        back_resid, gainffn_grad = pull_norm(normed_grad)
        ffn_summed, back_resid = lax.optimization_barrier((ffn_summed, back_resid))
        ffn_part = reduce_rows(ffn_summed)
        resid_grad = output_grad.astype(jnp.float32) + back_resid
        branch_low = resid_grad.astype(jnp.bfloat16)
        crossproj_grad = left_product(mixed_two, branch_low)
        mixed_grad = right_product(branch_low, cross_proj).astype(jnp.bfloat16)
        query_back, key_back, value_back, unused_table = attend_backward(
            query_two, key_two, value_two, mixed_grad, lse_two, None
        )
        crossquery_grad = left_product(normed_two, query_back)
        kv_back = jnp.concatenate([key_back, value_back], axis=1)
        crosskv_grad = left_product(encoder_states, kv_back)
        encoder_grad = right_product(kv_back, cross_kv)
        normed_grad = right_product(query_back, cross_query)
        norm_value, pull_norm = jax.vjp(rms_scale, after_self, gain_two.astype(jnp.float32))
        back_resid, gaincross_grad = pull_norm(normed_grad)
        resid_grad = resid_grad + back_resid
        branch_low = resid_grad.astype(jnp.bfloat16)
        selfproj_grad = left_product(mixed_one, branch_low)
        mixed_grad = right_product(branch_low, self_proj).astype(jnp.bfloat16)
        query_back, key_back, value_back, reltable_grad = attend_backward(
            query_one, key_one, value_one, mixed_grad, lse_one, context
        )
        qkv_back = jnp.concatenate([query_back, key_back, value_back], axis=1)
        selfqkv_grad = left_product(normed_one, qkv_back)
        normed_grad = right_product(qkv_back, self_full)
        norm_value, pull_norm = jax.vjp(rms_scale, resid_in, gain_one.astype(jnp.float32))
        back_resid, gainself_grad = pull_norm(normed_grad)
        hidden_grad = resid_grad + back_resid

        table_block_rows = table_rows
        table_cols = jnp.pad(
            reltable_grad.reshape(fsdp_size, table_block_rows, HEADS),
            ((0, 0), (0, shard_rows - table_block_rows), (0, 0)),
        ).reshape(width, HEADS)
        extra = jnp.concatenate(
            [
                gainffn_grad[:, None],
                gaincross_grad[:, None],
                gainself_grad[:, None],
                table_cols,
                jnp.zeros((width, 128 - 3 - HEADS), jnp.float32),
            ],
            axis=1,
        )
        attn_part = reduce_rows(core_sum(
            jnp.concatenate(
                [
                    crossproj_grad,
                    crossquery_grad,
                    crosskv_grad,
                    selfproj_grad,
                    selfqkv_grad,
                    extra,
                ],
                axis=1,
            )
        ))
        owned = lax.all_gather(
            jnp.concatenate([ffn_part, attn_part], axis=1), "replica", axis=0, tiled=True
        )
        ffn_owned = owned[:, : 3 * ff_width]
        cross_owned = owned[:, 3 * ff_width : 3 * ff_width + 4 * width]
        self_owned = owned[:, 3 * ff_width + 4 * width : 3 * ff_width + 8 * width]
        extra_owned = owned[:, 3 * ff_width + 8 * width :].astype(jnp.float32)

        as_f32 = lambda v: v.astype(jnp.float32)
        return (
            layer_out,
            hidden_grad,
            encoder_grad,
            as_f32(self_owned[:, width : 2 * width]),
            as_f32(self_owned[:, 2 * width : 3 * width]),
            as_f32(self_owned[:, 3 * width : 4 * width]),
            as_f32(self_owned[:, 0:width]),
            as_f32(cross_owned[:, width : 2 * width]),
            as_f32(cross_owned[:, 2 * width : 3 * width]),
            as_f32(cross_owned[:, 3 * width : 4 * width]),
            as_f32(cross_owned[:, 0:width]),
            as_f32(ffn_owned[:, 0:ff_width]),
            as_f32(ffn_owned[:, ff_width : 2 * ff_width]),
            as_f32(ffn_owned[:, 2 * ff_width :].reshape(-1, width)),
            extra_owned[:, 2],
            extra_owned[:, 1],
            extra_owned[:, 0],
            extra_owned[:table_block_rows, 3 : 3 + HEADS],
        )

    return on_device


def solution(mesh):
    fsdp_size = mesh.shape["fsdp"]
    replica_size = mesh.shape["replica"]
    split_mesh = jax.sharding.Mesh(
        mesh.devices.reshape(fsdp_size // 2, 2, replica_size), ("fx", "core", "replica")
    )
    rows = P(("fx", "core", "replica"), None)
    owned = P(("fx", "core"), None)
    owned_vec = P(("fx", "core"))
    placed = (rows, rows, rows, rows) + (owned,) * 11 + (owned_vec,) * 3 + (owned,)
    return jax.shard_map(
        make_on_device(fsdp_size, replica_size),
        mesh=split_mesh,
        in_specs=placed,
        out_specs=(rows, rows, rows) + (owned,) * 11 + (owned_vec,) * 3 + (owned,),
        check_vma=False,
    )
```

```python
import jax
import jax.numpy as jnp
from jax import lax
from jax.sharding import PartitionSpec as P

HEADS = 12
HEAD_DIM = 64
BUCKETS = 32
QBLOCK = 512


EPS = 1e-06
NEG = -1000000000.0
EDGES = (1, 2, 3, 4, 5, 6, 7, 8, 12, 16, 23, 32, 46, 64, 91)


def rms_scale(hidden, gain):
    return hidden * lax.rsqrt(jnp.mean(hidden * hidden, axis=-1, keepdims=True) + EPS) * gain


def gated(gate, upper):
    return jax.nn.gelu(gate, approximate=True) * upper


def product(left, right):
    return jnp.dot(left, right, preferred_element_type=jnp.float32)


def left_product(left, right):
    return lax.dot_general(
        left, right, (((0,), (0,)), ((), ())), preferred_element_type=jnp.float32
    )


def right_product(left, right):
    return lax.dot_general(
        left, right, (((1,), (1,)), ((), ())), preferred_element_type=jnp.float32
    )


def split_heads(matrix):
    return matrix.reshape(matrix.shape[0], HEADS, HEAD_DIM)


def block_terms(context, block_rows, key_count):
    if context is None:
        return (None, None, None)
    rel_table, piece_ids = context
    query_pos = jnp.arange(block_rows, dtype=jnp.int32)
    key_pos = jnp.arange(key_count, dtype=jnp.int32)
    relative = key_pos[None, :] - query_pos[:, None]
    distance = jnp.abs(relative)
    bucket = 16 * (relative > 0).astype(jnp.int32)
    for edge_len in EDGES:
        bucket = bucket + (distance >= edge_len).astype(jnp.int32)
    onehot = (
        bucket.reshape(1, -1) == jnp.arange(BUCKETS, dtype=jnp.int32)[:, None]
    ).astype(jnp.bfloat16)
    bias_block = lax.dot_general(
        rel_table, onehot, (((0,), (0,)), ((), ())), preferred_element_type=jnp.float32
    ).reshape(HEADS, block_rows, key_count)
    allowed = (key_pos[None, :] <= query_pos[:, None]) | (piece_ids[None, :] == piece_ids[:, None])
    return (onehot, bias_block, allowed)


def block_scores(query_block, key_heads, bias_block, allowed):
    scores = jnp.einsum("qhd,khd->hqk", query_block, key_heads, preferred_element_type=jnp.float32)
    if bias_block is not None:
        scores = jnp.where(allowed[None], scores + bias_block, NEG)
    return scores


def attend_forward(queries, key_rows, value_rows, context):
    key_heads = split_heads(key_rows)
    value_heads = split_heads(value_rows)
    query_block = split_heads(queries)
    onehot, bias_block, allowed = block_terms(context, QBLOCK, key_rows.shape[0])
    scores = block_scores(query_block, key_heads, bias_block, allowed)
    row_max = jnp.max(scores, axis=-1, keepdims=True)
    raised = jnp.exp(scores - row_max)
    row_sum = jnp.sum(raised, axis=-1, keepdims=True)
    prob_low = (raised / row_sum).astype(jnp.bfloat16)
    mixed_block = jnp.einsum(
        "hqk,khd->qhd", prob_low, value_heads, preferred_element_type=jnp.float32
    )
    mixed_parts = mixed_block.reshape(QBLOCK, HEADS * HEAD_DIM).astype(jnp.bfloat16)
    lse_parts = row_max + jnp.log(row_sum)
    return (mixed_parts, lse_parts)


def attend_backward(queries, key_rows, value_rows, grad_mixed, lse_rows, context):
    key_count = key_rows.shape[0]
    key_heads = split_heads(key_rows)
    value_heads = split_heads(value_rows)
    table_grad = jnp.zeros((BUCKETS, HEADS), jnp.float32)
    query_block = split_heads(queries)
    grad_block = split_heads(grad_mixed)
    onehot, bias_block, allowed = block_terms(context, QBLOCK, key_count)
    scores = block_scores(query_block, key_heads, bias_block, allowed)
    probs = jnp.exp(scores - lse_rows)
    prob_low = probs.astype(jnp.bfloat16)
    grad_probs = jnp.einsum(
        "qhd,khd->hqk", grad_block, value_heads, preferred_element_type=jnp.float32
    )
    inner_sum = jnp.sum(probs * grad_probs, axis=-1, keepdims=True)
    grad_scores = (probs * (grad_probs - inner_sum)).astype(jnp.bfloat16)
    query_grad = jnp.einsum(
        "hqk,khd->qhd", grad_scores, key_heads, preferred_element_type=jnp.float32
    )
    query_parts = query_grad.reshape(QBLOCK, HEADS * HEAD_DIM).astype(jnp.bfloat16)
    key_grad = jnp.einsum(
        "hqk,qhd->khd", grad_scores, query_block, preferred_element_type=jnp.float32
    )
    value_grad = jnp.einsum(
        "hqk,qhd->khd", prob_low, grad_block, preferred_element_type=jnp.float32
    )
    if onehot is not None:
        table_grad = lax.dot_general(
            onehot,
            grad_scores.reshape(HEADS, -1),
            (((1,), (1,)), ((), ())),
            preferred_element_type=jnp.float32,
        )
    key_low = key_grad.reshape(key_count, HEADS * HEAD_DIM).astype(jnp.bfloat16)
    value_low = value_grad.reshape(key_count, HEADS * HEAD_DIM).astype(jnp.bfloat16)
    return (query_parts, key_low, value_low, table_grad)


def pairs_of(size, bit):
    return [(i, i ^ bit) for i in range(size)]


def tree_reduce(packed, fsdp_size, replica_size, orders=2):
    me_f = lax.axis_index("fsdp")
    me_r = lax.axis_index("replica")
    rows = packed.shape[0] // fsdp_size
    cols = packed.shape[1]
    step = 128 * max(1, cols // (128 * orders))
    bounds = [0]
    for _ in range(orders - 1):
        bounds.append(min(cols, bounds[-1] + step))
    bounds.append(cols)
    fsdp_bits = [1 << b for b in range(fsdp_size.bit_length() - 1)]
    rep_bits = [1 << b for b in range(replica_size.bit_length() - 1)]

    def fsdp_step(cur, bit):
        mine = (me_f // bit) % 2
        cur = cur.reshape(cur.shape[0] // 2, 2, cur.shape[1], cur.shape[2])
        keep = lax.dynamic_index_in_dim(cur, mine, axis=1, keepdims=False)
        send = lax.dynamic_index_in_dim(cur, 1 - mine, axis=1, keepdims=False)
        recv = lax.ppermute(send.astype(jnp.bfloat16), "fsdp", pairs_of(fsdp_size, bit))
        return keep + recv.astype(jnp.float32)

    def replica_step(cur, bit):
        mine = (me_r // bit) % 2
        cur = cur.reshape(cur.shape[0], 2, cur.shape[1] // 2, cur.shape[2])
        keep = lax.dynamic_index_in_dim(cur, mine, axis=1, keepdims=False)
        send = lax.dynamic_index_in_dim(cur, 1 - mine, axis=1, keepdims=False)
        recv = lax.ppermute(send.astype(jnp.bfloat16), "replica", pairs_of(replica_size, bit))
        return keep + recv.astype(jnp.float32)

    def replica_back(cur, bit):
        mine = (me_r // bit) % 2
        recv = lax.ppermute(cur, "replica", pairs_of(replica_size, bit))
        low = jnp.where(mine == 0, cur, recv)
        high = jnp.where(mine == 0, recv, cur)
        return jnp.concatenate([low, high], axis=1)

    outs = []
    for part in range(orders):
        lo, hi = bounds[part], bounds[part + 1]
        if hi <= lo:
            continue
        cur = packed[:, lo:hi].reshape(fsdp_size, rows, hi - lo)
        cur = fsdp_step(cur, fsdp_bits[0])
        steps = [("f", bit) for bit in fsdp_bits[1:]] + [("r", bit) for bit in rep_bits]
        shift = part % len(steps) if steps else 0
        steps = steps[shift:] + steps[:shift]
        for kind, bit in steps:
            cur = fsdp_step(cur, bit) if kind == "f" else replica_step(cur, bit)
        rep_order = [bit for kind, bit in steps if kind == "r"]
        cur = cur.astype(jnp.bfloat16)
        for bit in reversed(rep_order):
            cur = replica_back(cur, bit)
        outs.append(cur.reshape(rows, hi - lo))
    return jnp.concatenate(outs, axis=1)


def make_on_device(fsdp_size, replica_size):
    def on_device(
        hidden_in,
        encoder_states,
        output_grad,
        piece_starts,
        selfquery,
        selfkey,
        selfvalue,
        selfproj,
        crossquery,
        crosskey,
        crossvalue,
        crossproj,
        gateproj,
        upproj,
        downproj,
        gainself,
        gaincross,
        gainffn,
        reltable,
    ):
        shard_rows, width = selfquery.shape
        ff_width = gateproj.shape[1]
        table_rows = reltable.shape[0]
        self_packed = jnp.concatenate([selfquery, selfkey, selfvalue], axis=1)
        small_packed = jnp.concatenate(
            [gainself, gaincross, gainffn, reltable.reshape(-1)]
        )
        mid_packed = jnp.concatenate(
            [selfproj, crossquery, crosskey, crossvalue, crossproj], axis=1
        )
        ffn_packed = jnp.concatenate(
            [gateproj, upproj, downproj.reshape(shard_rows, -1)], axis=1
        )
        self_full = lax.all_gather(self_packed, "fsdp", axis=0, tiled=True)
        small_full = lax.all_gather(small_packed, "fsdp", axis=0, tiled=False)
        mid_full = lax.all_gather(mid_packed, "fsdp", axis=0, tiled=True)
        ffn_full = lax.all_gather(ffn_packed, "fsdp", axis=0, tiled=True)

        gain_one = small_full[:, 0:shard_rows].reshape(-1)
        gain_two = small_full[:, shard_rows : 2 * shard_rows].reshape(-1)
        gain_three = small_full[:, 2 * shard_rows : 3 * shard_rows].reshape(-1)
        table_full = small_full[:, 3 * shard_rows :].reshape(-1, HEADS)
        self_proj = mid_full[:, 0:width]
        cross_query = mid_full[:, width : 2 * width]
        cross_kv = mid_full[:, 2 * width : 4 * width]
        cross_key = cross_kv[:, :width]
        cross_value = cross_kv[:, width:]
        cross_proj = mid_full[:, 4 * width : 5 * width]
        gate_up = ffn_full[:, : 2 * ff_width]
        down_full = (
            ffn_full[:, 2 * ff_width :]
            .reshape(fsdp_size, shard_rows, ff_width)
            .reshape(ff_width, width)
        )

        length = hidden_in.shape[0]
        position = jnp.arange(length, dtype=jnp.int32)
        piece_ids = (
            jnp.sum((piece_starts[0][None, :] <= position[:, None]).astype(jnp.int32), axis=1) - 1
        )
        context = (table_full, piece_ids)
        resid_in = hidden_in.astype(jnp.float32)
        normed_one = rms_scale(resid_in, gain_one.astype(jnp.float32)).astype(jnp.bfloat16)
        qkv_one = product(normed_one, self_full).astype(jnp.bfloat16)
        query_one = qkv_one[:, :width]
        key_one = qkv_one[:, width : 2 * width]
        value_one = qkv_one[:, 2 * width :]
        mixed_one, lse_one = attend_forward(query_one, key_one, value_one, context)
        after_self = resid_in + product(mixed_one, self_proj)
        normed_two = rms_scale(after_self, gain_two.astype(jnp.float32)).astype(jnp.bfloat16)
        query_two = product(normed_two, cross_query).astype(jnp.bfloat16)
        kv_two = product(encoder_states, cross_kv).astype(jnp.bfloat16)
        key_two = kv_two[:, :width]
        value_two = kv_two[:, width:]
        mixed_two, lse_two = attend_forward(query_two, key_two, value_two, None)
        after_cross = after_self + product(mixed_two, cross_proj)
        normed_three = rms_scale(after_cross, gain_three.astype(jnp.float32)).astype(jnp.bfloat16)
        gate_upper = product(normed_three, gate_up)
        gate_pre = gate_upper[:, :ff_width]
        upper_pre = gate_upper[:, ff_width:]
        inner = gated(gate_pre, upper_pre).astype(jnp.bfloat16)
        layer_out = (after_cross + product(inner, down_full)).astype(jnp.bfloat16)

        def reduce_rows(packed):
            return lax.psum_scatter(
                packed.astype(jnp.bfloat16), ("fsdp", "replica"), scatter_dimension=0, tiled=True
            )

        downproj_grad = left_product(inner, output_grad)
        inner_grad = right_product(output_grad, down_full)
        gated_value, pull_gate = jax.vjp(gated, gate_pre, upper_pre)
        gate_grad, upper_grad = pull_gate(inner_grad)
        gate_upper_low = jnp.concatenate(
            [gate_grad.astype(jnp.bfloat16), upper_grad.astype(jnp.bfloat16)], axis=1
        )
        gate_up_grad = left_product(normed_three, gate_upper_low)
        ffn_packed = jnp.concatenate(
            [gate_up_grad, downproj_grad.reshape(width, ff_width)], axis=1
        ).astype(jnp.bfloat16)
        normed_grad = right_product(gate_upper_low, gate_up)
        norm_value, pull_norm = jax.vjp(rms_scale, after_cross, gain_three.astype(jnp.float32))
        back_resid, gainffn_grad = pull_norm(normed_grad)
        ffn_packed, back_resid = lax.optimization_barrier((ffn_packed, back_resid))
        ffn_part = reduce_rows(ffn_packed)
        resid_grad = output_grad.astype(jnp.float32) + back_resid
        branch_low = resid_grad.astype(jnp.bfloat16)
        crossproj_grad = left_product(mixed_two, branch_low)
        mixed_grad = right_product(branch_low, cross_proj).astype(jnp.bfloat16)
        query_back, key_back, value_back, unused_table = attend_backward(
            query_two, key_two, value_two, mixed_grad, lse_two, None
        )
        crossquery_grad = left_product(normed_two, query_back)
        kv_back = jnp.concatenate([key_back, value_back], axis=1)
        crosskv_grad = left_product(encoder_states, kv_back)
        cross_packed = jnp.concatenate([crossproj_grad, crossquery_grad, crosskv_grad], axis=1)
        encoder_grad = right_product(kv_back, cross_kv)
        normed_grad = right_product(query_back, cross_query)
        norm_value, pull_norm = jax.vjp(rms_scale, after_self, gain_two.astype(jnp.float32))
        back_resid, gaincross_grad = pull_norm(normed_grad)
        resid_grad = resid_grad + back_resid
        branch_low = resid_grad.astype(jnp.bfloat16)
        selfproj_grad = left_product(mixed_one, branch_low)
        mixed_grad = right_product(branch_low, self_proj).astype(jnp.bfloat16)
        query_back, key_back, value_back, reltable_grad = attend_backward(
            query_one, key_one, value_one, mixed_grad, lse_one, context
        )
        qkv_back = jnp.concatenate([query_back, key_back, value_back], axis=1)
        selfqkv_grad = left_product(normed_one, qkv_back)
        normed_grad = right_product(qkv_back, self_full)
        norm_value, pull_norm = jax.vjp(rms_scale, resid_in, gain_one.astype(jnp.float32))
        back_resid, gainself_grad = pull_norm(normed_grad)
        hidden_grad = resid_grad + back_resid

        table_block_rows = table_rows
        table_cols = jnp.pad(
            reltable_grad.reshape(fsdp_size, table_block_rows, HEADS),
            ((0, 0), (0, shard_rows - table_block_rows), (0, 0)),
        ).reshape(width, HEADS)
        extra = jnp.concatenate(
            [
                gainffn_grad[:, None],
                gaincross_grad[:, None],
                gainself_grad[:, None],
                table_cols,
                jnp.zeros((width, 128 - 3 - HEADS), jnp.float32),
            ],
            axis=1,
        )
        attn_packed = jnp.concatenate([cross_packed, selfproj_grad, selfqkv_grad, extra], axis=1)
        attn_packed, ffn_part = lax.optimization_barrier((attn_packed, ffn_part))
        ffn_owned = lax.all_gather(ffn_part, "replica", axis=0, tiled=True)
        attn_owned = tree_reduce(attn_packed, fsdp_size, replica_size, orders=4)
        cross_owned = attn_owned[:, : 4 * width]
        self_owned = attn_owned[:, 4 * width : 8 * width]
        extra_owned = attn_owned[:, 8 * width :].astype(jnp.float32)

        as_f32 = lambda v: v.astype(jnp.float32)
        return (
            layer_out,
            hidden_grad,
            encoder_grad,
            as_f32(self_owned[:, width : 2 * width]),
            as_f32(self_owned[:, 2 * width : 3 * width]),
            as_f32(self_owned[:, 3 * width : 4 * width]),
            as_f32(self_owned[:, 0:width]),
            as_f32(cross_owned[:, width : 2 * width]),
            as_f32(cross_owned[:, 2 * width : 3 * width]),
            as_f32(cross_owned[:, 3 * width : 4 * width]),
            as_f32(cross_owned[:, 0:width]),
            as_f32(ffn_owned[:, 0:ff_width]),
            as_f32(ffn_owned[:, ff_width : 2 * ff_width]),
            as_f32(ffn_owned[:, 2 * ff_width :].reshape(-1, width)),
            extra_owned[:, 2],
            extra_owned[:, 1],
            extra_owned[:, 0],
            extra_owned[:table_block_rows, 3 : 3 + HEADS],
        )

    return on_device


def solution(mesh):
    placed = (
        P(("fsdp", "replica"), None),
        P(("fsdp", "replica"), None),
        P(("fsdp", "replica"), None),
        P(("fsdp", "replica"), None),
        P("fsdp", None),
        P("fsdp", None),
        P("fsdp", None),
        P("fsdp", None),
        P("fsdp", None),
        P("fsdp", None),
        P("fsdp", None),
        P("fsdp", None),
        P("fsdp", None),
        P("fsdp", None),
        P("fsdp", None),
        P("fsdp"),
        P("fsdp"),
        P("fsdp"),
        P("fsdp", None),
    )
    return jax.shard_map(
        make_on_device(mesh.shape["fsdp"], mesh.shape["replica"]),
        mesh=mesh,
        in_specs=placed,
        out_specs=(
            P(("fsdp", "replica"), None),
            P(("fsdp", "replica"), None),
            P(("fsdp", "replica"), None),
            P("fsdp", None),
            P("fsdp", None),
            P("fsdp", None),
            P("fsdp", None),
            P("fsdp", None),
            P("fsdp", None),
            P("fsdp", None),
            P("fsdp", None),
            P("fsdp", None),
            P("fsdp", None),
            P("fsdp", None),
            P("fsdp"),
            P("fsdp"),
            P("fsdp"),
            P("fsdp", None),
        ),
        check_vma=False,
    )
```

```python
import jax
import jax.numpy as jnp
from jax import lax
from jax.sharding import PartitionSpec as P

HEADS = 12
HEAD_DIM = 64
BUCKETS = 32
QBLOCK = 512


EPS = 1e-06
NEG = -1000000000.0
EDGES = (1, 2, 3, 4, 5, 6, 7, 8, 12, 16, 23, 32, 46, 64, 91)


def rms_scale(hidden, gain):
    return hidden * lax.rsqrt(jnp.mean(hidden * hidden, axis=-1, keepdims=True) + EPS) * gain


def gated(gate, upper):
    return jax.nn.gelu(gate, approximate=True) * upper


def product(left, right):
    return jnp.dot(left, right, preferred_element_type=jnp.float32)


def left_product(left, right):
    return lax.dot_general(
        left, right, (((0,), (0,)), ((), ())), preferred_element_type=jnp.float32
    )


def right_product(left, right):
    return lax.dot_general(
        left, right, (((1,), (1,)), ((), ())), preferred_element_type=jnp.float32
    )


def split_heads(matrix):
    return matrix.reshape(matrix.shape[0], HEADS, HEAD_DIM)


def block_terms(context, block_rows, key_count):
    if context is None:
        return (None, None, None)
    rel_table, piece_ids = context
    query_pos = jnp.arange(block_rows, dtype=jnp.int32)
    key_pos = jnp.arange(key_count, dtype=jnp.int32)
    relative = key_pos[None, :] - query_pos[:, None]
    distance = jnp.abs(relative)
    bucket = 16 * (relative > 0).astype(jnp.int32)
    for edge_len in EDGES:
        bucket = bucket + (distance >= edge_len).astype(jnp.int32)
    onehot = (
        bucket.T[None, :, :] == jnp.arange(BUCKETS, dtype=jnp.int32)[:, None, None]
    ).astype(jnp.bfloat16)
    bias_block = jnp.swapaxes(
        lax.dot_general(
            rel_table, onehot, (((0,), (0,)), ((), ())), preferred_element_type=jnp.float32
        ),
        1,
        2,
    )
    allowed = (key_pos[None, :] <= query_pos[:, None]) | (piece_ids[None, :] == piece_ids[:, None])
    return (onehot, bias_block, allowed)


def block_scores(query_block, key_heads, bias_block, allowed):
    scores = jnp.einsum("qhd,khd->hqk", query_block, key_heads, preferred_element_type=jnp.float32)
    if bias_block is not None:
        scores = jnp.where(allowed[None], scores + bias_block, NEG)
    return scores


def attend_forward(queries, key_rows, value_rows, context):
    key_heads = split_heads(key_rows)
    value_heads = split_heads(value_rows)
    query_block = split_heads(queries)
    onehot, bias_block, allowed = block_terms(context, QBLOCK, key_rows.shape[0])
    scores = block_scores(query_block, key_heads, bias_block, allowed)
    row_max = jnp.max(scores, axis=-1, keepdims=True)
    raised = jnp.exp(scores - row_max)
    row_sum = jnp.sum(raised, axis=-1, keepdims=True)
    prob_low = (raised / row_sum).astype(jnp.bfloat16)
    mixed_block = jnp.einsum(
        "hqk,khd->qhd", prob_low, value_heads, preferred_element_type=jnp.float32
    )
    mixed_parts = mixed_block.reshape(QBLOCK, HEADS * HEAD_DIM).astype(jnp.bfloat16)
    lse_parts = row_max + jnp.log(row_sum)
    return (mixed_parts, lse_parts)


def attend_backward(queries, key_rows, value_rows, grad_mixed, lse_rows, context):
    key_count = key_rows.shape[0]
    key_heads = split_heads(key_rows)
    value_heads = split_heads(value_rows)
    table_grad = jnp.zeros((BUCKETS, HEADS), jnp.float32)
    query_block = split_heads(queries)
    grad_block = split_heads(grad_mixed)
    onehot, bias_block, allowed = block_terms(context, QBLOCK, key_count)
    scores = block_scores(query_block, key_heads, bias_block, allowed)
    probs = jnp.exp(scores - lse_rows)
    prob_low = probs.astype(jnp.bfloat16)
    grad_probs = jnp.einsum(
        "qhd,khd->hqk", grad_block, value_heads, preferred_element_type=jnp.float32
    )
    inner_sum = jnp.sum(probs * grad_probs, axis=-1, keepdims=True)
    grad_scores = (probs * (grad_probs - inner_sum)).astype(jnp.bfloat16)
    query_grad = jnp.einsum(
        "hqk,khd->qhd", grad_scores, key_heads, preferred_element_type=jnp.float32
    )
    query_parts = query_grad.reshape(QBLOCK, HEADS * HEAD_DIM).astype(jnp.bfloat16)
    key_grad = jnp.einsum(
        "hqk,qhd->khd", grad_scores, query_block, preferred_element_type=jnp.float32
    )
    value_grad = jnp.einsum(
        "hqk,qhd->khd", prob_low, grad_block, preferred_element_type=jnp.float32
    )
    if onehot is not None:
        table_grad = lax.dot_general(
            onehot,
            grad_scores,
            (((1, 2), (2, 1)), ((), ())),
            preferred_element_type=jnp.float32,
        )
    key_low = key_grad.reshape(key_count, HEADS * HEAD_DIM).astype(jnp.bfloat16)
    value_low = value_grad.reshape(key_count, HEADS * HEAD_DIM).astype(jnp.bfloat16)
    return (query_parts, key_low, value_low, table_grad)


def pairs_of(size, bit):
    return [(i, i ^ bit) for i in range(size)]


def tree_reduce(parts, fsdp_size, replica_size):
    me_f = lax.axis_index("fsdp")
    me_r = lax.axis_index("replica")
    fsdp_bits = [1 << b for b in range(fsdp_size.bit_length() - 1)]
    rep_bits = [1 << b for b in range(replica_size.bit_length() - 1)]

    def fsdp_step(cur, bit):
        mine = (me_f // bit) % 2
        cur = cur.reshape(cur.shape[0] // 2, 2, cur.shape[1], cur.shape[2])
        keep = lax.dynamic_index_in_dim(cur, mine, axis=1, keepdims=False)
        send = lax.dynamic_index_in_dim(cur, 1 - mine, axis=1, keepdims=False)
        recv = lax.ppermute(send.astype(jnp.bfloat16), "fsdp", pairs_of(fsdp_size, bit))
        return keep + recv.astype(jnp.float32)

    def replica_step(cur, bit):
        mine = (me_r // bit) % 2
        cur = cur.reshape(cur.shape[0], 2, cur.shape[1] // 2, cur.shape[2])
        keep = lax.dynamic_index_in_dim(cur, mine, axis=1, keepdims=False)
        send = lax.dynamic_index_in_dim(cur, 1 - mine, axis=1, keepdims=False)
        recv = lax.ppermute(send.astype(jnp.bfloat16), "replica", pairs_of(replica_size, bit))
        return keep + recv.astype(jnp.float32)

    def replica_back(cur, bit):
        mine = (me_r // bit) % 2
        recv = lax.ppermute(cur, "replica", pairs_of(replica_size, bit))
        low = jnp.where(mine == 0, cur, recv)
        high = jnp.where(mine == 0, recv, cur)
        return jnp.concatenate([low, high], axis=1)

    outs = []
    for part, pieces in enumerate(parts):
        packed = jnp.concatenate(pieces, axis=1) if len(pieces) > 1 else pieces[0]
        rows = packed.shape[0] // fsdp_size
        cur = packed.reshape(fsdp_size, rows, packed.shape[1])
        cur = fsdp_step(cur, fsdp_bits[0])
        steps = [("f", bit) for bit in fsdp_bits[1:]] + [("r", bit) for bit in rep_bits]
        shift = part % len(steps) if steps else 0
        steps = steps[shift:] + steps[:shift]
        for kind, bit in steps:
            cur = fsdp_step(cur, bit) if kind == "f" else replica_step(cur, bit)
        rep_order = [bit for kind, bit in steps if kind == "r"]
        cur = cur.astype(jnp.bfloat16)
        for bit in reversed(rep_order):
            cur = replica_back(cur, bit)
        outs.append(cur.reshape(rows, -1))
    return jnp.concatenate(outs, axis=1)


def make_on_device(fsdp_size, replica_size):
    def on_device(
        hidden_in,
        encoder_states,
        output_grad,
        piece_starts,
        selfquery,
        selfkey,
        selfvalue,
        selfproj,
        crossquery,
        crosskey,
        crossvalue,
        crossproj,
        gateproj,
        upproj,
        downproj,
        gainself,
        gaincross,
        gainffn,
        reltable,
    ):
        shard_rows, width = selfquery.shape
        ff_width = gateproj.shape[1]
        table_rows = reltable.shape[0]
        self_packed = jnp.concatenate([selfquery, selfkey, selfvalue], axis=1)
        small_packed = jnp.concatenate(
            [gainself, gaincross, gainffn, reltable.reshape(-1)]
        )
        mid_packed = jnp.concatenate(
            [selfproj, crossquery, crosskey, crossvalue, crossproj], axis=1
        )
        ffn_packed = jnp.concatenate(
            [gateproj, upproj, downproj.reshape(shard_rows, -1)], axis=1
        )
        self_full = lax.all_gather(self_packed, "fsdp", axis=0, tiled=True)
        small_full = lax.all_gather(small_packed, "fsdp", axis=0, tiled=False)
        mid_full = lax.all_gather(mid_packed, "fsdp", axis=0, tiled=True)
        ffn_full = lax.all_gather(ffn_packed, "fsdp", axis=0, tiled=True)

        gain_one = small_full[:, 0:shard_rows].reshape(-1)
        gain_two = small_full[:, shard_rows : 2 * shard_rows].reshape(-1)
        gain_three = small_full[:, 2 * shard_rows : 3 * shard_rows].reshape(-1)
        table_full = small_full[:, 3 * shard_rows :].reshape(-1, HEADS)
        self_proj = mid_full[:, 0:width]
        cross_query = mid_full[:, width : 2 * width]
        cross_kv = mid_full[:, 2 * width : 4 * width]
        cross_key = cross_kv[:, :width]
        cross_value = cross_kv[:, width:]
        cross_proj = mid_full[:, 4 * width : 5 * width]
        gate_up = ffn_full[:, : 2 * ff_width]
        down_full = (
            ffn_full[:, 2 * ff_width :]
            .reshape(fsdp_size, shard_rows, ff_width)
            .reshape(ff_width, width)
        )

        length = hidden_in.shape[0]
        position = jnp.arange(length, dtype=jnp.int32)
        piece_ids = (
            jnp.sum((piece_starts[0][None, :] <= position[:, None]).astype(jnp.int32), axis=1) - 1
        )
        context = (table_full, piece_ids)
        resid_in = hidden_in.astype(jnp.float32)
        normed_one = rms_scale(resid_in, gain_one.astype(jnp.float32)).astype(jnp.bfloat16)
        qkv_one = product(normed_one, self_full).astype(jnp.bfloat16)
        query_one = qkv_one[:, :width]
        key_one = qkv_one[:, width : 2 * width]
        value_one = qkv_one[:, 2 * width :]
        mixed_one, lse_one = attend_forward(query_one, key_one, value_one, context)
        after_self = resid_in + product(mixed_one, self_proj)
        normed_two = rms_scale(after_self, gain_two.astype(jnp.float32)).astype(jnp.bfloat16)
        query_two = product(normed_two, cross_query).astype(jnp.bfloat16)
        kv_two = product(encoder_states, cross_kv).astype(jnp.bfloat16)
        key_two = kv_two[:, :width]
        value_two = kv_two[:, width:]
        mixed_two, lse_two = attend_forward(query_two, key_two, value_two, None)
        after_cross = after_self + product(mixed_two, cross_proj)
        normed_three = rms_scale(after_cross, gain_three.astype(jnp.float32)).astype(jnp.bfloat16)
        gate_upper = product(normed_three, gate_up)
        gate_pre = gate_upper[:, :ff_width]
        upper_pre = gate_upper[:, ff_width:]
        inner = gated(gate_pre, upper_pre).astype(jnp.bfloat16)
        layer_out = (after_cross + product(inner, down_full)).astype(jnp.bfloat16)

        def reduce_rows(packed):
            return lax.psum_scatter(
                packed.astype(jnp.bfloat16), ("fsdp", "replica"), scatter_dimension=0, tiled=True
            )

        downproj_grad = left_product(inner, output_grad)
        inner_grad = right_product(output_grad, down_full)
        gated_value, pull_gate = jax.vjp(gated, gate_pre, upper_pre)
        gate_grad, upper_grad = pull_gate(inner_grad)
        gate_upper_low = jnp.concatenate(
            [gate_grad.astype(jnp.bfloat16), upper_grad.astype(jnp.bfloat16)], axis=1
        )
        gate_up_grad = left_product(normed_three, gate_upper_low)
        ffn_packed = jnp.concatenate(
            [gate_up_grad, downproj_grad.reshape(width, ff_width)], axis=1
        ).astype(jnp.bfloat16)
        normed_grad = right_product(gate_upper_low, gate_up)
        norm_value, pull_norm = jax.vjp(rms_scale, after_cross, gain_three.astype(jnp.float32))
        back_resid, gainffn_grad = pull_norm(normed_grad)
        ffn_packed, back_resid = lax.optimization_barrier((ffn_packed, back_resid))
        ffn_part = reduce_rows(ffn_packed)
        resid_grad = output_grad.astype(jnp.float32) + back_resid
        branch_low = resid_grad.astype(jnp.bfloat16)
        crossproj_grad = left_product(mixed_two, branch_low)
        mixed_grad = right_product(branch_low, cross_proj).astype(jnp.bfloat16)
        query_back, key_back, value_back, unused_table = attend_backward(
            query_two, key_two, value_two, mixed_grad, lse_two, None
        )
        crossquery_grad = left_product(normed_two, query_back)
        kv_back = jnp.concatenate([key_back, value_back], axis=1)
        crosskv_grad = left_product(encoder_states, kv_back)
        encoder_grad = right_product(kv_back, cross_kv)
        normed_grad = right_product(query_back, cross_query)
        norm_value, pull_norm = jax.vjp(rms_scale, after_self, gain_two.astype(jnp.float32))
        back_resid, gaincross_grad = pull_norm(normed_grad)
        resid_grad = resid_grad + back_resid
        branch_low = resid_grad.astype(jnp.bfloat16)
        selfproj_grad = left_product(mixed_one, branch_low)
        mixed_grad = right_product(branch_low, self_proj).astype(jnp.bfloat16)
        query_back, key_back, value_back, reltable_grad = attend_backward(
            query_one, key_one, value_one, mixed_grad, lse_one, context
        )
        qkv_back = jnp.concatenate([query_back, key_back, value_back], axis=1)
        selfqkv_grad = left_product(normed_one, qkv_back)
        normed_grad = right_product(qkv_back, self_full)
        norm_value, pull_norm = jax.vjp(rms_scale, resid_in, gain_one.astype(jnp.float32))
        back_resid, gainself_grad = pull_norm(normed_grad)
        hidden_grad = resid_grad + back_resid

        table_block_rows = table_rows
        table_cols = jnp.pad(
            reltable_grad.reshape(fsdp_size, table_block_rows, HEADS),
            ((0, 0), (0, shard_rows - table_block_rows), (0, 0)),
        ).reshape(width, HEADS)
        extra = jnp.concatenate(
            [
                gainffn_grad[:, None],
                gaincross_grad[:, None],
                gainself_grad[:, None],
                table_cols,
                jnp.zeros((width, 128 - 3 - HEADS), jnp.float32),
            ],
            axis=1,
        )
        attn_parts = [
            [crossproj_grad, crossquery_grad],
            [crosskv_grad],
            [selfproj_grad, extra],
            [selfqkv_grad[:, : 2 * width]],
            [selfqkv_grad[:, 2 * width :]],
        ]
        attn_parts, ffn_part = lax.optimization_barrier((attn_parts, ffn_part))
        ffn_owned = lax.all_gather(ffn_part, "replica", axis=0, tiled=True)
        attn_owned = tree_reduce(attn_parts, fsdp_size, replica_size)
        cross_owned = attn_owned[:, : 4 * width]
        extra_owned = attn_owned[:, 5 * width : 5 * width + 128].astype(jnp.float32)
        self_owned = jnp.concatenate(
            [attn_owned[:, 4 * width : 5 * width], attn_owned[:, 5 * width + 128 :]], axis=1
        )

        as_f32 = lambda v: v.astype(jnp.float32)
        return (
            layer_out,
            hidden_grad,
            encoder_grad,
            as_f32(self_owned[:, width : 2 * width]),
            as_f32(self_owned[:, 2 * width : 3 * width]),
            as_f32(self_owned[:, 3 * width : 4 * width]),
            as_f32(self_owned[:, 0:width]),
            as_f32(cross_owned[:, width : 2 * width]),
            as_f32(cross_owned[:, 2 * width : 3 * width]),
            as_f32(cross_owned[:, 3 * width : 4 * width]),
            as_f32(cross_owned[:, 0:width]),
            as_f32(ffn_owned[:, 0:ff_width]),
            as_f32(ffn_owned[:, ff_width : 2 * ff_width]),
            as_f32(ffn_owned[:, 2 * ff_width :].reshape(-1, width)),
            extra_owned[:, 2],
            extra_owned[:, 1],
            extra_owned[:, 0],
            extra_owned[:table_block_rows, 3 : 3 + HEADS],
        )

    return on_device


def solution(mesh):
    placed = (
        P(("fsdp", "replica"), None),
        P(("fsdp", "replica"), None),
        P(("fsdp", "replica"), None),
        P(("fsdp", "replica"), None),
        P("fsdp", None),
        P("fsdp", None),
        P("fsdp", None),
        P("fsdp", None),
        P("fsdp", None),
        P("fsdp", None),
        P("fsdp", None),
        P("fsdp", None),
        P("fsdp", None),
        P("fsdp", None),
        P("fsdp", None),
        P("fsdp"),
        P("fsdp"),
        P("fsdp"),
        P("fsdp", None),
    )
    return jax.shard_map(
        make_on_device(mesh.shape["fsdp"], mesh.shape["replica"]),
        mesh=mesh,
        in_specs=placed,
        out_specs=(
            P(("fsdp", "replica"), None),
            P(("fsdp", "replica"), None),
            P(("fsdp", "replica"), None),
            P("fsdp", None),
            P("fsdp", None),
            P("fsdp", None),
            P("fsdp", None),
            P("fsdp", None),
            P("fsdp", None),
            P("fsdp", None),
            P("fsdp", None),
            P("fsdp", None),
            P("fsdp", None),
            P("fsdp", None),
            P("fsdp"),
            P("fsdp"),
            P("fsdp"),
            P("fsdp", None),
        ),
        check_vma=False,
    )
```

```python
import jax
import jax.numpy as jnp
from jax import lax
from jax.sharding import PartitionSpec as P

HEADS = 12
HEAD_DIM = 64
BUCKETS = 32
QBLOCK = 512


EPS = 1e-06
NEG = -1000000000.0
EDGES = (1, 2, 3, 4, 5, 6, 7, 8, 12, 16, 23, 32, 46, 64, 91)


def rms_scale(hidden, gain):
    return hidden * lax.rsqrt(jnp.mean(hidden * hidden, axis=-1, keepdims=True) + EPS) * gain


def gated(gate, upper):
    return jax.nn.gelu(gate, approximate=True) * upper


def product(left, right):
    return jnp.dot(left, right, preferred_element_type=jnp.float32)


def left_product(left, right):
    return lax.dot_general(
        left, right, (((0,), (0,)), ((), ())), preferred_element_type=jnp.float32
    )


def right_product(left, right):
    return lax.dot_general(
        left, right, (((1,), (1,)), ((), ())), preferred_element_type=jnp.float32
    )


def split_heads(matrix):
    return matrix.reshape(matrix.shape[0], HEADS, HEAD_DIM)


def block_terms(context, block_rows, key_count):
    if context is None:
        return (None, None, None)
    rel_table, piece_ids = context
    query_pos = jnp.arange(block_rows, dtype=jnp.int32)
    key_pos = jnp.arange(key_count, dtype=jnp.int32)
    relative = key_pos[None, :] - query_pos[:, None]
    distance = jnp.abs(relative)
    bucket = 16 * (relative > 0).astype(jnp.int32)
    for edge_len in EDGES:
        bucket = bucket + (distance >= edge_len).astype(jnp.int32)
    onehot = (
        bucket.T[None, :, :] == jnp.arange(BUCKETS, dtype=jnp.int32)[:, None, None]
    ).astype(jnp.bfloat16)
    bias_block = jnp.swapaxes(
        lax.dot_general(
            rel_table, onehot, (((0,), (0,)), ((), ())), preferred_element_type=jnp.float32
        ),
        1,
        2,
    )
    allowed = (key_pos[None, :] <= query_pos[:, None]) | (piece_ids[None, :] == piece_ids[:, None])
    return (onehot, bias_block, allowed)


def block_scores(query_block, key_heads, bias_block, allowed):
    scores = jnp.einsum("qhd,khd->hqk", query_block, key_heads, preferred_element_type=jnp.float32)
    if bias_block is not None:
        scores = jnp.where(allowed[None], scores + bias_block, NEG)
    return scores


def attend_forward(queries, key_rows, value_rows, context):
    key_heads = split_heads(key_rows)
    value_heads = split_heads(value_rows)
    query_block = split_heads(queries)
    onehot, bias_block, allowed = block_terms(context, QBLOCK, key_rows.shape[0])
    scores = block_scores(query_block, key_heads, bias_block, allowed)
    row_max = jnp.max(scores, axis=-1, keepdims=True)
    raised = jnp.exp(scores - row_max)
    row_sum = jnp.sum(raised, axis=-1, keepdims=True)
    prob_low = (raised / row_sum).astype(jnp.bfloat16)
    mixed_block = jnp.einsum(
        "hqk,khd->qhd", prob_low, value_heads, preferred_element_type=jnp.float32
    )
    mixed_parts = mixed_block.reshape(QBLOCK, HEADS * HEAD_DIM).astype(jnp.bfloat16)
    lse_parts = row_max + jnp.log(row_sum)
    return (mixed_parts, lse_parts)


def attend_backward(queries, key_rows, value_rows, grad_mixed, lse_rows, context):
    key_count = key_rows.shape[0]
    key_heads = split_heads(key_rows)
    value_heads = split_heads(value_rows)
    table_grad = jnp.zeros((BUCKETS, HEADS), jnp.float32)
    query_block = split_heads(queries)
    grad_block = split_heads(grad_mixed)
    onehot, bias_block, allowed = block_terms(context, QBLOCK, key_count)
    scores = block_scores(query_block, key_heads, bias_block, allowed)
    probs = jnp.exp(scores - lse_rows)
    prob_low = probs.astype(jnp.bfloat16)
    grad_probs = jnp.einsum(
        "qhd,khd->hqk", grad_block, value_heads, preferred_element_type=jnp.float32
    )
    inner_sum = jnp.sum(probs * grad_probs, axis=-1, keepdims=True)
    grad_scores = (probs * (grad_probs - inner_sum)).astype(jnp.bfloat16)
    query_grad = jnp.einsum(
        "hqk,khd->qhd", grad_scores, key_heads, preferred_element_type=jnp.float32
    )
    query_parts = query_grad.reshape(QBLOCK, HEADS * HEAD_DIM).astype(jnp.bfloat16)
    key_grad = jnp.einsum(
        "hqk,qhd->khd", grad_scores, query_block, preferred_element_type=jnp.float32
    )
    value_grad = jnp.einsum(
        "hqk,qhd->khd", prob_low, grad_block, preferred_element_type=jnp.float32
    )
    if onehot is not None:
        table_grad = lax.dot_general(
            onehot,
            grad_scores,
            (((1, 2), (2, 1)), ((), ())),
            preferred_element_type=jnp.float32,
        )
    key_low = key_grad.reshape(key_count, HEADS * HEAD_DIM).astype(jnp.bfloat16)
    value_low = value_grad.reshape(key_count, HEADS * HEAD_DIM).astype(jnp.bfloat16)
    return (query_parts, key_low, value_low, table_grad)


def pairs_of(size, bit):
    return [(i, i ^ bit) for i in range(size)]


def tree_gather(shard, fsdp_size):
    me_f = lax.axis_index("fsdp")
    cur = shard[None]
    for b in range(fsdp_size.bit_length() - 1):
        bit = 1 << b
        mine = (me_f // bit) % 2
        recv = lax.ppermute(cur, "fsdp", pairs_of(fsdp_size, bit))
        low = jnp.where(mine == 0, cur, recv)
        high = jnp.where(mine == 0, recv, cur)
        cur = jnp.concatenate([low, high], axis=0)
    return cur.reshape(-1, shard.shape[1])


def tree_reduce(parts, fsdp_size, replica_size, carry=None):
    me_f = lax.axis_index("fsdp")
    me_r = lax.axis_index("replica")
    fsdp_bits = [1 << b for b in range(fsdp_size.bit_length() - 1)]
    rep_bits = [1 << b for b in range(replica_size.bit_length() - 1)]

    def fsdp_step(cur, bit):
        mine = (me_f // bit) % 2
        cur = cur.reshape(cur.shape[0] // 2, 2, cur.shape[1], cur.shape[2])
        keep = lax.dynamic_index_in_dim(cur, mine, axis=1, keepdims=False)
        send = lax.dynamic_index_in_dim(cur, 1 - mine, axis=1, keepdims=False)
        recv = lax.ppermute(send.astype(jnp.bfloat16), "fsdp", pairs_of(fsdp_size, bit))
        return keep + recv.astype(jnp.float32)

    def replica_step(cur, bit):
        mine = (me_r // bit) % 2
        cur = cur.reshape(cur.shape[0], 2, cur.shape[1] // 2, cur.shape[2])
        keep = lax.dynamic_index_in_dim(cur, mine, axis=1, keepdims=False)
        send = lax.dynamic_index_in_dim(cur, 1 - mine, axis=1, keepdims=False)
        recv = lax.ppermute(send.astype(jnp.bfloat16), "replica", pairs_of(replica_size, bit))
        return keep + recv.astype(jnp.float32)

    def replica_back(cur, bit):
        mine = (me_r // bit) % 2
        recv = lax.ppermute(cur, "replica", pairs_of(replica_size, bit))
        low = jnp.where(mine == 0, cur, recv)
        high = jnp.where(mine == 0, recv, cur)
        return jnp.concatenate([low, high], axis=1)

    firsts = []
    for pieces in parts:
        packed = jnp.concatenate(pieces, axis=1) if len(pieces) > 1 else pieces[0]
        rows = packed.shape[0] // fsdp_size
        cur = packed.reshape(fsdp_size, rows, packed.shape[1])
        firsts.append(fsdp_step(cur, fsdp_bits[0]))
    if carry is not None:
        firsts, carry = lax.optimization_barrier((firsts, carry))
    outs = []
    for part, cur in enumerate(firsts):
        rows = cur.shape[1]
        steps = [("f", bit) for bit in fsdp_bits[1:]] + [("r", bit) for bit in rep_bits]
        shift = part % len(steps) if steps else 0
        steps = steps[shift:] + steps[:shift]
        for kind, bit in steps:
            cur = fsdp_step(cur, bit) if kind == "f" else replica_step(cur, bit)
        rep_order = [bit for kind, bit in steps if kind == "r"]
        cur = cur.astype(jnp.bfloat16)
        for bit in reversed(rep_order):
            cur = replica_back(cur, bit)
        outs.append(cur.reshape(rows, -1))
    return jnp.concatenate(outs, axis=1), carry


def make_on_device(fsdp_size, replica_size):
    def on_device(
        hidden_in,
        encoder_states,
        output_grad,
        piece_starts,
        selfquery,
        selfkey,
        selfvalue,
        selfproj,
        crossquery,
        crosskey,
        crossvalue,
        crossproj,
        gateproj,
        upproj,
        downproj,
        gainself,
        gaincross,
        gainffn,
        reltable,
    ):
        shard_rows, width = selfquery.shape
        ff_width = gateproj.shape[1]
        table_rows = reltable.shape[0]
        self_packed = jnp.concatenate([selfquery, selfkey, selfvalue], axis=1)
        small_packed = jnp.concatenate(
            [gainself, gaincross, gainffn, reltable.reshape(-1)]
        )
        mid_packed = jnp.concatenate(
            [selfproj, crossquery, crosskey, crossvalue, crossproj], axis=1
        )
        ffn_packed = jnp.concatenate([gateproj, upproj], axis=1)
        self_full = lax.all_gather(self_packed, "fsdp", axis=0, tiled=True)
        small_full = lax.all_gather(small_packed, "fsdp", axis=0, tiled=False)
        mid_full = lax.all_gather(mid_packed, "fsdp", axis=0, tiled=True)
        ffn_full = lax.all_gather(ffn_packed, "fsdp", axis=0, tiled=True)

        gain_one = small_full[:, 0:shard_rows].reshape(-1)
        gain_two = small_full[:, shard_rows : 2 * shard_rows].reshape(-1)
        gain_three = small_full[:, 2 * shard_rows : 3 * shard_rows].reshape(-1)
        table_full = small_full[:, 3 * shard_rows :].reshape(-1, HEADS)
        self_proj = mid_full[:, 0:width]
        cross_query = mid_full[:, width : 2 * width]
        cross_kv = mid_full[:, 2 * width : 4 * width]
        cross_key = cross_kv[:, :width]
        cross_value = cross_kv[:, width:]
        cross_proj = mid_full[:, 4 * width : 5 * width]
        gate_up = ffn_full
        down_full = tree_gather(downproj, fsdp_size)

        length = hidden_in.shape[0]
        position = jnp.arange(length, dtype=jnp.int32)
        piece_ids = (
            jnp.sum((piece_starts[0][None, :] <= position[:, None]).astype(jnp.int32), axis=1) - 1
        )
        context = (table_full, piece_ids)
        resid_in = hidden_in.astype(jnp.float32)
        normed_one = rms_scale(resid_in, gain_one.astype(jnp.float32)).astype(jnp.bfloat16)
        qkv_one = product(normed_one, self_full).astype(jnp.bfloat16)
        query_one = qkv_one[:, :width]
        key_one = qkv_one[:, width : 2 * width]
        value_one = qkv_one[:, 2 * width :]
        mixed_one, lse_one = attend_forward(query_one, key_one, value_one, context)
        after_self = resid_in + product(mixed_one, self_proj)
        normed_two = rms_scale(after_self, gain_two.astype(jnp.float32)).astype(jnp.bfloat16)
        query_two = product(normed_two, cross_query).astype(jnp.bfloat16)
        kv_two = product(encoder_states, cross_kv).astype(jnp.bfloat16)
        key_two = kv_two[:, :width]
        value_two = kv_two[:, width:]
        mixed_two, lse_two = attend_forward(query_two, key_two, value_two, None)
        after_cross = after_self + product(mixed_two, cross_proj)
        normed_three = rms_scale(after_cross, gain_three.astype(jnp.float32)).astype(jnp.bfloat16)
        gate_upper = product(normed_three, gate_up)
        gate_pre = gate_upper[:, :ff_width]
        upper_pre = gate_upper[:, ff_width:]
        inner = gated(gate_pre, upper_pre).astype(jnp.bfloat16)
        layer_out = (after_cross + product(inner, down_full)).astype(jnp.bfloat16)

        def reduce_rows(packed):
            return lax.psum_scatter(
                packed.astype(jnp.bfloat16), ("fsdp", "replica"), scatter_dimension=0, tiled=True
            )

        downproj_grad = left_product(inner, output_grad)
        inner_grad = right_product(output_grad, down_full)
        gated_value, pull_gate = jax.vjp(gated, gate_pre, upper_pre)
        gate_grad, upper_grad = pull_gate(inner_grad)
        gate_upper_low = jnp.concatenate(
            [gate_grad.astype(jnp.bfloat16), upper_grad.astype(jnp.bfloat16)], axis=1
        )
        gate_up_grad = left_product(normed_three, gate_upper_low)
        ffn_packed = jnp.concatenate(
            [gate_up_grad, downproj_grad.reshape(width, ff_width)], axis=1
        ).astype(jnp.bfloat16)
        normed_grad = right_product(gate_upper_low, gate_up)
        norm_value, pull_norm = jax.vjp(rms_scale, after_cross, gain_three.astype(jnp.float32))
        back_resid, gainffn_grad = pull_norm(normed_grad)
        ffn_packed, back_resid = lax.optimization_barrier((ffn_packed, back_resid))
        ffn_part = reduce_rows(ffn_packed)
        resid_grad = output_grad.astype(jnp.float32) + back_resid
        branch_low = resid_grad.astype(jnp.bfloat16)
        crossproj_grad = left_product(mixed_two, branch_low)
        mixed_grad = right_product(branch_low, cross_proj).astype(jnp.bfloat16)
        query_back, key_back, value_back, unused_table = attend_backward(
            query_two, key_two, value_two, mixed_grad, lse_two, None
        )
        crossquery_grad = left_product(normed_two, query_back)
        kv_back = jnp.concatenate([key_back, value_back], axis=1)
        crosskv_grad = left_product(encoder_states, kv_back)
        encoder_grad = right_product(kv_back, cross_kv)
        normed_grad = right_product(query_back, cross_query)
        norm_value, pull_norm = jax.vjp(rms_scale, after_self, gain_two.astype(jnp.float32))
        back_resid, gaincross_grad = pull_norm(normed_grad)
        resid_grad = resid_grad + back_resid
        branch_low = resid_grad.astype(jnp.bfloat16)
        selfproj_grad = left_product(mixed_one, branch_low)
        mixed_grad = right_product(branch_low, self_proj).astype(jnp.bfloat16)
        query_back, key_back, value_back, reltable_grad = attend_backward(
            query_one, key_one, value_one, mixed_grad, lse_one, context
        )
        qkv_back = jnp.concatenate([query_back, key_back, value_back], axis=1)
        selfqkv_grad = left_product(normed_one, qkv_back)
        normed_grad = right_product(qkv_back, self_full)
        norm_value, pull_norm = jax.vjp(rms_scale, resid_in, gain_one.astype(jnp.float32))
        back_resid, gainself_grad = pull_norm(normed_grad)
        hidden_grad = resid_grad + back_resid

        table_block_rows = table_rows
        table_cols = jnp.pad(
            reltable_grad.reshape(fsdp_size, table_block_rows, HEADS),
            ((0, 0), (0, shard_rows - table_block_rows), (0, 0)),
        ).reshape(width, HEADS)
        extra = jnp.concatenate(
            [
                gainffn_grad[:, None],
                gaincross_grad[:, None],
                gainself_grad[:, None],
                table_cols,
                jnp.zeros((width, 128 - 3 - HEADS), jnp.float32),
            ],
            axis=1,
        )
        attn_parts = [
            [crossproj_grad, crossquery_grad],
            [crosskv_grad],
            [selfproj_grad, extra],
            [selfqkv_grad[:, : 2 * width]],
            [selfqkv_grad[:, 2 * width :]],
        ]
        attn_owned, ffn_part = tree_reduce(attn_parts, fsdp_size, replica_size, carry=ffn_part)
        ffn_owned = lax.all_gather(ffn_part, "replica", axis=0, tiled=True)
        cross_owned = attn_owned[:, : 4 * width]
        extra_owned = attn_owned[:, 5 * width : 5 * width + 128].astype(jnp.float32)
        self_owned = jnp.concatenate(
            [attn_owned[:, 4 * width : 5 * width], attn_owned[:, 5 * width + 128 :]], axis=1
        )

        as_f32 = lambda v: v.astype(jnp.float32)
        return (
            layer_out,
            hidden_grad,
            encoder_grad,
            as_f32(self_owned[:, width : 2 * width]),
            as_f32(self_owned[:, 2 * width : 3 * width]),
            as_f32(self_owned[:, 3 * width : 4 * width]),
            as_f32(self_owned[:, 0:width]),
            as_f32(cross_owned[:, width : 2 * width]),
            as_f32(cross_owned[:, 2 * width : 3 * width]),
            as_f32(cross_owned[:, 3 * width : 4 * width]),
            as_f32(cross_owned[:, 0:width]),
            as_f32(ffn_owned[:, 0:ff_width]),
            as_f32(ffn_owned[:, ff_width : 2 * ff_width]),
            as_f32(ffn_owned[:, 2 * ff_width :].reshape(-1, width)),
            extra_owned[:, 2],
            extra_owned[:, 1],
            extra_owned[:, 0],
            extra_owned[:table_block_rows, 3 : 3 + HEADS],
        )

    return on_device


def solution(mesh):
    placed = (
        P(("fsdp", "replica"), None),
        P(("fsdp", "replica"), None),
        P(("fsdp", "replica"), None),
        P(("fsdp", "replica"), None),
        P("fsdp", None),
        P("fsdp", None),
        P("fsdp", None),
        P("fsdp", None),
        P("fsdp", None),
        P("fsdp", None),
        P("fsdp", None),
        P("fsdp", None),
        P("fsdp", None),
        P("fsdp", None),
        P("fsdp", None),
        P("fsdp"),
        P("fsdp"),
        P("fsdp"),
        P("fsdp", None),
    )
    return jax.shard_map(
        make_on_device(mesh.shape["fsdp"], mesh.shape["replica"]),
        mesh=mesh,
        in_specs=placed,
        out_specs=(
            P(("fsdp", "replica"), None),
            P(("fsdp", "replica"), None),
            P(("fsdp", "replica"), None),
            P("fsdp", None),
            P("fsdp", None),
            P("fsdp", None),
            P("fsdp", None),
            P("fsdp", None),
            P("fsdp", None),
            P("fsdp", None),
            P("fsdp", None),
            P("fsdp", None),
            P("fsdp", None),
            P("fsdp", None),
            P("fsdp"),
            P("fsdp"),
            P("fsdp"),
            P("fsdp", None),
        ),
        check_vma=False,
    )
```

```python
import jax
import jax.numpy as jnp
from jax import lax
from jax.sharding import PartitionSpec as P

HEADS = 12
HEAD_DIM = 64
BUCKETS = 32
QBLOCK = 512


EPS = 1e-06
NEG = -1000000000.0
EDGES = (1, 2, 3, 4, 5, 6, 7, 8, 12, 16, 23, 32, 46, 64, 91)


def rms_scale(hidden, gain):
    return hidden * lax.rsqrt(jnp.mean(hidden * hidden, axis=-1, keepdims=True) + EPS) * gain


def gated(gate, upper):
    return jax.nn.gelu(gate, approximate=True) * upper


def product(left, right):
    return jnp.dot(left, right, preferred_element_type=jnp.float32)


def left_product(left, right):
    return lax.dot_general(
        left, right, (((0,), (0,)), ((), ())), preferred_element_type=jnp.float32
    )


def right_product(left, right):
    return lax.dot_general(
        left, right, (((1,), (1,)), ((), ())), preferred_element_type=jnp.float32
    )


def split_heads(matrix):
    return matrix.reshape(matrix.shape[0], HEADS, HEAD_DIM)


def block_terms(context, block_rows, key_count):
    if context is None:
        return (None, None, None)
    rel_table, piece_ids = context
    query_pos = jnp.arange(block_rows, dtype=jnp.int32)
    key_pos = jnp.arange(key_count, dtype=jnp.int32)
    relative = key_pos[None, :] - query_pos[:, None]
    distance = jnp.abs(relative)
    bucket = 16 * (relative > 0).astype(jnp.int32)
    for edge_len in EDGES:
        bucket = bucket + (distance >= edge_len).astype(jnp.int32)
    onehot = (
        bucket.T[None, :, :] == jnp.arange(BUCKETS, dtype=jnp.int32)[:, None, None]
    ).astype(jnp.bfloat16)
    bias_block = jnp.swapaxes(
        lax.dot_general(
            rel_table, onehot, (((0,), (0,)), ((), ())), preferred_element_type=jnp.float32
        ),
        1,
        2,
    )
    allowed = (key_pos[None, :] <= query_pos[:, None]) | (piece_ids[None, :] == piece_ids[:, None])
    return (onehot, bias_block, allowed)


def block_scores(query_block, key_heads, bias_block, allowed):
    scores = jnp.einsum("qhd,khd->hqk", query_block, key_heads, preferred_element_type=jnp.float32)
    if bias_block is not None:
        scores = jnp.where(allowed[None], scores + bias_block, NEG)
    return scores


def attend_forward(queries, key_rows, value_rows, context):
    key_heads = split_heads(key_rows)
    value_heads = split_heads(value_rows)
    query_block = split_heads(queries)
    onehot, bias_block, allowed = block_terms(context, QBLOCK, key_rows.shape[0])
    scores = block_scores(query_block, key_heads, bias_block, allowed)
    row_max = jnp.max(scores, axis=-1, keepdims=True)
    raised = jnp.exp(scores - row_max)
    row_sum = jnp.sum(raised, axis=-1, keepdims=True)
    prob_low = (raised / row_sum).astype(jnp.bfloat16)
    mixed_block = jnp.einsum(
        "hqk,khd->qhd", prob_low, value_heads, preferred_element_type=jnp.float32
    )
    mixed_parts = mixed_block.reshape(QBLOCK, HEADS * HEAD_DIM).astype(jnp.bfloat16)
    lse_parts = row_max + jnp.log(row_sum)
    return (mixed_parts, lse_parts)


def attend_backward(queries, key_rows, value_rows, grad_mixed, lse_rows, context):
    key_count = key_rows.shape[0]
    key_heads = split_heads(key_rows)
    value_heads = split_heads(value_rows)
    table_grad = jnp.zeros((BUCKETS, HEADS), jnp.float32)
    query_block = split_heads(queries)
    grad_block = split_heads(grad_mixed)
    onehot, bias_block, allowed = block_terms(context, QBLOCK, key_count)
    scores = block_scores(query_block, key_heads, bias_block, allowed)
    probs = jnp.exp(scores - lse_rows)
    prob_low = probs.astype(jnp.bfloat16)
    grad_probs = jnp.einsum(
        "qhd,khd->hqk", grad_block, value_heads, preferred_element_type=jnp.float32
    )
    inner_sum = jnp.sum(probs * grad_probs, axis=-1, keepdims=True)
    grad_scores = (probs * (grad_probs - inner_sum)).astype(jnp.bfloat16)
    query_grad = jnp.einsum(
        "hqk,khd->qhd", grad_scores, key_heads, preferred_element_type=jnp.float32
    )
    query_parts = query_grad.reshape(QBLOCK, HEADS * HEAD_DIM).astype(jnp.bfloat16)
    key_grad = jnp.einsum(
        "hqk,qhd->khd", grad_scores, query_block, preferred_element_type=jnp.float32
    )
    value_grad = jnp.einsum(
        "hqk,qhd->khd", prob_low, grad_block, preferred_element_type=jnp.float32
    )
    if onehot is not None:
        table_grad = lax.dot_general(
            onehot,
            grad_scores,
            (((1, 2), (2, 1)), ((), ())),
            preferred_element_type=jnp.float32,
        )
    key_low = key_grad.reshape(key_count, HEADS * HEAD_DIM).astype(jnp.bfloat16)
    value_low = value_grad.reshape(key_count, HEADS * HEAD_DIM).astype(jnp.bfloat16)
    return (query_parts, key_low, value_low, table_grad)


def pairs_of(size, bit):
    return [(i, i ^ bit) for i in range(size)]


def tree_gather(shard, fsdp_size):
    me_f = lax.axis_index("fsdp")
    cur = shard
    levels = fsdp_size.bit_length() - 1
    for k in range(levels):
        bit = 1 << (levels - 1 - k)
        mine = (me_f // bit) % 2
        recv = lax.ppermute(cur, "fsdp", pairs_of(fsdp_size, bit))
        cur = jnp.where(
            mine == 0, jnp.stack([cur, recv], axis=k), jnp.stack([recv, cur], axis=k)
        )
    return cur.reshape(-1, shard.shape[1])


def tree_reduce(parts, fsdp_size, replica_size, carry=None):
    me_f = lax.axis_index("fsdp")
    me_r = lax.axis_index("replica")
    fsdp_bits = [1 << b for b in range(fsdp_size.bit_length() - 1)]
    rep_bits = [1 << b for b in range(replica_size.bit_length() - 1)]

    def fsdp_step(cur, bit):
        mine = (me_f // bit) % 2
        cur = cur.reshape(cur.shape[0] // 2, 2, cur.shape[1], cur.shape[2])
        keep = lax.dynamic_index_in_dim(cur, mine, axis=1, keepdims=False)
        send = lax.dynamic_index_in_dim(cur, 1 - mine, axis=1, keepdims=False)
        recv = lax.ppermute(send.astype(jnp.bfloat16), "fsdp", pairs_of(fsdp_size, bit))
        return keep + recv.astype(jnp.float32)

    def replica_step(cur, bit):
        mine = (me_r // bit) % 2
        cur = cur.reshape(cur.shape[0], 2, cur.shape[1] // 2, cur.shape[2])
        keep = lax.dynamic_index_in_dim(cur, mine, axis=1, keepdims=False)
        send = lax.dynamic_index_in_dim(cur, 1 - mine, axis=1, keepdims=False)
        recv = lax.ppermute(send.astype(jnp.bfloat16), "replica", pairs_of(replica_size, bit))
        return keep + recv.astype(jnp.float32)

    def replica_back(cur, bit):
        mine = (me_r // bit) % 2
        recv = lax.ppermute(cur, "replica", pairs_of(replica_size, bit))
        low = jnp.where(mine == 0, cur, recv)
        high = jnp.where(mine == 0, recv, cur)
        return jnp.concatenate([low, high], axis=1)

    firsts = []
    for pieces in parts:
        packed = jnp.concatenate(pieces, axis=1) if len(pieces) > 1 else pieces[0]
        rows = packed.shape[0] // fsdp_size
        cur = packed.reshape(fsdp_size, rows, packed.shape[1])
        firsts.append(fsdp_step(cur, fsdp_bits[0]))
    if carry is not None:
        firsts, carry = lax.optimization_barrier((firsts, carry))
    outs = []
    for part, cur in enumerate(firsts):
        rows = cur.shape[1]
        steps = [("f", bit) for bit in fsdp_bits[1:]] + [("r", bit) for bit in rep_bits]
        shift = part % len(steps) if steps else 0
        steps = steps[shift:] + steps[:shift]
        for kind, bit in steps:
            cur = fsdp_step(cur, bit) if kind == "f" else replica_step(cur, bit)
        rep_order = [bit for kind, bit in steps if kind == "r"]
        cur = cur.astype(jnp.bfloat16)
        for bit in reversed(rep_order):
            cur = replica_back(cur, bit)
        outs.append(cur.reshape(rows, -1))
    return jnp.concatenate(outs, axis=1), carry


def make_on_device(fsdp_size, replica_size):
    def on_device(
        hidden_in,
        encoder_states,
        output_grad,
        piece_starts,
        selfquery,
        selfkey,
        selfvalue,
        selfproj,
        crossquery,
        crosskey,
        crossvalue,
        crossproj,
        gateproj,
        upproj,
        downproj,
        gainself,
        gaincross,
        gainffn,
        reltable,
    ):
        shard_rows, width = selfquery.shape
        ff_width = gateproj.shape[1]
        table_rows = reltable.shape[0]
        self_packed = jnp.concatenate([selfquery, selfkey, selfvalue], axis=1)
        small_packed = jnp.concatenate(
            [gainself, gaincross, gainffn, reltable.reshape(-1)]
        )
        mid_packed = jnp.concatenate(
            [selfproj, crossquery, crosskey, crossvalue, crossproj], axis=1
        )
        ffn_packed = jnp.concatenate([gateproj, upproj], axis=1)
        self_full = lax.all_gather(self_packed, "fsdp", axis=0, tiled=True)
        small_full = lax.all_gather(small_packed, "fsdp", axis=0, tiled=False)
        mid_full = lax.all_gather(mid_packed, "fsdp", axis=0, tiled=True)
        ffn_full = lax.all_gather(ffn_packed, "fsdp", axis=0, tiled=True)

        gain_one = small_full[:, 0:shard_rows].reshape(-1)
        gain_two = small_full[:, shard_rows : 2 * shard_rows].reshape(-1)
        gain_three = small_full[:, 2 * shard_rows : 3 * shard_rows].reshape(-1)
        table_full = small_full[:, 3 * shard_rows :].reshape(-1, HEADS)
        self_proj = mid_full[:, 0:width]
        cross_query = mid_full[:, width : 2 * width]
        cross_kv = mid_full[:, 2 * width : 4 * width]
        cross_key = cross_kv[:, :width]
        cross_value = cross_kv[:, width:]
        cross_proj = mid_full[:, 4 * width : 5 * width]
        gate_up = ffn_full
        down_full = tree_gather(downproj, fsdp_size)

        length = hidden_in.shape[0]
        position = jnp.arange(length, dtype=jnp.int32)
        piece_ids = (
            jnp.sum((piece_starts[0][None, :] <= position[:, None]).astype(jnp.int32), axis=1) - 1
        )
        context = (table_full, piece_ids)
        resid_in = hidden_in.astype(jnp.float32)
        normed_one = rms_scale(resid_in, gain_one.astype(jnp.float32)).astype(jnp.bfloat16)
        qkv_one = product(normed_one, self_full).astype(jnp.bfloat16)
        query_one = qkv_one[:, :width]
        key_one = qkv_one[:, width : 2 * width]
        value_one = qkv_one[:, 2 * width :]
        mixed_one, lse_one = attend_forward(query_one, key_one, value_one, context)
        after_self = resid_in + product(mixed_one, self_proj)
        normed_two = rms_scale(after_self, gain_two.astype(jnp.float32)).astype(jnp.bfloat16)
        query_two = product(normed_two, cross_query).astype(jnp.bfloat16)
        kv_two = product(encoder_states, cross_kv).astype(jnp.bfloat16)
        key_two = kv_two[:, :width]
        value_two = kv_two[:, width:]
        mixed_two, lse_two = attend_forward(query_two, key_two, value_two, None)
        after_cross = after_self + product(mixed_two, cross_proj)
        normed_three = rms_scale(after_cross, gain_three.astype(jnp.float32)).astype(jnp.bfloat16)
        gate_upper = product(normed_three, gate_up)
        gate_pre = gate_upper[:, :ff_width]
        upper_pre = gate_upper[:, ff_width:]
        inner = gated(gate_pre, upper_pre).astype(jnp.bfloat16)
        layer_out = (after_cross + product(inner, down_full)).astype(jnp.bfloat16)

        def reduce_rows(packed):
            return lax.psum_scatter(
                packed.astype(jnp.bfloat16), ("fsdp", "replica"), scatter_dimension=0, tiled=True
            )

        downproj_grad = left_product(inner, output_grad)
        inner_grad = right_product(output_grad, down_full)
        gated_value, pull_gate = jax.vjp(gated, gate_pre, upper_pre)
        gate_grad, upper_grad = pull_gate(inner_grad)
        gate_upper_low = jnp.concatenate(
            [gate_grad.astype(jnp.bfloat16), upper_grad.astype(jnp.bfloat16)], axis=1
        )
        gate_up_grad = left_product(normed_three, gate_upper_low)
        ffn_packed = jnp.concatenate(
            [gate_up_grad, downproj_grad.reshape(width, ff_width)], axis=1
        ).astype(jnp.bfloat16)
        normed_grad = right_product(gate_upper_low, gate_up)
        norm_value, pull_norm = jax.vjp(rms_scale, after_cross, gain_three.astype(jnp.float32))
        back_resid, gainffn_grad = pull_norm(normed_grad)
        ffn_packed, back_resid = lax.optimization_barrier((ffn_packed, back_resid))
        ffn_part = reduce_rows(ffn_packed)
        resid_grad = output_grad.astype(jnp.float32) + back_resid
        branch_low = resid_grad.astype(jnp.bfloat16)
        crossproj_grad = left_product(mixed_two, branch_low)
        mixed_grad = right_product(branch_low, cross_proj).astype(jnp.bfloat16)
        query_back, key_back, value_back, unused_table = attend_backward(
            query_two, key_two, value_two, mixed_grad, lse_two, None
        )
        crossquery_grad = left_product(normed_two, query_back)
        kv_back = jnp.concatenate([key_back, value_back], axis=1)
        crosskv_grad = left_product(encoder_states, kv_back)
        encoder_grad = right_product(kv_back, cross_kv)
        normed_grad = right_product(query_back, cross_query)
        norm_value, pull_norm = jax.vjp(rms_scale, after_self, gain_two.astype(jnp.float32))
        back_resid, gaincross_grad = pull_norm(normed_grad)
        resid_grad = resid_grad + back_resid
        branch_low = resid_grad.astype(jnp.bfloat16)
        selfproj_grad = left_product(mixed_one, branch_low)
        mixed_grad = right_product(branch_low, self_proj).astype(jnp.bfloat16)
        query_back, key_back, value_back, reltable_grad = attend_backward(
            query_one, key_one, value_one, mixed_grad, lse_one, context
        )
        qkv_back = jnp.concatenate([query_back, key_back, value_back], axis=1)
        selfqkv_grad = left_product(normed_one, qkv_back)
        normed_grad = right_product(qkv_back, self_full)
        norm_value, pull_norm = jax.vjp(rms_scale, resid_in, gain_one.astype(jnp.float32))
        back_resid, gainself_grad = pull_norm(normed_grad)
        hidden_grad = resid_grad + back_resid

        table_block_rows = table_rows
        table_cols = jnp.pad(
            reltable_grad.reshape(fsdp_size, table_block_rows, HEADS),
            ((0, 0), (0, shard_rows - table_block_rows), (0, 0)),
        ).reshape(width, HEADS)
        extra = jnp.concatenate(
            [
                gainffn_grad[:, None],
                gaincross_grad[:, None],
                gainself_grad[:, None],
                table_cols,
                jnp.zeros((width, 128 - 3 - HEADS), jnp.float32),
            ],
            axis=1,
        )
        attn_parts = [
            [crossproj_grad, crossquery_grad],
            [crosskv_grad],
            [selfproj_grad, extra],
            [selfqkv_grad[:, : 2 * width]],
            [selfqkv_grad[:, 2 * width :]],
        ]
        attn_owned, ffn_part = tree_reduce(attn_parts, fsdp_size, replica_size, carry=ffn_part)
        ffn_owned = lax.all_gather(ffn_part, "replica", axis=0, tiled=True)
        cross_owned = attn_owned[:, : 4 * width]
        extra_owned = attn_owned[:, 5 * width : 5 * width + 128].astype(jnp.float32)
        self_owned = jnp.concatenate(
            [attn_owned[:, 4 * width : 5 * width], attn_owned[:, 5 * width + 128 :]], axis=1
        )

        as_f32 = lambda v: v.astype(jnp.float32)
        return (
            layer_out,
            hidden_grad,
            encoder_grad,
            as_f32(self_owned[:, width : 2 * width]),
            as_f32(self_owned[:, 2 * width : 3 * width]),
            as_f32(self_owned[:, 3 * width : 4 * width]),
            as_f32(self_owned[:, 0:width]),
            as_f32(cross_owned[:, width : 2 * width]),
            as_f32(cross_owned[:, 2 * width : 3 * width]),
            as_f32(cross_owned[:, 3 * width : 4 * width]),
            as_f32(cross_owned[:, 0:width]),
            as_f32(ffn_owned[:, 0:ff_width]),
            as_f32(ffn_owned[:, ff_width : 2 * ff_width]),
            as_f32(ffn_owned[:, 2 * ff_width :].reshape(-1, width)),
            extra_owned[:, 2],
            extra_owned[:, 1],
            extra_owned[:, 0],
            extra_owned[:table_block_rows, 3 : 3 + HEADS],
        )

    return on_device


def solution(mesh):
    placed = (
        P(("fsdp", "replica"), None),
        P(("fsdp", "replica"), None),
        P(("fsdp", "replica"), None),
        P(("fsdp", "replica"), None),
        P("fsdp", None),
        P("fsdp", None),
        P("fsdp", None),
        P("fsdp", None),
        P("fsdp", None),
        P("fsdp", None),
        P("fsdp", None),
        P("fsdp", None),
        P("fsdp", None),
        P("fsdp", None),
        P("fsdp", None),
        P("fsdp"),
        P("fsdp"),
        P("fsdp"),
        P("fsdp", None),
    )
    return jax.shard_map(
        make_on_device(mesh.shape["fsdp"], mesh.shape["replica"]),
        mesh=mesh,
        in_specs=placed,
        out_specs=(
            P(("fsdp", "replica"), None),
            P(("fsdp", "replica"), None),
            P(("fsdp", "replica"), None),
            P("fsdp", None),
            P("fsdp", None),
            P("fsdp", None),
            P("fsdp", None),
            P("fsdp", None),
            P("fsdp", None),
            P("fsdp", None),
            P("fsdp", None),
            P("fsdp", None),
            P("fsdp", None),
            P("fsdp", None),
            P("fsdp"),
            P("fsdp"),
            P("fsdp"),
            P("fsdp", None),
        ),
        check_vma=False,
    )
```

```python
import jax
import jax.numpy as jnp
from jax import lax
from jax.sharding import PartitionSpec as P

HEADS = 12
HEAD_DIM = 64
BUCKETS = 32
QBLOCK = 512


EPS = 1e-06
NEG = -1000000000.0
EDGES = (1, 2, 3, 4, 5, 6, 7, 8, 12, 16, 23, 32, 46, 64, 91)


def rms_scale(hidden, gain):
    return hidden * lax.rsqrt(jnp.mean(hidden * hidden, axis=-1, keepdims=True) + EPS) * gain


def gated(gate, upper):
    return jax.nn.gelu(gate, approximate=True) * upper


def product(left, right):
    return jnp.dot(left, right, preferred_element_type=jnp.float32)


def left_product(left, right):
    return lax.dot_general(
        left, right, (((0,), (0,)), ((), ())), preferred_element_type=jnp.float32
    )


def right_product(left, right):
    return lax.dot_general(
        left, right, (((1,), (1,)), ((), ())), preferred_element_type=jnp.float32
    )


def split_heads(matrix):
    return matrix.reshape(matrix.shape[0], HEADS, HEAD_DIM)


def block_terms(context, block_rows, key_count):
    if context is None:
        return (None, None, None)
    rel_table, piece_ids = context
    query_pos = jnp.arange(block_rows, dtype=jnp.int32)
    key_pos = jnp.arange(key_count, dtype=jnp.int32)
    relative = key_pos[None, :] - query_pos[:, None]
    distance = jnp.abs(relative)
    bucket = 16 * (relative > 0).astype(jnp.int32)
    for edge_len in EDGES:
        bucket = bucket + (distance >= edge_len).astype(jnp.int32)
    onehot = (
        bucket.T[None, :, :] == jnp.arange(BUCKETS, dtype=jnp.int32)[:, None, None]
    ).astype(jnp.bfloat16)
    bias_block = jnp.swapaxes(
        lax.dot_general(
            rel_table, onehot, (((0,), (0,)), ((), ())), preferred_element_type=jnp.float32
        ),
        1,
        2,
    )
    allowed = (key_pos[None, :] <= query_pos[:, None]) | (piece_ids[None, :] == piece_ids[:, None])
    return (onehot, bias_block, allowed)


def block_scores(query_block, key_heads, bias_block, allowed):
    scores = jnp.einsum("qhd,khd->hqk", query_block, key_heads, preferred_element_type=jnp.float32)
    if bias_block is not None:
        scores = jnp.where(allowed[None], scores + bias_block, NEG)
    return scores


def attend_forward(queries, key_rows, value_rows, context):
    key_heads = split_heads(key_rows)
    value_heads = split_heads(value_rows)
    query_block = split_heads(queries)
    onehot, bias_block, allowed = block_terms(context, QBLOCK, key_rows.shape[0])
    scores = block_scores(query_block, key_heads, bias_block, allowed)
    row_max = jnp.max(scores, axis=-1, keepdims=True)
    raised = jnp.exp(scores - row_max)
    row_sum = jnp.sum(raised, axis=-1, keepdims=True)
    prob_low = (raised / row_sum).astype(jnp.bfloat16)
    mixed_block = jnp.einsum(
        "hqk,khd->qhd", prob_low, value_heads, preferred_element_type=jnp.float32
    )
    mixed_parts = mixed_block.reshape(QBLOCK, HEADS * HEAD_DIM).astype(jnp.bfloat16)
    lse_parts = row_max + jnp.log(row_sum)
    return (mixed_parts, lse_parts)


def attend_backward(queries, key_rows, value_rows, grad_mixed, lse_rows, context):
    key_count = key_rows.shape[0]
    key_heads = split_heads(key_rows)
    value_heads = split_heads(value_rows)
    table_grad = jnp.zeros((BUCKETS, HEADS), jnp.float32)
    query_block = split_heads(queries)
    grad_block = split_heads(grad_mixed)
    onehot, bias_block, allowed = block_terms(context, QBLOCK, key_count)
    scores = block_scores(query_block, key_heads, bias_block, allowed)
    probs = jnp.exp(scores - lse_rows)
    prob_low = probs.astype(jnp.bfloat16)
    grad_probs = jnp.einsum(
        "qhd,khd->hqk", grad_block, value_heads, preferred_element_type=jnp.float32
    )
    inner_sum = jnp.sum(probs * grad_probs, axis=-1, keepdims=True)
    grad_scores = (probs * (grad_probs - inner_sum)).astype(jnp.bfloat16)
    query_grad = jnp.einsum(
        "hqk,khd->qhd", grad_scores, key_heads, preferred_element_type=jnp.float32
    )
    query_parts = query_grad.reshape(QBLOCK, HEADS * HEAD_DIM).astype(jnp.bfloat16)
    key_grad = jnp.einsum(
        "hqk,qhd->khd", grad_scores, query_block, preferred_element_type=jnp.float32
    )
    value_grad = jnp.einsum(
        "hqk,qhd->khd", prob_low, grad_block, preferred_element_type=jnp.float32
    )
    if onehot is not None:
        table_grad = lax.dot_general(
            onehot,
            grad_scores,
            (((1, 2), (2, 1)), ((), ())),
            preferred_element_type=jnp.float32,
        )
    key_low = key_grad.reshape(key_count, HEADS * HEAD_DIM).astype(jnp.bfloat16)
    value_low = value_grad.reshape(key_count, HEADS * HEAD_DIM).astype(jnp.bfloat16)
    return (query_parts, key_low, value_low, table_grad)


def pairs_of(size, bit):
    return [(i, i ^ bit) for i in range(size)]


def tree_gather(shard, fsdp_size):
    me_f = lax.axis_index("fsdp")
    cur = shard
    levels = fsdp_size.bit_length() - 1
    for k in range(levels):
        bit = 1 << (levels - 1 - k)
        mine = (me_f // bit) % 2
        recv = lax.ppermute(cur, "fsdp", pairs_of(fsdp_size, bit))
        cur = jnp.where(
            mine == 0, jnp.stack([cur, recv], axis=k), jnp.stack([recv, cur], axis=k)
        )
    return cur.reshape(-1, shard.shape[1])


def tree_reduce(parts, fsdp_size, replica_size, carry=None):
    me_f = lax.axis_index("fsdp")
    me_r = lax.axis_index("replica")
    fsdp_bits = [1 << b for b in range(fsdp_size.bit_length() - 1)]
    rep_bits = [1 << b for b in range(replica_size.bit_length() - 1)]

    def fsdp_step(cur, bit):
        mine = (me_f // bit) % 2
        cur = cur.reshape(cur.shape[0] // 2, 2, cur.shape[1], cur.shape[2])
        keep = lax.dynamic_index_in_dim(cur, mine, axis=1, keepdims=False)
        send = lax.dynamic_index_in_dim(cur, 1 - mine, axis=1, keepdims=False)
        recv = lax.ppermute(send.astype(jnp.bfloat16), "fsdp", pairs_of(fsdp_size, bit))
        return keep + recv.astype(jnp.float32)

    def replica_step(cur, bit):
        mine = (me_r // bit) % 2
        cur = cur.reshape(cur.shape[0], 2, cur.shape[1] // 2, cur.shape[2])
        keep = lax.dynamic_index_in_dim(cur, mine, axis=1, keepdims=False)
        send = lax.dynamic_index_in_dim(cur, 1 - mine, axis=1, keepdims=False)
        recv = lax.ppermute(send.astype(jnp.bfloat16), "replica", pairs_of(replica_size, bit))
        return keep + recv.astype(jnp.float32)

    def replica_back(cur, bit):
        mine = (me_r // bit) % 2
        recv = lax.ppermute(cur, "replica", pairs_of(replica_size, bit))
        low = jnp.where(mine == 0, cur, recv)
        high = jnp.where(mine == 0, recv, cur)
        return jnp.concatenate([low, high], axis=1)

    firsts = []
    for pieces in parts:
        packed = jnp.concatenate(pieces, axis=1) if len(pieces) > 1 else pieces[0]
        rows = packed.shape[0] // fsdp_size
        cur = packed.reshape(fsdp_size, rows, packed.shape[1])
        firsts.append(fsdp_step(cur, fsdp_bits[0]))
    if carry is not None:
        firsts, carry = lax.optimization_barrier((firsts, carry))
    outs = []
    for part, cur in enumerate(firsts):
        rows = cur.shape[1]
        steps = [("f", bit) for bit in fsdp_bits[1:]] + [("r", bit) for bit in rep_bits]
        shift = part % len(steps) if steps else 0
        steps = steps[shift:] + steps[:shift]
        for kind, bit in steps:
            cur = fsdp_step(cur, bit) if kind == "f" else replica_step(cur, bit)
        rep_order = [bit for kind, bit in steps if kind == "r"]
        cur = cur.astype(jnp.bfloat16)
        for bit in reversed(rep_order):
            cur = replica_back(cur, bit)
        outs.append(cur.reshape(rows, -1))
    return jnp.concatenate(outs, axis=1), carry


def make_on_device(fsdp_size, replica_size):
    def on_device(
        hidden_in,
        encoder_states,
        output_grad,
        piece_starts,
        selfquery,
        selfkey,
        selfvalue,
        selfproj,
        crossquery,
        crosskey,
        crossvalue,
        crossproj,
        gateproj,
        upproj,
        downproj,
        gainself,
        gaincross,
        gainffn,
        reltable,
    ):
        shard_rows, width = selfquery.shape
        ff_width = gateproj.shape[1]
        table_rows = reltable.shape[0]
        small_cols = jnp.concatenate(
            [
                gainself[:, None],
                gaincross[:, None],
                gainffn[:, None],
                jnp.pad(reltable, ((0, shard_rows - table_rows), (0, 0))),
                jnp.zeros((shard_rows, 128 - 3 - HEADS), selfquery.dtype),
            ],
            axis=1,
        )
        self_packed = jnp.concatenate([selfquery, selfkey, selfvalue, small_cols], axis=1)
        mid_packed = jnp.concatenate(
            [selfproj, crossquery, crosskey, crossvalue, crossproj], axis=1
        )
        ffn_packed = jnp.concatenate([gateproj, upproj], axis=1)
        self_full = lax.all_gather(self_packed, "fsdp", axis=0, tiled=True)
        mid_full = lax.all_gather(mid_packed, "fsdp", axis=0, tiled=True)
        ffn_full = lax.all_gather(ffn_packed, "fsdp", axis=0, tiled=True)

        small_full = self_full[:, 3 * width :]
        self_full = self_full[:, : 3 * width]
        gain_one = small_full[:, 0]
        gain_two = small_full[:, 1]
        gain_three = small_full[:, 2]
        table_full = (
            small_full[:, 3 : 3 + HEADS]
            .reshape(fsdp_size, shard_rows, HEADS)[:, :table_rows]
            .reshape(-1, HEADS)
        )
        self_proj = mid_full[:, 0:width]
        cross_query = mid_full[:, width : 2 * width]
        cross_kv = mid_full[:, 2 * width : 4 * width]
        cross_key = cross_kv[:, :width]
        cross_value = cross_kv[:, width:]
        cross_proj = mid_full[:, 4 * width : 5 * width]
        gate_up = ffn_full
        down_full = tree_gather(downproj, fsdp_size)

        length = hidden_in.shape[0]
        position = jnp.arange(length, dtype=jnp.int32)
        piece_ids = (
            jnp.sum((piece_starts[0][None, :] <= position[:, None]).astype(jnp.int32), axis=1) - 1
        )
        context = (table_full, piece_ids)
        resid_in = hidden_in.astype(jnp.float32)
        normed_one = rms_scale(resid_in, gain_one.astype(jnp.float32)).astype(jnp.bfloat16)
        qkv_one = product(normed_one, self_full).astype(jnp.bfloat16)
        query_one = qkv_one[:, :width]
        key_one = qkv_one[:, width : 2 * width]
        value_one = qkv_one[:, 2 * width :]
        mixed_one, lse_one = attend_forward(query_one, key_one, value_one, context)
        after_self = resid_in + product(mixed_one, self_proj)
        normed_two = rms_scale(after_self, gain_two.astype(jnp.float32)).astype(jnp.bfloat16)
        query_two = product(normed_two, cross_query).astype(jnp.bfloat16)
        kv_two = product(encoder_states, cross_kv).astype(jnp.bfloat16)
        key_two = kv_two[:, :width]
        value_two = kv_two[:, width:]
        mixed_two, lse_two = attend_forward(query_two, key_two, value_two, None)
        after_cross = after_self + product(mixed_two, cross_proj)
        normed_three = rms_scale(after_cross, gain_three.astype(jnp.float32)).astype(jnp.bfloat16)
        gate_upper = product(normed_three, gate_up)
        gate_pre = gate_upper[:, :ff_width]
        upper_pre = gate_upper[:, ff_width:]
        inner = gated(gate_pre, upper_pre).astype(jnp.bfloat16)
        layer_out = (after_cross + product(inner, down_full)).astype(jnp.bfloat16)

        def reduce_rows(packed):
            return lax.psum_scatter(
                packed.astype(jnp.bfloat16), ("fsdp", "replica"), scatter_dimension=0, tiled=True
            )

        downproj_grad = left_product(inner, output_grad)
        inner_grad = right_product(output_grad, down_full)
        gated_value, pull_gate = jax.vjp(gated, gate_pre, upper_pre)
        gate_grad, upper_grad = pull_gate(inner_grad)
        gate_upper_low = jnp.concatenate(
            [gate_grad.astype(jnp.bfloat16), upper_grad.astype(jnp.bfloat16)], axis=1
        )
        gate_up_grad = left_product(normed_three, gate_upper_low)
        ffn_packed = jnp.concatenate(
            [gate_up_grad, downproj_grad.reshape(width, ff_width)], axis=1
        ).astype(jnp.bfloat16)
        normed_grad = right_product(gate_upper_low, gate_up)
        norm_value, pull_norm = jax.vjp(rms_scale, after_cross, gain_three.astype(jnp.float32))
        back_resid, gainffn_grad = pull_norm(normed_grad)
        ffn_packed, back_resid = lax.optimization_barrier((ffn_packed, back_resid))
        ffn_part = reduce_rows(ffn_packed)
        resid_grad = output_grad.astype(jnp.float32) + back_resid
        branch_low = resid_grad.astype(jnp.bfloat16)
        crossproj_grad = left_product(mixed_two, branch_low)
        mixed_grad = right_product(branch_low, cross_proj).astype(jnp.bfloat16)
        query_back, key_back, value_back, unused_table = attend_backward(
            query_two, key_two, value_two, mixed_grad, lse_two, None
        )
        crossquery_grad = left_product(normed_two, query_back)
        kv_back = jnp.concatenate([key_back, value_back], axis=1)
        crosskv_grad = left_product(encoder_states, kv_back)
        encoder_grad = right_product(kv_back, cross_kv)
        normed_grad = right_product(query_back, cross_query)
        norm_value, pull_norm = jax.vjp(rms_scale, after_self, gain_two.astype(jnp.float32))
        back_resid, gaincross_grad = pull_norm(normed_grad)
        resid_grad = resid_grad + back_resid
        branch_low = resid_grad.astype(jnp.bfloat16)
        selfproj_grad = left_product(mixed_one, branch_low)
        mixed_grad = right_product(branch_low, self_proj).astype(jnp.bfloat16)
        query_back, key_back, value_back, reltable_grad = attend_backward(
            query_one, key_one, value_one, mixed_grad, lse_one, context
        )
        qkv_back = jnp.concatenate([query_back, key_back, value_back], axis=1)
        selfqkv_grad = left_product(normed_one, qkv_back)
        normed_grad = right_product(qkv_back, self_full)
        norm_value, pull_norm = jax.vjp(rms_scale, resid_in, gain_one.astype(jnp.float32))
        back_resid, gainself_grad = pull_norm(normed_grad)
        hidden_grad = resid_grad + back_resid

        table_block_rows = table_rows
        table_cols = jnp.pad(
            reltable_grad.reshape(fsdp_size, table_block_rows, HEADS),
            ((0, 0), (0, shard_rows - table_block_rows), (0, 0)),
        ).reshape(width, HEADS)
        extra = jnp.concatenate(
            [
                gainffn_grad[:, None],
                gaincross_grad[:, None],
                gainself_grad[:, None],
                table_cols,
                jnp.zeros((width, 128 - 3 - HEADS), jnp.float32),
            ],
            axis=1,
        )
        attn_parts = [
            [crossproj_grad, crossquery_grad],
            [crosskv_grad],
            [selfproj_grad, extra],
            [selfqkv_grad[:, : 2 * width]],
            [selfqkv_grad[:, 2 * width :]],
        ]
        attn_owned, ffn_part = tree_reduce(attn_parts, fsdp_size, replica_size, carry=ffn_part)
        ffn_owned = lax.all_gather(ffn_part, "replica", axis=0, tiled=True)
        cross_owned = attn_owned[:, : 4 * width]
        extra_owned = attn_owned[:, 5 * width : 5 * width + 128].astype(jnp.float32)
        self_owned = jnp.concatenate(
            [attn_owned[:, 4 * width : 5 * width], attn_owned[:, 5 * width + 128 :]], axis=1
        )

        as_f32 = lambda v: v.astype(jnp.float32)
        return (
            layer_out,
            hidden_grad,
            encoder_grad,
            as_f32(self_owned[:, width : 2 * width]),
            as_f32(self_owned[:, 2 * width : 3 * width]),
            as_f32(self_owned[:, 3 * width : 4 * width]),
            as_f32(self_owned[:, 0:width]),
            as_f32(cross_owned[:, width : 2 * width]),
            as_f32(cross_owned[:, 2 * width : 3 * width]),
            as_f32(cross_owned[:, 3 * width : 4 * width]),
            as_f32(cross_owned[:, 0:width]),
            as_f32(ffn_owned[:, 0:ff_width]),
            as_f32(ffn_owned[:, ff_width : 2 * ff_width]),
            as_f32(ffn_owned[:, 2 * ff_width :].reshape(-1, width)),
            extra_owned[:, 2],
            extra_owned[:, 1],
            extra_owned[:, 0],
            extra_owned[:table_block_rows, 3 : 3 + HEADS],
        )

    return on_device


def solution(mesh):
    placed = (
        P(("fsdp", "replica"), None),
        P(("fsdp", "replica"), None),
        P(("fsdp", "replica"), None),
        P(("fsdp", "replica"), None),
        P("fsdp", None),
        P("fsdp", None),
        P("fsdp", None),
        P("fsdp", None),
        P("fsdp", None),
        P("fsdp", None),
        P("fsdp", None),
        P("fsdp", None),
        P("fsdp", None),
        P("fsdp", None),
        P("fsdp", None),
        P("fsdp"),
        P("fsdp"),
        P("fsdp"),
        P("fsdp", None),
    )
    return jax.shard_map(
        make_on_device(mesh.shape["fsdp"], mesh.shape["replica"]),
        mesh=mesh,
        in_specs=placed,
        out_specs=(
            P(("fsdp", "replica"), None),
            P(("fsdp", "replica"), None),
            P(("fsdp", "replica"), None),
            P("fsdp", None),
            P("fsdp", None),
            P("fsdp", None),
            P("fsdp", None),
            P("fsdp", None),
            P("fsdp", None),
            P("fsdp", None),
            P("fsdp", None),
            P("fsdp", None),
            P("fsdp", None),
            P("fsdp", None),
            P("fsdp"),
            P("fsdp"),
            P("fsdp"),
            P("fsdp", None),
        ),
        check_vma=False,
    )
```

```python
import jax
import jax.numpy as jnp
from jax import lax
from jax.sharding import PartitionSpec as P

HEADS = 12
HEAD_DIM = 64
BUCKETS = 32
QBLOCK = 512


EPS = 1e-06
NEG = -1000000000.0
EDGES = (1, 2, 3, 4, 5, 6, 7, 8, 12, 16, 23, 32, 46, 64, 91)


def rms_scale(hidden, gain):
    return hidden * lax.rsqrt(jnp.mean(hidden * hidden, axis=-1, keepdims=True) + EPS) * gain


def gated(gate, upper):
    return jax.nn.gelu(gate, approximate=True) * upper


def product(left, right):
    return jnp.dot(left, right, preferred_element_type=jnp.float32)


def left_product(left, right):
    return lax.dot_general(
        left, right, (((0,), (0,)), ((), ())), preferred_element_type=jnp.float32
    )


def right_product(left, right):
    return lax.dot_general(
        left, right, (((1,), (1,)), ((), ())), preferred_element_type=jnp.float32
    )


def split_heads(matrix):
    return matrix.reshape(matrix.shape[0], HEADS, HEAD_DIM)


def block_terms(context, block_rows, key_count):
    if context is None:
        return (None, None, None)
    rel_table, piece_ids = context
    query_pos = jnp.arange(block_rows, dtype=jnp.int32)
    key_pos = jnp.arange(key_count, dtype=jnp.int32)
    relative = key_pos[None, :] - query_pos[:, None]
    distance = jnp.abs(relative)
    bucket = 16 * (relative > 0).astype(jnp.int32)
    for edge_len in EDGES:
        bucket = bucket + (distance >= edge_len).astype(jnp.int32)
    onehot = (
        bucket.T[None, :, :] == jnp.arange(BUCKETS, dtype=jnp.int32)[:, None, None]
    ).astype(jnp.bfloat16)
    bias_block = jnp.swapaxes(
        lax.dot_general(
            rel_table, onehot, (((0,), (0,)), ((), ())), preferred_element_type=jnp.float32
        ),
        1,
        2,
    )
    allowed = (key_pos[None, :] <= query_pos[:, None]) | (piece_ids[None, :] == piece_ids[:, None])
    return (onehot, bias_block, allowed)


def block_scores(query_block, key_heads, bias_block, allowed):
    scores = jnp.einsum("qhd,khd->hqk", query_block, key_heads, preferred_element_type=jnp.float32)
    if bias_block is not None:
        scores = jnp.where(allowed[None], scores + bias_block, NEG)
    return scores


def attend_forward(queries, key_rows, value_rows, context):
    key_heads = split_heads(key_rows)
    value_heads = split_heads(value_rows)
    query_block = split_heads(queries)
    onehot, bias_block, allowed = block_terms(context, QBLOCK, key_rows.shape[0])
    scores = block_scores(query_block, key_heads, bias_block, allowed)
    row_max = jnp.max(scores, axis=-1, keepdims=True)
    raised = jnp.exp(scores - row_max)
    row_sum = jnp.sum(raised, axis=-1, keepdims=True)
    prob_low = (raised / row_sum).astype(jnp.bfloat16)
    mixed_block = jnp.einsum(
        "hqk,khd->qhd", prob_low, value_heads, preferred_element_type=jnp.float32
    )
    mixed_parts = mixed_block.reshape(QBLOCK, HEADS * HEAD_DIM).astype(jnp.bfloat16)
    lse_parts = row_max + jnp.log(row_sum)
    return (mixed_parts, lse_parts)


def attend_backward(queries, key_rows, value_rows, grad_mixed, lse_rows, context):
    key_count = key_rows.shape[0]
    key_heads = split_heads(key_rows)
    value_heads = split_heads(value_rows)
    table_grad = jnp.zeros((BUCKETS, HEADS), jnp.float32)
    query_block = split_heads(queries)
    grad_block = split_heads(grad_mixed)
    onehot, bias_block, allowed = block_terms(context, QBLOCK, key_count)
    scores = block_scores(query_block, key_heads, bias_block, allowed)
    probs = jnp.exp(scores - lse_rows)
    prob_low = probs.astype(jnp.bfloat16)
    grad_probs = jnp.einsum(
        "qhd,khd->hqk", grad_block, value_heads, preferred_element_type=jnp.float32
    )
    inner_sum = jnp.sum(probs * grad_probs, axis=-1, keepdims=True)
    grad_scores = (probs * (grad_probs - inner_sum)).astype(jnp.bfloat16)
    query_grad = jnp.einsum(
        "hqk,khd->qhd", grad_scores, key_heads, preferred_element_type=jnp.float32
    )
    query_parts = query_grad.reshape(QBLOCK, HEADS * HEAD_DIM).astype(jnp.bfloat16)
    key_grad = jnp.einsum(
        "hqk,qhd->khd", grad_scores, query_block, preferred_element_type=jnp.float32
    )
    value_grad = jnp.einsum(
        "hqk,qhd->khd", prob_low, grad_block, preferred_element_type=jnp.float32
    )
    if onehot is not None:
        table_grad = lax.dot_general(
            onehot,
            grad_scores,
            (((1, 2), (2, 1)), ((), ())),
            preferred_element_type=jnp.float32,
        )
    key_low = key_grad.reshape(key_count, HEADS * HEAD_DIM).astype(jnp.bfloat16)
    value_low = value_grad.reshape(key_count, HEADS * HEAD_DIM).astype(jnp.bfloat16)
    return (query_parts, key_low, value_low, table_grad)


def pairs_of(size, bit):
    return [(i, i ^ bit) for i in range(size)]


def tree_gather(shard, fsdp_size):
    me_f = lax.axis_index("fsdp")
    cur = shard
    levels = fsdp_size.bit_length() - 1
    for k in range(levels):
        bit = 1 << (levels - 1 - k)
        mine = (me_f // bit) % 2
        recv = lax.ppermute(cur, "fsdp", pairs_of(fsdp_size, bit))
        cur = jnp.where(
            mine == 0, jnp.stack([cur, recv], axis=k), jnp.stack([recv, cur], axis=k)
        )
    return cur.reshape(-1, shard.shape[1])


def tree_reduce(parts, fsdp_size, replica_size, carry=None):
    me_f = lax.axis_index("fsdp")
    me_r = lax.axis_index("replica")
    fsdp_bits = [1 << b for b in range(fsdp_size.bit_length() - 1)]
    rep_bits = [1 << b for b in range(replica_size.bit_length() - 1)]

    def fsdp_step(cur, bit):
        mine = (me_f // bit) % 2
        cur = cur.reshape(cur.shape[0] // 2, 2, cur.shape[1], cur.shape[2])
        keep = lax.dynamic_index_in_dim(cur, mine, axis=1, keepdims=False)
        send = lax.dynamic_index_in_dim(cur, 1 - mine, axis=1, keepdims=False)
        recv = lax.ppermute(send.astype(jnp.bfloat16), "fsdp", pairs_of(fsdp_size, bit))
        return keep + recv.astype(jnp.float32)

    def replica_step(cur, bit):
        mine = (me_r // bit) % 2
        cur = cur.reshape(cur.shape[0], 2, cur.shape[1] // 2, cur.shape[2])
        keep = lax.dynamic_index_in_dim(cur, mine, axis=1, keepdims=False)
        send = lax.dynamic_index_in_dim(cur, 1 - mine, axis=1, keepdims=False)
        recv = lax.ppermute(send.astype(jnp.bfloat16), "replica", pairs_of(replica_size, bit))
        return keep + recv.astype(jnp.float32)

    def replica_back(cur, bit):
        mine = (me_r // bit) % 2
        recv = lax.ppermute(cur, "replica", pairs_of(replica_size, bit))
        low = jnp.where(mine == 0, cur, recv)
        high = jnp.where(mine == 0, recv, cur)
        return jnp.concatenate([low, high], axis=1)

    firsts = []
    for pieces in parts:
        packed = jnp.concatenate(pieces, axis=1) if len(pieces) > 1 else pieces[0]
        rows = packed.shape[0] // fsdp_size
        cur = packed.reshape(fsdp_size, rows, packed.shape[1])
        firsts.append(fsdp_step(cur, fsdp_bits[0]))
    if carry is not None:
        firsts, carry = lax.optimization_barrier((firsts, carry))
    outs = []
    for part, cur in enumerate(firsts):
        rows = cur.shape[1]
        steps = [("f", bit) for bit in fsdp_bits[1:]] + [("r", bit) for bit in rep_bits]
        shift = part % len(steps) if steps else 0
        steps = steps[shift:] + steps[:shift]
        for kind, bit in steps:
            cur = fsdp_step(cur, bit) if kind == "f" else replica_step(cur, bit)
        rep_order = [bit for kind, bit in steps if kind == "r"]
        cur = cur.astype(jnp.bfloat16)
        for bit in reversed(rep_order):
            cur = replica_back(cur, bit)
        outs.append(cur.reshape(rows, -1))
    return jnp.concatenate(outs, axis=1), carry


def make_on_device(fsdp_size, replica_size):
    def on_device(
        hidden_in,
        encoder_states,
        output_grad,
        piece_starts,
        selfquery,
        selfkey,
        selfvalue,
        selfproj,
        crossquery,
        crosskey,
        crossvalue,
        crossproj,
        gateproj,
        upproj,
        downproj,
        gainself,
        gaincross,
        gainffn,
        reltable,
    ):
        shard_rows, width = selfquery.shape
        ff_width = gateproj.shape[1]
        table_rows = reltable.shape[0]
        small_cols = jnp.concatenate(
            [
                gainself[:, None],
                gaincross[:, None],
                gainffn[:, None],
                jnp.pad(reltable, ((0, shard_rows - table_rows), (0, 0))),
                jnp.zeros((shard_rows, 128 - 3 - HEADS), selfquery.dtype),
            ],
            axis=1,
        )
        self_packed = jnp.concatenate([selfquery, selfkey, selfvalue, small_cols], axis=1)
        mid_packed = jnp.concatenate(
            [selfproj, crossquery, crosskey, crossvalue, crossproj], axis=1
        )
        ffn_packed = jnp.concatenate([gateproj, upproj], axis=1)
        self_full = lax.all_gather(self_packed, "fsdp", axis=0, tiled=True)
        mid_full = lax.all_gather(mid_packed, "fsdp", axis=0, tiled=True)
        ffn_full = lax.all_gather(ffn_packed, "fsdp", axis=0, tiled=True)

        small_full = self_full[:, 3 * width :]
        self_full = self_full[:, : 3 * width]
        gain_one = small_full[:, 0]
        gain_two = small_full[:, 1]
        gain_three = small_full[:, 2]
        table_full = (
            small_full[:, 3 : 3 + HEADS]
            .reshape(fsdp_size, shard_rows, HEADS)[:, :table_rows]
            .reshape(-1, HEADS)
        )
        self_proj = mid_full[:, 0:width]
        cross_query = mid_full[:, width : 2 * width]
        cross_kv = mid_full[:, 2 * width : 4 * width]
        cross_key = cross_kv[:, :width]
        cross_value = cross_kv[:, width:]
        cross_proj = mid_full[:, 4 * width : 5 * width]
        gate_up = ffn_full
        down_full = lax.all_gather(downproj, "fsdp", axis=0, tiled=True)

        length = hidden_in.shape[0]
        position = jnp.arange(length, dtype=jnp.int32)
        piece_ids = (
            jnp.sum((piece_starts[0][None, :] <= position[:, None]).astype(jnp.int32), axis=1) - 1
        )
        context = (table_full, piece_ids)
        resid_in = hidden_in.astype(jnp.float32)
        normed_one = rms_scale(resid_in, gain_one.astype(jnp.float32)).astype(jnp.bfloat16)
        qkv_one = product(normed_one, self_full).astype(jnp.bfloat16)
        query_one = qkv_one[:, :width]
        key_one = qkv_one[:, width : 2 * width]
        value_one = qkv_one[:, 2 * width :]
        mixed_one, lse_one = attend_forward(query_one, key_one, value_one, context)
        after_self = resid_in + product(mixed_one, self_proj)
        normed_two = rms_scale(after_self, gain_two.astype(jnp.float32)).astype(jnp.bfloat16)
        query_two = product(normed_two, cross_query).astype(jnp.bfloat16)
        kv_two = product(encoder_states, cross_kv).astype(jnp.bfloat16)
        key_two = kv_two[:, :width]
        value_two = kv_two[:, width:]
        mixed_two, lse_two = attend_forward(query_two, key_two, value_two, None)
        after_cross = after_self + product(mixed_two, cross_proj)
        normed_three = rms_scale(after_cross, gain_three.astype(jnp.float32)).astype(jnp.bfloat16)
        gate_upper = product(normed_three, gate_up)
        gate_pre = gate_upper[:, :ff_width]
        upper_pre = gate_upper[:, ff_width:]
        inner = gated(gate_pre, upper_pre).astype(jnp.bfloat16)
        layer_out = (after_cross + product(inner, down_full)).astype(jnp.bfloat16)

        def reduce_rows(packed):
            return lax.psum_scatter(
                packed.astype(jnp.bfloat16), ("fsdp", "replica"), scatter_dimension=0, tiled=True
            )

        downproj_grad = left_product(inner, output_grad)
        inner_grad = right_product(output_grad, down_full)
        gated_value, pull_gate = jax.vjp(gated, gate_pre, upper_pre)
        gate_grad, upper_grad = pull_gate(inner_grad)
        gate_upper_low = jnp.concatenate(
            [gate_grad.astype(jnp.bfloat16), upper_grad.astype(jnp.bfloat16)], axis=1
        )
        gate_up_grad = left_product(normed_three, gate_upper_low)
        ffn_packed = jnp.concatenate(
            [gate_up_grad, downproj_grad.reshape(width, ff_width)], axis=1
        ).astype(jnp.bfloat16)
        normed_grad = right_product(gate_upper_low, gate_up)
        norm_value, pull_norm = jax.vjp(rms_scale, after_cross, gain_three.astype(jnp.float32))
        back_resid, gainffn_grad = pull_norm(normed_grad)
        ffn_packed, back_resid = lax.optimization_barrier((ffn_packed, back_resid))
        ffn_part = reduce_rows(ffn_packed)
        resid_grad = output_grad.astype(jnp.float32) + back_resid
        branch_low = resid_grad.astype(jnp.bfloat16)
        crossproj_grad = left_product(mixed_two, branch_low)
        mixed_grad = right_product(branch_low, cross_proj).astype(jnp.bfloat16)
        query_back, key_back, value_back, unused_table = attend_backward(
            query_two, key_two, value_two, mixed_grad, lse_two, None
        )
        crossquery_grad = left_product(normed_two, query_back)
        kv_back = jnp.concatenate([key_back, value_back], axis=1)
        crosskv_grad = left_product(encoder_states, kv_back)
        encoder_grad = right_product(kv_back, cross_kv)
        normed_grad = right_product(query_back, cross_query)
        norm_value, pull_norm = jax.vjp(rms_scale, after_self, gain_two.astype(jnp.float32))
        back_resid, gaincross_grad = pull_norm(normed_grad)
        resid_grad = resid_grad + back_resid
        branch_low = resid_grad.astype(jnp.bfloat16)
        selfproj_grad = left_product(mixed_one, branch_low)
        mixed_grad = right_product(branch_low, self_proj).astype(jnp.bfloat16)
        query_back, key_back, value_back, reltable_grad = attend_backward(
            query_one, key_one, value_one, mixed_grad, lse_one, context
        )
        qkv_back = jnp.concatenate([query_back, key_back, value_back], axis=1)
        selfqkv_grad = left_product(normed_one, qkv_back)
        normed_grad = right_product(qkv_back, self_full)
        norm_value, pull_norm = jax.vjp(rms_scale, resid_in, gain_one.astype(jnp.float32))
        back_resid, gainself_grad = pull_norm(normed_grad)
        hidden_grad = resid_grad + back_resid

        table_block_rows = table_rows
        table_cols = jnp.pad(
            reltable_grad.reshape(fsdp_size, table_block_rows, HEADS),
            ((0, 0), (0, shard_rows - table_block_rows), (0, 0)),
        ).reshape(width, HEADS)
        extra = jnp.concatenate(
            [
                gainffn_grad[:, None],
                gaincross_grad[:, None],
                gainself_grad[:, None],
                table_cols,
                jnp.zeros((width, 128 - 3 - HEADS), jnp.float32),
            ],
            axis=1,
        )
        attn_parts = [
            [crossproj_grad, crossquery_grad],
            [crosskv_grad],
            [selfproj_grad, extra],
            [selfqkv_grad[:, : 2 * width]],
            [selfqkv_grad[:, 2 * width :]],
        ]
        attn_owned, ffn_part = tree_reduce(attn_parts, fsdp_size, replica_size, carry=ffn_part)
        ffn_owned = lax.all_gather(ffn_part, "replica", axis=0, tiled=True)
        cross_owned = attn_owned[:, : 4 * width]
        extra_owned = attn_owned[:, 5 * width : 5 * width + 128].astype(jnp.float32)
        self_owned = jnp.concatenate(
            [attn_owned[:, 4 * width : 5 * width], attn_owned[:, 5 * width + 128 :]], axis=1
        )

        as_f32 = lambda v: v.astype(jnp.float32)
        return (
            layer_out,
            hidden_grad,
            encoder_grad,
            as_f32(self_owned[:, width : 2 * width]),
            as_f32(self_owned[:, 2 * width : 3 * width]),
            as_f32(self_owned[:, 3 * width : 4 * width]),
            as_f32(self_owned[:, 0:width]),
            as_f32(cross_owned[:, width : 2 * width]),
            as_f32(cross_owned[:, 2 * width : 3 * width]),
            as_f32(cross_owned[:, 3 * width : 4 * width]),
            as_f32(cross_owned[:, 0:width]),
            as_f32(ffn_owned[:, 0:ff_width]),
            as_f32(ffn_owned[:, ff_width : 2 * ff_width]),
            as_f32(ffn_owned[:, 2 * ff_width :].reshape(-1, width)),
            extra_owned[:, 2],
            extra_owned[:, 1],
            extra_owned[:, 0],
            extra_owned[:table_block_rows, 3 : 3 + HEADS],
        )

    return on_device


def solution(mesh):
    placed = (
        P(("fsdp", "replica"), None),
        P(("fsdp", "replica"), None),
        P(("fsdp", "replica"), None),
        P(("fsdp", "replica"), None),
        P("fsdp", None),
        P("fsdp", None),
        P("fsdp", None),
        P("fsdp", None),
        P("fsdp", None),
        P("fsdp", None),
        P("fsdp", None),
        P("fsdp", None),
        P("fsdp", None),
        P("fsdp", None),
        P("fsdp", None),
        P("fsdp"),
        P("fsdp"),
        P("fsdp"),
        P("fsdp", None),
    )
    return jax.shard_map(
        make_on_device(mesh.shape["fsdp"], mesh.shape["replica"]),
        mesh=mesh,
        in_specs=placed,
        out_specs=(
            P(("fsdp", "replica"), None),
            P(("fsdp", "replica"), None),
            P(("fsdp", "replica"), None),
            P("fsdp", None),
            P("fsdp", None),
            P("fsdp", None),
            P("fsdp", None),
            P("fsdp", None),
            P("fsdp", None),
            P("fsdp", None),
            P("fsdp", None),
            P("fsdp", None),
            P("fsdp", None),
            P("fsdp", None),
            P("fsdp"),
            P("fsdp"),
            P("fsdp"),
            P("fsdp", None),
        ),
        check_vma=False,
    )
```

```python
import jax
import jax.numpy as jnp
from jax import lax
from jax.sharding import PartitionSpec as P

HEADS = 12
HEAD_DIM = 64
BUCKETS = 32
QBLOCK = 512


EPS = 1e-06
NEG = -1000000000.0
EDGES = (1, 2, 3, 4, 5, 6, 7, 8, 12, 16, 23, 32, 46, 64, 91)


def rms_scale(hidden, gain):
    return hidden * lax.rsqrt(jnp.mean(hidden * hidden, axis=-1, keepdims=True) + EPS) * gain


def gated(gate, upper):
    return jax.nn.gelu(gate, approximate=True) * upper


def product(left, right):
    return jnp.dot(left, right, preferred_element_type=jnp.float32)


def left_product(left, right):
    return lax.dot_general(
        left, right, (((0,), (0,)), ((), ())), preferred_element_type=jnp.float32
    )


def right_product(left, right):
    return lax.dot_general(
        left, right, (((1,), (1,)), ((), ())), preferred_element_type=jnp.float32
    )


def split_heads(matrix):
    return matrix.reshape(matrix.shape[0], HEADS, HEAD_DIM)


def block_terms(context, block_rows, key_count):
    if context is None:
        return (None, None, None)
    rel_table, piece_ids = context
    query_pos = jnp.arange(block_rows, dtype=jnp.int32)
    key_pos = jnp.arange(key_count, dtype=jnp.int32)
    relative = key_pos[None, :] - query_pos[:, None]
    distance = jnp.abs(relative)
    bucket = 16 * (relative > 0).astype(jnp.int32)
    for edge_len in EDGES:
        bucket = bucket + (distance >= edge_len).astype(jnp.int32)
    onehot = (
        bucket.T[None, :, :] == jnp.arange(BUCKETS, dtype=jnp.int32)[:, None, None]
    ).astype(jnp.bfloat16)
    bias_block = jnp.swapaxes(
        lax.dot_general(
            rel_table, onehot, (((0,), (0,)), ((), ())), preferred_element_type=jnp.float32
        ),
        1,
        2,
    )
    allowed = (key_pos[None, :] <= query_pos[:, None]) | (piece_ids[None, :] == piece_ids[:, None])
    return (onehot, bias_block, allowed)


def block_scores(query_block, key_heads, bias_block, allowed):
    scores = jnp.einsum("qhd,khd->hqk", query_block, key_heads, preferred_element_type=jnp.float32)
    if bias_block is not None:
        scores = jnp.where(allowed[None], scores + bias_block, NEG)
    return scores


def attend_forward(queries, key_rows, value_rows, context):
    key_heads = split_heads(key_rows)
    value_heads = split_heads(value_rows)
    query_block = split_heads(queries)
    onehot, bias_block, allowed = block_terms(context, QBLOCK, key_rows.shape[0])
    scores = block_scores(query_block, key_heads, bias_block, allowed)
    row_max = jnp.max(scores, axis=-1, keepdims=True)
    raised = jnp.exp(scores - row_max)
    row_sum = jnp.sum(raised, axis=-1, keepdims=True)
    prob_low = (raised / row_sum).astype(jnp.bfloat16)
    mixed_block = jnp.einsum(
        "hqk,khd->qhd", prob_low, value_heads, preferred_element_type=jnp.float32
    )
    mixed_parts = mixed_block.reshape(QBLOCK, HEADS * HEAD_DIM).astype(jnp.bfloat16)
    lse_parts = row_max + jnp.log(row_sum)
    return (mixed_parts, lse_parts)


def attend_backward(queries, key_rows, value_rows, grad_mixed, lse_rows, context):
    key_count = key_rows.shape[0]
    key_heads = split_heads(key_rows)
    value_heads = split_heads(value_rows)
    table_grad = jnp.zeros((BUCKETS, HEADS), jnp.float32)
    query_block = split_heads(queries)
    grad_block = split_heads(grad_mixed)
    onehot, bias_block, allowed = block_terms(context, QBLOCK, key_count)
    scores = block_scores(query_block, key_heads, bias_block, allowed)
    probs = jnp.exp(scores - lse_rows)
    prob_low = probs.astype(jnp.bfloat16)
    grad_probs = jnp.einsum(
        "qhd,khd->hqk", grad_block, value_heads, preferred_element_type=jnp.float32
    )
    inner_sum = jnp.sum(probs * grad_probs, axis=-1, keepdims=True)
    grad_scores = (probs * (grad_probs - inner_sum)).astype(jnp.bfloat16)
    query_grad = jnp.einsum(
        "hqk,khd->qhd", grad_scores, key_heads, preferred_element_type=jnp.float32
    )
    query_parts = query_grad.reshape(QBLOCK, HEADS * HEAD_DIM).astype(jnp.bfloat16)
    key_grad = jnp.einsum(
        "hqk,qhd->khd", grad_scores, query_block, preferred_element_type=jnp.float32
    )
    value_grad = jnp.einsum(
        "hqk,qhd->khd", prob_low, grad_block, preferred_element_type=jnp.float32
    )
    if onehot is not None:
        table_grad = lax.dot_general(
            onehot,
            grad_scores,
            (((1, 2), (2, 1)), ((), ())),
            preferred_element_type=jnp.float32,
        )
    key_low = key_grad.reshape(key_count, HEADS * HEAD_DIM).astype(jnp.bfloat16)
    value_low = value_grad.reshape(key_count, HEADS * HEAD_DIM).astype(jnp.bfloat16)
    return (query_parts, key_low, value_low, table_grad)


def pairs_of(size, bit):
    return [(i, i ^ bit) for i in range(size)]


def tree_gather(shard, fsdp_size):
    me_f = lax.axis_index("fsdp")
    cur = shard
    levels = fsdp_size.bit_length() - 1
    for k in range(levels):
        bit = 1 << (levels - 1 - k)
        mine = (me_f // bit) % 2
        recv = lax.ppermute(cur, "fsdp", pairs_of(fsdp_size, bit))
        cur = jnp.where(
            mine == 0, jnp.stack([cur, recv], axis=k), jnp.stack([recv, cur], axis=k)
        )
    return cur.reshape(-1, shard.shape[1])


def tree_reduce(parts, fsdp_size, replica_size, carry=None):
    me_f = lax.axis_index("fsdp")
    me_r = lax.axis_index("replica")
    fsdp_bits = [1 << b for b in range(fsdp_size.bit_length() - 1)]
    rep_bits = [1 << b for b in range(replica_size.bit_length() - 1)]

    def fsdp_step(cur, bit):
        mine = (me_f // bit) % 2
        cur = cur.reshape(cur.shape[0] // 2, 2, cur.shape[1], cur.shape[2])
        keep = lax.dynamic_index_in_dim(cur, mine, axis=1, keepdims=False)
        send = lax.dynamic_index_in_dim(cur, 1 - mine, axis=1, keepdims=False)
        recv = lax.ppermute(send.astype(jnp.bfloat16), "fsdp", pairs_of(fsdp_size, bit))
        return keep + recv.astype(jnp.float32)

    def replica_step(cur, bit):
        mine = (me_r // bit) % 2
        cur = cur.reshape(cur.shape[0], 2, cur.shape[1] // 2, cur.shape[2])
        keep = lax.dynamic_index_in_dim(cur, mine, axis=1, keepdims=False)
        send = lax.dynamic_index_in_dim(cur, 1 - mine, axis=1, keepdims=False)
        recv = lax.ppermute(send.astype(jnp.bfloat16), "replica", pairs_of(replica_size, bit))
        return keep + recv.astype(jnp.float32)

    def replica_back(cur, bit):
        mine = (me_r // bit) % 2
        recv = lax.ppermute(cur, "replica", pairs_of(replica_size, bit))
        low = jnp.where(mine == 0, cur, recv)
        high = jnp.where(mine == 0, recv, cur)
        return jnp.concatenate([low, high], axis=1)

    firsts = []
    for pieces in parts:
        packed = jnp.concatenate(pieces, axis=1) if len(pieces) > 1 else pieces[0]
        rows = packed.shape[0] // fsdp_size
        cur = packed.reshape(fsdp_size, rows, packed.shape[1])
        firsts.append(fsdp_step(cur, fsdp_bits[0]))
    if carry is not None:
        firsts, carry = lax.optimization_barrier((firsts, carry))
    outs = []
    for part, cur in enumerate(firsts):
        rows = cur.shape[1]
        steps = [("f", bit) for bit in fsdp_bits[1:]] + [("r", bit) for bit in rep_bits]
        shift = part % len(steps) if steps else 0
        steps = steps[shift:] + steps[:shift]
        for kind, bit in steps:
            cur = fsdp_step(cur, bit) if kind == "f" else replica_step(cur, bit)
        rep_order = [bit for kind, bit in steps if kind == "r"]
        cur = cur.astype(jnp.bfloat16)
        for bit in reversed(rep_order):
            cur = replica_back(cur, bit)
        outs.append(cur.reshape(rows, -1))
    return jnp.concatenate(outs, axis=1), carry


def make_on_device(fsdp_size, replica_size):
    def on_device(
        hidden_in,
        encoder_states,
        output_grad,
        piece_starts,
        selfquery,
        selfkey,
        selfvalue,
        selfproj,
        crossquery,
        crosskey,
        crossvalue,
        crossproj,
        gateproj,
        upproj,
        downproj,
        gainself,
        gaincross,
        gainffn,
        reltable,
    ):
        shard_rows, width = selfquery.shape
        ff_width = gateproj.shape[1]
        table_rows = reltable.shape[0]
        small_cols = jnp.concatenate(
            [
                gainself[:, None],
                gaincross[:, None],
                gainffn[:, None],
                jnp.pad(reltable, ((0, shard_rows - table_rows), (0, 0))),
                jnp.zeros((shard_rows, 128 - 3 - HEADS), selfquery.dtype),
            ],
            axis=1,
        )
        self_packed = jnp.concatenate([selfquery, selfkey, selfvalue, small_cols], axis=1)
        mid_packed = jnp.concatenate(
            [selfproj, crossquery, crosskey, crossvalue, crossproj], axis=1
        )
        ffn_packed = jnp.concatenate([gateproj, upproj], axis=1)
        self_full = lax.all_gather(self_packed, "fsdp", axis=0, tiled=True)
        mid_full = tree_gather(mid_packed, fsdp_size)
        ffn_full = lax.all_gather(ffn_packed, "fsdp", axis=0, tiled=True)

        small_full = self_full[:, 3 * width :]
        self_full = self_full[:, : 3 * width]
        gain_one = small_full[:, 0]
        gain_two = small_full[:, 1]
        gain_three = small_full[:, 2]
        table_full = (
            small_full[:, 3 : 3 + HEADS]
            .reshape(fsdp_size, shard_rows, HEADS)[:, :table_rows]
            .reshape(-1, HEADS)
        )
        self_proj = mid_full[:, 0:width]
        cross_query = mid_full[:, width : 2 * width]
        cross_kv = mid_full[:, 2 * width : 4 * width]
        cross_key = cross_kv[:, :width]
        cross_value = cross_kv[:, width:]
        cross_proj = mid_full[:, 4 * width : 5 * width]
        gate_up = ffn_full
        down_full = tree_gather(downproj, fsdp_size)

        length = hidden_in.shape[0]
        position = jnp.arange(length, dtype=jnp.int32)
        piece_ids = (
            jnp.sum((piece_starts[0][None, :] <= position[:, None]).astype(jnp.int32), axis=1) - 1
        )
        context = (table_full, piece_ids)
        resid_in = hidden_in.astype(jnp.float32)
        normed_one = rms_scale(resid_in, gain_one.astype(jnp.float32)).astype(jnp.bfloat16)
        qkv_one = product(normed_one, self_full).astype(jnp.bfloat16)
        query_one = qkv_one[:, :width]
        key_one = qkv_one[:, width : 2 * width]
        value_one = qkv_one[:, 2 * width :]
        mixed_one, lse_one = attend_forward(query_one, key_one, value_one, context)
        after_self = resid_in + product(mixed_one, self_proj)
        normed_two = rms_scale(after_self, gain_two.astype(jnp.float32)).astype(jnp.bfloat16)
        query_two = product(normed_two, cross_query).astype(jnp.bfloat16)
        kv_two = product(encoder_states, cross_kv).astype(jnp.bfloat16)
        key_two = kv_two[:, :width]
        value_two = kv_two[:, width:]
        mixed_two, lse_two = attend_forward(query_two, key_two, value_two, None)
        after_cross = after_self + product(mixed_two, cross_proj)
        normed_three = rms_scale(after_cross, gain_three.astype(jnp.float32)).astype(jnp.bfloat16)
        gate_upper = product(normed_three, gate_up)
        gate_pre = gate_upper[:, :ff_width]
        upper_pre = gate_upper[:, ff_width:]
        inner = gated(gate_pre, upper_pre).astype(jnp.bfloat16)
        layer_out = (after_cross + product(inner, down_full)).astype(jnp.bfloat16)

        def reduce_rows(packed):
            return lax.psum_scatter(
                packed.astype(jnp.bfloat16), ("fsdp", "replica"), scatter_dimension=0, tiled=True
            )

        downproj_grad = left_product(inner, output_grad)
        inner_grad = right_product(output_grad, down_full)
        gated_value, pull_gate = jax.vjp(gated, gate_pre, upper_pre)
        gate_grad, upper_grad = pull_gate(inner_grad)
        gate_upper_low = jnp.concatenate(
            [gate_grad.astype(jnp.bfloat16), upper_grad.astype(jnp.bfloat16)], axis=1
        )
        gate_up_grad = left_product(normed_three, gate_upper_low)
        ffn_packed = jnp.concatenate(
            [gate_up_grad, downproj_grad.reshape(width, ff_width)], axis=1
        ).astype(jnp.bfloat16)
        normed_grad = right_product(gate_upper_low, gate_up)
        norm_value, pull_norm = jax.vjp(rms_scale, after_cross, gain_three.astype(jnp.float32))
        back_resid, gainffn_grad = pull_norm(normed_grad)
        ffn_packed, back_resid = lax.optimization_barrier((ffn_packed, back_resid))
        ffn_part = reduce_rows(ffn_packed)
        resid_grad = output_grad.astype(jnp.float32) + back_resid
        branch_low = resid_grad.astype(jnp.bfloat16)
        crossproj_grad = left_product(mixed_two, branch_low)
        mixed_grad = right_product(branch_low, cross_proj).astype(jnp.bfloat16)
        query_back, key_back, value_back, unused_table = attend_backward(
            query_two, key_two, value_two, mixed_grad, lse_two, None
        )
        crossquery_grad = left_product(normed_two, query_back)
        kv_back = jnp.concatenate([key_back, value_back], axis=1)
        crosskv_grad = left_product(encoder_states, kv_back)
        encoder_grad = right_product(kv_back, cross_kv)
        normed_grad = right_product(query_back, cross_query)
        norm_value, pull_norm = jax.vjp(rms_scale, after_self, gain_two.astype(jnp.float32))
        back_resid, gaincross_grad = pull_norm(normed_grad)
        resid_grad = resid_grad + back_resid
        branch_low = resid_grad.astype(jnp.bfloat16)
        selfproj_grad = left_product(mixed_one, branch_low)
        mixed_grad = right_product(branch_low, self_proj).astype(jnp.bfloat16)
        query_back, key_back, value_back, reltable_grad = attend_backward(
            query_one, key_one, value_one, mixed_grad, lse_one, context
        )
        qkv_back = jnp.concatenate([query_back, key_back, value_back], axis=1)
        selfqkv_grad = left_product(normed_one, qkv_back)
        normed_grad = right_product(qkv_back, self_full)
        norm_value, pull_norm = jax.vjp(rms_scale, resid_in, gain_one.astype(jnp.float32))
        back_resid, gainself_grad = pull_norm(normed_grad)
        hidden_grad = resid_grad + back_resid

        table_block_rows = table_rows
        table_cols = jnp.pad(
            reltable_grad.reshape(fsdp_size, table_block_rows, HEADS),
            ((0, 0), (0, shard_rows - table_block_rows), (0, 0)),
        ).reshape(width, HEADS)
        extra = jnp.concatenate(
            [
                gainffn_grad[:, None],
                gaincross_grad[:, None],
                gainself_grad[:, None],
                table_cols,
                jnp.zeros((width, 128 - 3 - HEADS), jnp.float32),
            ],
            axis=1,
        )
        attn_parts = [
            [crossproj_grad, crossquery_grad],
            [crosskv_grad],
            [selfproj_grad, extra],
            [selfqkv_grad[:, : 2 * width]],
            [selfqkv_grad[:, 2 * width :]],
        ]
        attn_owned, ffn_part = tree_reduce(attn_parts, fsdp_size, replica_size, carry=ffn_part)
        ffn_owned = lax.all_gather(ffn_part, "replica", axis=0, tiled=True)
        cross_owned = attn_owned[:, : 4 * width]
        extra_owned = attn_owned[:, 5 * width : 5 * width + 128].astype(jnp.float32)
        self_owned = jnp.concatenate(
            [attn_owned[:, 4 * width : 5 * width], attn_owned[:, 5 * width + 128 :]], axis=1
        )

        as_f32 = lambda v: v.astype(jnp.float32)
        return (
            layer_out,
            hidden_grad,
            encoder_grad,
            as_f32(self_owned[:, width : 2 * width]),
            as_f32(self_owned[:, 2 * width : 3 * width]),
            as_f32(self_owned[:, 3 * width : 4 * width]),
            as_f32(self_owned[:, 0:width]),
            as_f32(cross_owned[:, width : 2 * width]),
            as_f32(cross_owned[:, 2 * width : 3 * width]),
            as_f32(cross_owned[:, 3 * width : 4 * width]),
            as_f32(cross_owned[:, 0:width]),
            as_f32(ffn_owned[:, 0:ff_width]),
            as_f32(ffn_owned[:, ff_width : 2 * ff_width]),
            as_f32(ffn_owned[:, 2 * ff_width :].reshape(-1, width)),
            extra_owned[:, 2],
            extra_owned[:, 1],
            extra_owned[:, 0],
            extra_owned[:table_block_rows, 3 : 3 + HEADS],
        )

    return on_device


def solution(mesh):
    placed = (
        P(("fsdp", "replica"), None),
        P(("fsdp", "replica"), None),
        P(("fsdp", "replica"), None),
        P(("fsdp", "replica"), None),
        P("fsdp", None),
        P("fsdp", None),
        P("fsdp", None),
        P("fsdp", None),
        P("fsdp", None),
        P("fsdp", None),
        P("fsdp", None),
        P("fsdp", None),
        P("fsdp", None),
        P("fsdp", None),
        P("fsdp", None),
        P("fsdp"),
        P("fsdp"),
        P("fsdp"),
        P("fsdp", None),
    )
    return jax.shard_map(
        make_on_device(mesh.shape["fsdp"], mesh.shape["replica"]),
        mesh=mesh,
        in_specs=placed,
        out_specs=(
            P(("fsdp", "replica"), None),
            P(("fsdp", "replica"), None),
            P(("fsdp", "replica"), None),
            P("fsdp", None),
            P("fsdp", None),
            P("fsdp", None),
            P("fsdp", None),
            P("fsdp", None),
            P("fsdp", None),
            P("fsdp", None),
            P("fsdp", None),
            P("fsdp", None),
            P("fsdp", None),
            P("fsdp", None),
            P("fsdp"),
            P("fsdp"),
            P("fsdp"),
            P("fsdp", None),
        ),
        check_vma=False,
    )
```

```python
import jax
import jax.numpy as jnp
from jax import lax
from jax.sharding import PartitionSpec as P

HEADS = 12
HEAD_DIM = 64
BUCKETS = 32
QBLOCK = 512


EPS = 1e-06
NEG = -1000000000.0
EDGES = (1, 2, 3, 4, 5, 6, 7, 8, 12, 16, 23, 32, 46, 64, 91)


def rms_scale(hidden, gain):
    return hidden * lax.rsqrt(jnp.mean(hidden * hidden, axis=-1, keepdims=True) + EPS) * gain


def gated(gate, upper):
    return jax.nn.gelu(gate, approximate=True) * upper


def product(left, right):
    return jnp.dot(left, right, preferred_element_type=jnp.float32)


def left_product(left, right):
    return lax.dot_general(
        left, right, (((0,), (0,)), ((), ())), preferred_element_type=jnp.float32
    )


def right_product(left, right):
    return lax.dot_general(
        left, right, (((1,), (1,)), ((), ())), preferred_element_type=jnp.float32
    )


def split_heads(matrix):
    return matrix.reshape(matrix.shape[0], HEADS, HEAD_DIM)


def block_terms(context, block_rows, key_count):
    if context is None:
        return (None, None, None)
    rel_table, piece_ids = context
    query_pos = jnp.arange(block_rows, dtype=jnp.int32)
    key_pos = jnp.arange(key_count, dtype=jnp.int32)
    relative = key_pos[None, :] - query_pos[:, None]
    distance = jnp.abs(relative)
    bucket = 16 * (relative > 0).astype(jnp.int32)
    for edge_len in EDGES:
        bucket = bucket + (distance >= edge_len).astype(jnp.int32)
    onehot = (
        bucket.T[None, :, :] == jnp.arange(BUCKETS, dtype=jnp.int32)[:, None, None]
    ).astype(jnp.bfloat16)
    bias_block = jnp.swapaxes(
        lax.dot_general(
            rel_table, onehot, (((0,), (0,)), ((), ())), preferred_element_type=jnp.float32
        ),
        1,
        2,
    )
    allowed = (key_pos[None, :] <= query_pos[:, None]) | (piece_ids[None, :] == piece_ids[:, None])
    return (onehot, bias_block, allowed)


def block_scores(query_block, key_heads, bias_block, allowed):
    scores = jnp.einsum("qhd,khd->hqk", query_block, key_heads, preferred_element_type=jnp.float32)
    if bias_block is not None:
        scores = jnp.where(allowed[None], scores + bias_block, NEG)
    return scores


def attend_forward(queries, key_rows, value_rows, context):
    key_heads = split_heads(key_rows)
    value_heads = split_heads(value_rows)
    query_block = split_heads(queries)
    onehot, bias_block, allowed = block_terms(context, QBLOCK, key_rows.shape[0])
    scores = block_scores(query_block, key_heads, bias_block, allowed)
    row_max = jnp.max(scores, axis=-1, keepdims=True)
    raised = jnp.exp(scores - row_max)
    row_sum = jnp.sum(raised, axis=-1, keepdims=True)
    prob_low = (raised / row_sum).astype(jnp.bfloat16)
    mixed_block = jnp.einsum(
        "hqk,khd->qhd", prob_low, value_heads, preferred_element_type=jnp.float32
    )
    mixed_parts = mixed_block.reshape(QBLOCK, HEADS * HEAD_DIM).astype(jnp.bfloat16)
    lse_parts = row_max + jnp.log(row_sum)
    return (mixed_parts, lse_parts)


def attend_backward(queries, key_rows, value_rows, grad_mixed, lse_rows, context):
    key_count = key_rows.shape[0]
    key_heads = split_heads(key_rows)
    value_heads = split_heads(value_rows)
    table_grad = jnp.zeros((BUCKETS, HEADS), jnp.float32)
    query_block = split_heads(queries)
    grad_block = split_heads(grad_mixed)
    onehot, bias_block, allowed = block_terms(context, QBLOCK, key_count)
    scores = block_scores(query_block, key_heads, bias_block, allowed)
    probs = jnp.exp(scores - lse_rows)
    prob_low = probs.astype(jnp.bfloat16)
    grad_probs = jnp.einsum(
        "qhd,khd->hqk", grad_block, value_heads, preferred_element_type=jnp.float32
    )
    inner_sum = jnp.sum(probs * grad_probs, axis=-1, keepdims=True)
    grad_scores = (probs * (grad_probs - inner_sum)).astype(jnp.bfloat16)
    query_grad = jnp.einsum(
        "hqk,khd->qhd", grad_scores, key_heads, preferred_element_type=jnp.float32
    )
    query_parts = query_grad.reshape(QBLOCK, HEADS * HEAD_DIM).astype(jnp.bfloat16)
    key_grad = jnp.einsum(
        "hqk,qhd->khd", grad_scores, query_block, preferred_element_type=jnp.float32
    )
    value_grad = jnp.einsum(
        "hqk,qhd->khd", prob_low, grad_block, preferred_element_type=jnp.float32
    )
    if onehot is not None:
        table_grad = lax.dot_general(
            onehot,
            grad_scores,
            (((1, 2), (2, 1)), ((), ())),
            preferred_element_type=jnp.float32,
        )
    key_low = key_grad.reshape(key_count, HEADS * HEAD_DIM).astype(jnp.bfloat16)
    value_low = value_grad.reshape(key_count, HEADS * HEAD_DIM).astype(jnp.bfloat16)
    return (query_parts, key_low, value_low, table_grad)


def pairs_of(size, bit):
    return [(i, i ^ bit) for i in range(size)]


def tree_gather(shard, fsdp_size):
    me_f = lax.axis_index("fsdp")
    cur = shard
    levels = fsdp_size.bit_length() - 1
    for k in range(levels):
        bit = 1 << (levels - 1 - k)
        mine = (me_f // bit) % 2
        recv = lax.ppermute(cur, "fsdp", pairs_of(fsdp_size, bit))
        cur = jnp.where(
            mine == 0, jnp.stack([cur, recv], axis=k), jnp.stack([recv, cur], axis=k)
        )
    return cur.reshape(-1, shard.shape[1])


def tree_reduce(parts, fsdp_size, replica_size, carry=None):
    me_f = lax.axis_index("fsdp")
    me_r = lax.axis_index("replica")
    fsdp_bits = [1 << b for b in range(fsdp_size.bit_length() - 1)]
    rep_bits = [1 << b for b in range(replica_size.bit_length() - 1)]

    def fsdp_step(cur, bit):
        mine = (me_f // bit) % 2
        cur = cur.reshape(cur.shape[0] // 2, 2, cur.shape[1], cur.shape[2])
        keep = lax.dynamic_index_in_dim(cur, mine, axis=1, keepdims=False)
        send = lax.dynamic_index_in_dim(cur, 1 - mine, axis=1, keepdims=False)
        recv = lax.ppermute(send.astype(jnp.bfloat16), "fsdp", pairs_of(fsdp_size, bit))
        return keep + recv.astype(jnp.float32)

    def replica_step(cur, bit):
        mine = (me_r // bit) % 2
        cur = cur.reshape(cur.shape[0], 2, cur.shape[1] // 2, cur.shape[2])
        keep = lax.dynamic_index_in_dim(cur, mine, axis=1, keepdims=False)
        send = lax.dynamic_index_in_dim(cur, 1 - mine, axis=1, keepdims=False)
        recv = lax.ppermute(send.astype(jnp.bfloat16), "replica", pairs_of(replica_size, bit))
        return keep + recv.astype(jnp.float32)

    def replica_back(cur, bit):
        mine = (me_r // bit) % 2
        recv = lax.ppermute(cur, "replica", pairs_of(replica_size, bit))
        low = jnp.where(mine == 0, cur, recv)
        high = jnp.where(mine == 0, recv, cur)
        return jnp.concatenate([low, high], axis=1)

    firsts = []
    for pieces in parts:
        packed = jnp.concatenate(pieces, axis=1) if len(pieces) > 1 else pieces[0]
        rows = packed.shape[0] // fsdp_size
        cur = packed.reshape(fsdp_size, rows, packed.shape[1])
        firsts.append(fsdp_step(cur, fsdp_bits[0]))
    if carry is not None:
        firsts, carry = lax.optimization_barrier((firsts, carry))
    outs = []
    for part, cur in enumerate(firsts):
        rows = cur.shape[1]
        steps = [("f", bit) for bit in fsdp_bits[1:]] + [("r", bit) for bit in rep_bits]
        shift = part % len(steps) if steps else 0
        steps = steps[shift:] + steps[:shift]
        for kind, bit in steps:
            cur = fsdp_step(cur, bit) if kind == "f" else replica_step(cur, bit)
        rep_order = [bit for kind, bit in steps if kind == "r"]
        cur = cur.astype(jnp.bfloat16)
        for bit in reversed(rep_order):
            cur = replica_back(cur, bit)
        outs.append(cur.reshape(rows, -1))
    return jnp.concatenate(outs, axis=1), carry


def make_on_device(fsdp_size, replica_size):
    def on_device(
        hidden_in,
        encoder_states,
        output_grad,
        piece_starts,
        selfquery,
        selfkey,
        selfvalue,
        selfproj,
        crossquery,
        crosskey,
        crossvalue,
        crossproj,
        gateproj,
        upproj,
        downproj,
        gainself,
        gaincross,
        gainffn,
        reltable,
    ):
        shard_rows, width = selfquery.shape
        ff_width = gateproj.shape[1]
        table_rows = reltable.shape[0]
        self_packed = jnp.concatenate([selfquery, selfkey, selfvalue], axis=1)
        small_packed = jnp.concatenate(
            [gainself, gaincross, gainffn, reltable.reshape(-1)]
        )
        mid_packed = jnp.concatenate(
            [selfproj, crossquery, crosskey, crossvalue, crossproj], axis=1
        )
        ffn_packed = jnp.concatenate([gateproj, upproj], axis=1)
        self_full = lax.all_gather(self_packed, "fsdp", axis=0, tiled=True)
        small_full = lax.all_gather(small_packed, "fsdp", axis=0, tiled=False)
        mid_full = lax.all_gather(mid_packed, "fsdp", axis=0, tiled=True)
        ffn_full = lax.all_gather(ffn_packed, "fsdp", axis=0, tiled=True)

        gain_one = small_full[:, 0:shard_rows].reshape(-1)
        gain_two = small_full[:, shard_rows : 2 * shard_rows].reshape(-1)
        gain_three = small_full[:, 2 * shard_rows : 3 * shard_rows].reshape(-1)
        table_full = small_full[:, 3 * shard_rows :].reshape(-1, HEADS)
        self_proj = mid_full[:, 0:width]
        cross_query = mid_full[:, width : 2 * width]
        cross_kv = mid_full[:, 2 * width : 4 * width]
        cross_key = cross_kv[:, :width]
        cross_value = cross_kv[:, width:]
        cross_proj = mid_full[:, 4 * width : 5 * width]
        gate_up = ffn_full
        down_full = tree_gather(downproj, fsdp_size)

        length = hidden_in.shape[0]
        position = jnp.arange(length, dtype=jnp.int32)
        piece_ids = (
            jnp.sum((piece_starts[0][None, :] <= position[:, None]).astype(jnp.int32), axis=1) - 1
        )
        context = (table_full, piece_ids)
        resid_in = hidden_in.astype(jnp.float32)
        normed_one = rms_scale(resid_in, gain_one.astype(jnp.float32)).astype(jnp.bfloat16)
        qkv_one = product(normed_one, self_full).astype(jnp.bfloat16)
        query_one = qkv_one[:, :width]
        key_one = qkv_one[:, width : 2 * width]
        value_one = qkv_one[:, 2 * width :]
        mixed_one, lse_one = attend_forward(query_one, key_one, value_one, context)
        after_self = resid_in + product(mixed_one, self_proj)
        normed_two = rms_scale(after_self, gain_two.astype(jnp.float32)).astype(jnp.bfloat16)
        query_two = product(normed_two, cross_query).astype(jnp.bfloat16)
        kv_two = product(encoder_states, cross_kv).astype(jnp.bfloat16)
        key_two = kv_two[:, :width]
        value_two = kv_two[:, width:]
        mixed_two, lse_two = attend_forward(query_two, key_two, value_two, None)
        after_cross = after_self + product(mixed_two, cross_proj)
        normed_three = rms_scale(after_cross, gain_three.astype(jnp.float32)).astype(jnp.bfloat16)
        gate_upper = product(normed_three, gate_up)
        gate_pre = gate_upper[:, :ff_width]
        upper_pre = gate_upper[:, ff_width:]
        inner = gated(gate_pre, upper_pre).astype(jnp.bfloat16)
        layer_out = (after_cross + product(inner, down_full)).astype(jnp.bfloat16)

        def reduce_rows(packed):
            return lax.psum_scatter(
                packed.astype(jnp.bfloat16), ("fsdp", "replica"), scatter_dimension=0, tiled=True
            )

        downproj_grad = left_product(inner, output_grad)
        inner_grad = right_product(output_grad, down_full)
        gated_value, pull_gate = jax.vjp(gated, gate_pre, upper_pre)
        gate_grad, upper_grad = pull_gate(inner_grad)
        gate_upper_low = jnp.concatenate(
            [gate_grad.astype(jnp.bfloat16), upper_grad.astype(jnp.bfloat16)], axis=1
        )
        gate_up_grad = left_product(normed_three, gate_upper_low)
        ffn_packed = jnp.concatenate(
            [gate_up_grad, downproj_grad.reshape(width, ff_width)], axis=1
        ).astype(jnp.bfloat16)
        normed_grad = right_product(gate_upper_low, gate_up)
        norm_value, pull_norm = jax.vjp(rms_scale, after_cross, gain_three.astype(jnp.float32))
        back_resid, gainffn_grad = pull_norm(normed_grad)
        ffn_packed, back_resid = lax.optimization_barrier((ffn_packed, back_resid))
        ffn_part = reduce_rows(ffn_packed)
        resid_grad = output_grad.astype(jnp.float32) + back_resid
        branch_low = resid_grad.astype(jnp.bfloat16)
        crossproj_grad = left_product(mixed_two, branch_low)
        mixed_grad = right_product(branch_low, cross_proj).astype(jnp.bfloat16)
        query_back, key_back, value_back, unused_table = attend_backward(
            query_two, key_two, value_two, mixed_grad, lse_two, None
        )
        crossquery_grad = left_product(normed_two, query_back)
        kv_back = jnp.concatenate([key_back, value_back], axis=1)
        crosskv_grad = left_product(encoder_states, kv_back)
        encoder_grad = right_product(kv_back, cross_kv)
        normed_grad = right_product(query_back, cross_query)
        norm_value, pull_norm = jax.vjp(rms_scale, after_self, gain_two.astype(jnp.float32))
        back_resid, gaincross_grad = pull_norm(normed_grad)
        resid_grad = resid_grad + back_resid
        branch_low = resid_grad.astype(jnp.bfloat16)
        selfproj_grad = left_product(mixed_one, branch_low)
        mixed_grad = right_product(branch_low, self_proj).astype(jnp.bfloat16)
        query_back, key_back, value_back, reltable_grad = attend_backward(
            query_one, key_one, value_one, mixed_grad, lse_one, context
        )
        qkv_back = jnp.concatenate([query_back, key_back, value_back], axis=1)
        selfqkv_grad = left_product(normed_one, qkv_back)
        normed_grad = right_product(qkv_back, self_full)
        norm_value, pull_norm = jax.vjp(rms_scale, resid_in, gain_one.astype(jnp.float32))
        back_resid, gainself_grad = pull_norm(normed_grad)
        hidden_grad = resid_grad + back_resid

        table_block_rows = table_rows
        table_cols = jnp.pad(
            reltable_grad.reshape(fsdp_size, table_block_rows, HEADS),
            ((0, 0), (0, shard_rows - table_block_rows), (0, 0)),
        ).reshape(width, HEADS)
        extra = jnp.concatenate(
            [
                gainffn_grad[:, None],
                gaincross_grad[:, None],
                gainself_grad[:, None],
                table_cols,
                jnp.zeros((width, 128 - 3 - HEADS), jnp.float32),
            ],
            axis=1,
        )
        attn_parts = [
            [crossproj_grad, crossquery_grad],
            [crosskv_grad[:, :width]],
            [crosskv_grad[:, width:]],
            [selfproj_grad, extra],
            [selfqkv_grad[:, : 2 * width]],
            [selfqkv_grad[:, 2 * width :]],
        ]
        attn_owned, ffn_part = tree_reduce(attn_parts, fsdp_size, replica_size, carry=ffn_part)
        ffn_owned = lax.all_gather(ffn_part, "replica", axis=0, tiled=True)
        cross_owned = attn_owned[:, : 4 * width]
        extra_owned = attn_owned[:, 5 * width : 5 * width + 128].astype(jnp.float32)
        self_owned = jnp.concatenate(
            [attn_owned[:, 4 * width : 5 * width], attn_owned[:, 5 * width + 128 :]], axis=1
        )

        as_f32 = lambda v: v.astype(jnp.float32)
        return (
            layer_out,
            hidden_grad,
            encoder_grad,
            as_f32(self_owned[:, width : 2 * width]),
            as_f32(self_owned[:, 2 * width : 3 * width]),
            as_f32(self_owned[:, 3 * width : 4 * width]),
            as_f32(self_owned[:, 0:width]),
            as_f32(cross_owned[:, width : 2 * width]),
            as_f32(cross_owned[:, 2 * width : 3 * width]),
            as_f32(cross_owned[:, 3 * width : 4 * width]),
            as_f32(cross_owned[:, 0:width]),
            as_f32(ffn_owned[:, 0:ff_width]),
            as_f32(ffn_owned[:, ff_width : 2 * ff_width]),
            as_f32(ffn_owned[:, 2 * ff_width :].reshape(-1, width)),
            extra_owned[:, 2],
            extra_owned[:, 1],
            extra_owned[:, 0],
            extra_owned[:table_block_rows, 3 : 3 + HEADS],
        )

    return on_device


def solution(mesh):
    placed = (
        P(("fsdp", "replica"), None),
        P(("fsdp", "replica"), None),
        P(("fsdp", "replica"), None),
        P(("fsdp", "replica"), None),
        P("fsdp", None),
        P("fsdp", None),
        P("fsdp", None),
        P("fsdp", None),
        P("fsdp", None),
        P("fsdp", None),
        P("fsdp", None),
        P("fsdp", None),
        P("fsdp", None),
        P("fsdp", None),
        P("fsdp", None),
        P("fsdp"),
        P("fsdp"),
        P("fsdp"),
        P("fsdp", None),
    )
    return jax.shard_map(
        make_on_device(mesh.shape["fsdp"], mesh.shape["replica"]),
        mesh=mesh,
        in_specs=placed,
        out_specs=(
            P(("fsdp", "replica"), None),
            P(("fsdp", "replica"), None),
            P(("fsdp", "replica"), None),
            P("fsdp", None),
            P("fsdp", None),
            P("fsdp", None),
            P("fsdp", None),
            P("fsdp", None),
            P("fsdp", None),
            P("fsdp", None),
            P("fsdp", None),
            P("fsdp", None),
            P("fsdp", None),
            P("fsdp", None),
            P("fsdp"),
            P("fsdp"),
            P("fsdp"),
            P("fsdp", None),
        ),
        check_vma=False,
    )
```

```python
import jax
import jax.numpy as jnp
from jax import lax
from jax.sharding import PartitionSpec as P

HEADS = 12
HEAD_DIM = 64
BUCKETS = 32
QBLOCK = 512


EPS = 1e-06
NEG = -1000000000.0
EDGES = (1, 2, 3, 4, 5, 6, 7, 8, 12, 16, 23, 32, 46, 64, 91)


def rms_scale(hidden, gain):
    return hidden * lax.rsqrt(jnp.mean(hidden * hidden, axis=-1, keepdims=True) + EPS) * gain


def gated(gate, upper):
    return jax.nn.gelu(gate, approximate=True) * upper


def product(left, right):
    return jnp.dot(left, right, preferred_element_type=jnp.float32)


def left_product(left, right):
    return lax.dot_general(
        left, right, (((0,), (0,)), ((), ())), preferred_element_type=jnp.float32
    )


def right_product(left, right):
    return lax.dot_general(
        left, right, (((1,), (1,)), ((), ())), preferred_element_type=jnp.float32
    )


def split_heads(matrix):
    return matrix.reshape(matrix.shape[0], HEADS, HEAD_DIM)


def block_terms(context, block_rows, key_count):
    if context is None:
        return (None, None, None)
    rel_table, piece_ids = context
    query_pos = jnp.arange(block_rows, dtype=jnp.int32)
    key_pos = jnp.arange(key_count, dtype=jnp.int32)
    relative = key_pos[None, :] - query_pos[:, None]
    distance = jnp.abs(relative)
    bucket = 16 * (relative > 0).astype(jnp.int32)
    for edge_len in EDGES:
        bucket = bucket + (distance >= edge_len).astype(jnp.int32)
    onehot = (
        bucket.T[None, :, :] == jnp.arange(BUCKETS, dtype=jnp.int32)[:, None, None]
    ).astype(jnp.bfloat16)
    bias_block = jnp.swapaxes(
        lax.dot_general(
            rel_table, onehot, (((0,), (0,)), ((), ())), preferred_element_type=jnp.float32
        ),
        1,
        2,
    )
    allowed = (key_pos[None, :] <= query_pos[:, None]) | (piece_ids[None, :] == piece_ids[:, None])
    return (onehot, bias_block, allowed)


def block_scores(query_block, key_heads, bias_block, allowed):
    scores = jnp.einsum("qhd,khd->hqk", query_block, key_heads, preferred_element_type=jnp.float32)
    if bias_block is not None:
        scores = jnp.where(allowed[None], scores + bias_block, NEG)
    return scores


def attend_forward(queries, key_rows, value_rows, context):
    key_heads = split_heads(key_rows)
    value_heads = split_heads(value_rows)
    query_block = split_heads(queries)
    onehot, bias_block, allowed = block_terms(context, QBLOCK, key_rows.shape[0])
    scores = block_scores(query_block, key_heads, bias_block, allowed)
    row_max = jnp.max(scores, axis=-1, keepdims=True)
    raised = jnp.exp(scores - row_max)
    row_sum = jnp.sum(raised, axis=-1, keepdims=True)
    prob_low = (raised / row_sum).astype(jnp.bfloat16)
    mixed_block = jnp.einsum(
        "hqk,khd->qhd", prob_low, value_heads, preferred_element_type=jnp.float32
    )
    mixed_parts = mixed_block.reshape(QBLOCK, HEADS * HEAD_DIM).astype(jnp.bfloat16)
    lse_parts = row_max + jnp.log(row_sum)
    return (mixed_parts, lse_parts)


def attend_backward(queries, key_rows, value_rows, grad_mixed, lse_rows, context):
    key_count = key_rows.shape[0]
    key_heads = split_heads(key_rows)
    value_heads = split_heads(value_rows)
    table_grad = jnp.zeros((BUCKETS, HEADS), jnp.float32)
    query_block = split_heads(queries)
    grad_block = split_heads(grad_mixed)
    onehot, bias_block, allowed = block_terms(context, QBLOCK, key_count)
    scores = block_scores(query_block, key_heads, bias_block, allowed)
    probs = jnp.exp(scores - lse_rows)
    prob_low = probs.astype(jnp.bfloat16)
    grad_probs = jnp.einsum(
        "qhd,khd->hqk", grad_block, value_heads, preferred_element_type=jnp.float32
    )
    inner_sum = jnp.sum(probs * grad_probs, axis=-1, keepdims=True)
    grad_scores = (probs * (grad_probs - inner_sum)).astype(jnp.bfloat16)
    query_grad = jnp.einsum(
        "hqk,khd->qhd", grad_scores, key_heads, preferred_element_type=jnp.float32
    )
    query_parts = query_grad.reshape(QBLOCK, HEADS * HEAD_DIM).astype(jnp.bfloat16)
    key_grad = jnp.einsum(
        "hqk,qhd->khd", grad_scores, query_block, preferred_element_type=jnp.float32
    )
    value_grad = jnp.einsum(
        "hqk,qhd->khd", prob_low, grad_block, preferred_element_type=jnp.float32
    )
    if onehot is not None:
        table_grad = lax.dot_general(
            onehot,
            grad_scores,
            (((1, 2), (2, 1)), ((), ())),
            preferred_element_type=jnp.float32,
        )
    key_low = key_grad.reshape(key_count, HEADS * HEAD_DIM).astype(jnp.bfloat16)
    value_low = value_grad.reshape(key_count, HEADS * HEAD_DIM).astype(jnp.bfloat16)
    return (query_parts, key_low, value_low, table_grad)


def pairs_of(size, bit):
    return [(i, i ^ bit) for i in range(size)]


def tree_gather(shard, fsdp_size):
    me_f = lax.axis_index("fsdp")
    cur = shard
    levels = fsdp_size.bit_length() - 1
    for k in range(levels):
        bit = 1 << (levels - 1 - k)
        mine = (me_f // bit) % 2
        recv = lax.ppermute(cur, "fsdp", pairs_of(fsdp_size, bit))
        cur = jnp.where(
            mine == 0, jnp.stack([cur, recv], axis=k), jnp.stack([recv, cur], axis=k)
        )
    return cur.reshape(-1, shard.shape[1])


def tree_first(pieces, fsdp_size):
    me_f = lax.axis_index("fsdp")
    packed = jnp.concatenate(pieces, axis=1) if len(pieces) > 1 else pieces[0]
    rows = packed.shape[0] // fsdp_size
    cur = packed.reshape(fsdp_size // 2, 2, rows, packed.shape[1])
    mine = me_f % 2
    keep = lax.dynamic_index_in_dim(cur, mine, axis=1, keepdims=False)
    send = lax.dynamic_index_in_dim(cur, 1 - mine, axis=1, keepdims=False)
    recv = lax.ppermute(send.astype(jnp.bfloat16), "fsdp", pairs_of(fsdp_size, 1))
    return keep + recv.astype(jnp.float32)


def tree_reduce(parts, fsdp_size, replica_size, carry=None):
    me_f = lax.axis_index("fsdp")
    me_r = lax.axis_index("replica")
    fsdp_bits = [1 << b for b in range(fsdp_size.bit_length() - 1)]
    rep_bits = [1 << b for b in range(replica_size.bit_length() - 1)]

    def fsdp_step(cur, bit):
        mine = (me_f // bit) % 2
        cur = cur.reshape(cur.shape[0] // 2, 2, cur.shape[1], cur.shape[2])
        keep = lax.dynamic_index_in_dim(cur, mine, axis=1, keepdims=False)
        send = lax.dynamic_index_in_dim(cur, 1 - mine, axis=1, keepdims=False)
        recv = lax.ppermute(send.astype(jnp.bfloat16), "fsdp", pairs_of(fsdp_size, bit))
        return keep + recv.astype(jnp.float32)

    def replica_step(cur, bit):
        mine = (me_r // bit) % 2
        cur = cur.reshape(cur.shape[0], 2, cur.shape[1] // 2, cur.shape[2])
        keep = lax.dynamic_index_in_dim(cur, mine, axis=1, keepdims=False)
        send = lax.dynamic_index_in_dim(cur, 1 - mine, axis=1, keepdims=False)
        recv = lax.ppermute(send.astype(jnp.bfloat16), "replica", pairs_of(replica_size, bit))
        return keep + recv.astype(jnp.float32)

    def replica_back(cur, bit):
        mine = (me_r // bit) % 2
        recv = lax.ppermute(cur, "replica", pairs_of(replica_size, bit))
        low = jnp.where(mine == 0, cur, recv)
        high = jnp.where(mine == 0, recv, cur)
        return jnp.concatenate([low, high], axis=1)

    firsts = []
    for pieces in parts:
        if isinstance(pieces, dict):
            firsts.append(pieces["first"])
            continue
        firsts.append(tree_first(pieces, fsdp_size))
    if carry is not None:
        firsts, carry = lax.optimization_barrier((firsts, carry))
    outs = []
    for part, cur in enumerate(firsts):
        rows = cur.shape[1]
        steps = [("f", bit) for bit in fsdp_bits[1:]] + [("r", bit) for bit in rep_bits]
        shift = part % len(steps) if steps else 0
        steps = steps[shift:] + steps[:shift]
        for kind, bit in steps:
            cur = fsdp_step(cur, bit) if kind == "f" else replica_step(cur, bit)
        rep_order = [bit for kind, bit in steps if kind == "r"]
        cur = cur.astype(jnp.bfloat16)
        for bit in reversed(rep_order):
            cur = replica_back(cur, bit)
        outs.append(cur.reshape(rows, -1))
    return jnp.concatenate(outs, axis=1), carry


def make_on_device(fsdp_size, replica_size):
    def on_device(
        hidden_in,
        encoder_states,
        output_grad,
        piece_starts,
        selfquery,
        selfkey,
        selfvalue,
        selfproj,
        crossquery,
        crosskey,
        crossvalue,
        crossproj,
        gateproj,
        upproj,
        downproj,
        gainself,
        gaincross,
        gainffn,
        reltable,
    ):
        shard_rows, width = selfquery.shape
        ff_width = gateproj.shape[1]
        table_rows = reltable.shape[0]
        self_packed = jnp.concatenate([selfquery, selfkey, selfvalue], axis=1)
        small_packed = jnp.concatenate(
            [gainself, gaincross, gainffn, reltable.reshape(-1)]
        )
        mid_packed = jnp.concatenate(
            [selfproj, crossquery, crosskey, crossvalue, crossproj], axis=1
        )
        ffn_packed = jnp.concatenate([gateproj, upproj], axis=1)
        self_full = lax.all_gather(self_packed, "fsdp", axis=0, tiled=True)
        small_full = lax.all_gather(small_packed, "fsdp", axis=0, tiled=False)
        mid_full = lax.all_gather(mid_packed, "fsdp", axis=0, tiled=True)
        ffn_full = lax.all_gather(ffn_packed, "fsdp", axis=0, tiled=True)

        gain_one = small_full[:, 0:shard_rows].reshape(-1)
        gain_two = small_full[:, shard_rows : 2 * shard_rows].reshape(-1)
        gain_three = small_full[:, 2 * shard_rows : 3 * shard_rows].reshape(-1)
        table_full = small_full[:, 3 * shard_rows :].reshape(-1, HEADS)
        self_proj = mid_full[:, 0:width]
        cross_query = mid_full[:, width : 2 * width]
        cross_kv = mid_full[:, 2 * width : 4 * width]
        cross_key = cross_kv[:, :width]
        cross_value = cross_kv[:, width:]
        cross_proj = mid_full[:, 4 * width : 5 * width]
        gate_up = ffn_full
        down_full = tree_gather(downproj, fsdp_size)

        length = hidden_in.shape[0]
        position = jnp.arange(length, dtype=jnp.int32)
        piece_ids = (
            jnp.sum((piece_starts[0][None, :] <= position[:, None]).astype(jnp.int32), axis=1) - 1
        )
        context = (table_full, piece_ids)
        resid_in = hidden_in.astype(jnp.float32)
        normed_one = rms_scale(resid_in, gain_one.astype(jnp.float32)).astype(jnp.bfloat16)
        qkv_one = product(normed_one, self_full).astype(jnp.bfloat16)
        query_one = qkv_one[:, :width]
        key_one = qkv_one[:, width : 2 * width]
        value_one = qkv_one[:, 2 * width :]
        mixed_one, lse_one = attend_forward(query_one, key_one, value_one, context)
        after_self = resid_in + product(mixed_one, self_proj)
        normed_two = rms_scale(after_self, gain_two.astype(jnp.float32)).astype(jnp.bfloat16)
        query_two = product(normed_two, cross_query).astype(jnp.bfloat16)
        kv_two = product(encoder_states, cross_kv).astype(jnp.bfloat16)
        key_two = kv_two[:, :width]
        value_two = kv_two[:, width:]
        mixed_two, lse_two = attend_forward(query_two, key_two, value_two, None)
        after_cross = after_self + product(mixed_two, cross_proj)
        normed_three = rms_scale(after_cross, gain_three.astype(jnp.float32)).astype(jnp.bfloat16)
        gate_upper = product(normed_three, gate_up)
        gate_pre = gate_upper[:, :ff_width]
        upper_pre = gate_upper[:, ff_width:]
        inner = gated(gate_pre, upper_pre).astype(jnp.bfloat16)
        layer_out = (after_cross + product(inner, down_full)).astype(jnp.bfloat16)

        def reduce_rows(packed):
            return lax.psum_scatter(
                packed.astype(jnp.bfloat16), ("fsdp", "replica"), scatter_dimension=0, tiled=True
            )

        downproj_grad = left_product(inner, output_grad)
        inner_grad = right_product(output_grad, down_full)
        gated_value, pull_gate = jax.vjp(gated, gate_pre, upper_pre)
        gate_grad, upper_grad = pull_gate(inner_grad)
        gate_upper_low = jnp.concatenate(
            [gate_grad.astype(jnp.bfloat16), upper_grad.astype(jnp.bfloat16)], axis=1
        )
        gate_up_grad = left_product(normed_three, gate_upper_low)
        ffn_packed = jnp.concatenate(
            [gate_up_grad, downproj_grad.reshape(width, ff_width)], axis=1
        ).astype(jnp.bfloat16)
        normed_grad = right_product(gate_upper_low, gate_up)
        norm_value, pull_norm = jax.vjp(rms_scale, after_cross, gain_three.astype(jnp.float32))
        back_resid, gainffn_grad = pull_norm(normed_grad)
        ffn_packed, back_resid = lax.optimization_barrier((ffn_packed, back_resid))
        ffn_part = reduce_rows(ffn_packed)
        resid_grad = output_grad.astype(jnp.float32) + back_resid
        branch_low = resid_grad.astype(jnp.bfloat16)
        crossproj_grad = left_product(mixed_two, branch_low)
        mixed_grad = right_product(branch_low, cross_proj).astype(jnp.bfloat16)
        query_back, key_back, value_back, unused_table = attend_backward(
            query_two, key_two, value_two, mixed_grad, lse_two, None
        )
        crossquery_grad = left_product(normed_two, query_back)
        kv_back = jnp.concatenate([key_back, value_back], axis=1)
        crosskv_grad = left_product(encoder_states, kv_back)
        encoder_grad = right_product(kv_back, cross_kv)
        normed_grad = right_product(query_back, cross_query)
        norm_value, pull_norm = jax.vjp(rms_scale, after_self, gain_two.astype(jnp.float32))
        back_resid, gaincross_grad = pull_norm(normed_grad)
        resid_grad = resid_grad + back_resid
        cross_firsts = [
            {"first": tree_first(pieces, fsdp_size)}
            for pieces in (
                [crossproj_grad, crossquery_grad],
                [crosskv_grad[:, :width]],
                [crosskv_grad[:, width:]],
            )
        ]
        cross_firsts, resid_grad = lax.optimization_barrier((cross_firsts, resid_grad))
        branch_low = resid_grad.astype(jnp.bfloat16)
        selfproj_grad = left_product(mixed_one, branch_low)
        mixed_grad = right_product(branch_low, self_proj).astype(jnp.bfloat16)
        query_back, key_back, value_back, reltable_grad = attend_backward(
            query_one, key_one, value_one, mixed_grad, lse_one, context
        )
        qkv_back = jnp.concatenate([query_back, key_back, value_back], axis=1)
        selfqkv_grad = left_product(normed_one, qkv_back)
        normed_grad = right_product(qkv_back, self_full)
        norm_value, pull_norm = jax.vjp(rms_scale, resid_in, gain_one.astype(jnp.float32))
        back_resid, gainself_grad = pull_norm(normed_grad)
        hidden_grad = resid_grad + back_resid

        table_block_rows = table_rows
        table_cols = jnp.pad(
            reltable_grad.reshape(fsdp_size, table_block_rows, HEADS),
            ((0, 0), (0, shard_rows - table_block_rows), (0, 0)),
        ).reshape(width, HEADS)
        extra = jnp.concatenate(
            [
                gainffn_grad[:, None],
                gaincross_grad[:, None],
                gainself_grad[:, None],
                table_cols,
                jnp.zeros((width, 128 - 3 - HEADS), jnp.float32),
            ],
            axis=1,
        )
        attn_parts = [
            *cross_firsts,
            [selfproj_grad, extra],
            [selfqkv_grad[:, : 2 * width]],
            [selfqkv_grad[:, 2 * width :]],
        ]
        attn_owned, ffn_part = tree_reduce(attn_parts, fsdp_size, replica_size, carry=ffn_part)
        ffn_owned = lax.all_gather(ffn_part, "replica", axis=0, tiled=True)
        cross_owned = attn_owned[:, : 4 * width]
        extra_owned = attn_owned[:, 5 * width : 5 * width + 128].astype(jnp.float32)
        self_owned = jnp.concatenate(
            [attn_owned[:, 4 * width : 5 * width], attn_owned[:, 5 * width + 128 :]], axis=1
        )

        as_f32 = lambda v: v.astype(jnp.float32)
        return (
            layer_out,
            hidden_grad,
            encoder_grad,
            as_f32(self_owned[:, width : 2 * width]),
            as_f32(self_owned[:, 2 * width : 3 * width]),
            as_f32(self_owned[:, 3 * width : 4 * width]),
            as_f32(self_owned[:, 0:width]),
            as_f32(cross_owned[:, width : 2 * width]),
            as_f32(cross_owned[:, 2 * width : 3 * width]),
            as_f32(cross_owned[:, 3 * width : 4 * width]),
            as_f32(cross_owned[:, 0:width]),
            as_f32(ffn_owned[:, 0:ff_width]),
            as_f32(ffn_owned[:, ff_width : 2 * ff_width]),
            as_f32(ffn_owned[:, 2 * ff_width :].reshape(-1, width)),
            extra_owned[:, 2],
            extra_owned[:, 1],
            extra_owned[:, 0],
            extra_owned[:table_block_rows, 3 : 3 + HEADS],
        )

    return on_device


def solution(mesh):
    placed = (
        P(("fsdp", "replica"), None),
        P(("fsdp", "replica"), None),
        P(("fsdp", "replica"), None),
        P(("fsdp", "replica"), None),
        P("fsdp", None),
        P("fsdp", None),
        P("fsdp", None),
        P("fsdp", None),
        P("fsdp", None),
        P("fsdp", None),
        P("fsdp", None),
        P("fsdp", None),
        P("fsdp", None),
        P("fsdp", None),
        P("fsdp", None),
        P("fsdp"),
        P("fsdp"),
        P("fsdp"),
        P("fsdp", None),
    )
    return jax.shard_map(
        make_on_device(mesh.shape["fsdp"], mesh.shape["replica"]),
        mesh=mesh,
        in_specs=placed,
        out_specs=(
            P(("fsdp", "replica"), None),
            P(("fsdp", "replica"), None),
            P(("fsdp", "replica"), None),
            P("fsdp", None),
            P("fsdp", None),
            P("fsdp", None),
            P("fsdp", None),
            P("fsdp", None),
            P("fsdp", None),
            P("fsdp", None),
            P("fsdp", None),
            P("fsdp", None),
            P("fsdp", None),
            P("fsdp", None),
            P("fsdp"),
            P("fsdp"),
            P("fsdp"),
            P("fsdp", None),
        ),
        check_vma=False,
    )
```

```python
import jax
import jax.numpy as jnp
from jax import lax
from jax.sharding import PartitionSpec as P

HEADS = 12
HEAD_DIM = 64
BUCKETS = 32
QBLOCK = 512


EPS = 1e-06
NEG = -1000000000.0
EDGES = (1, 2, 3, 4, 5, 6, 7, 8, 12, 16, 23, 32, 46, 64, 91)


def rms_scale(hidden, gain):
    return hidden * lax.rsqrt(jnp.mean(hidden * hidden, axis=-1, keepdims=True) + EPS) * gain


def gated(gate, upper):
    return jax.nn.gelu(gate, approximate=True) * upper


def product(left, right):
    return jnp.dot(left, right, preferred_element_type=jnp.float32)


def left_product(left, right):
    return lax.dot_general(
        left, right, (((0,), (0,)), ((), ())), preferred_element_type=jnp.float32
    )


def right_product(left, right):
    return lax.dot_general(
        left, right, (((1,), (1,)), ((), ())), preferred_element_type=jnp.float32
    )


def split_heads(matrix):
    return matrix.reshape(matrix.shape[0], HEADS, HEAD_DIM)


def block_terms(context, block_rows, key_count):
    if context is None:
        return (None, None, None)
    rel_table, piece_ids = context
    query_pos = jnp.arange(block_rows, dtype=jnp.int32)
    key_pos = jnp.arange(key_count, dtype=jnp.int32)
    relative = key_pos[None, :] - query_pos[:, None]
    distance = jnp.abs(relative)
    bucket = 16 * (relative > 0).astype(jnp.int32)
    for edge_len in EDGES:
        bucket = bucket + (distance >= edge_len).astype(jnp.int32)
    onehot = (
        bucket.T[None, :, :] == jnp.arange(BUCKETS, dtype=jnp.int32)[:, None, None]
    ).astype(jnp.bfloat16)
    bias_block = jnp.swapaxes(
        lax.dot_general(
            rel_table, onehot, (((0,), (0,)), ((), ())), preferred_element_type=jnp.float32
        ),
        1,
        2,
    )
    allowed = (key_pos[None, :] <= query_pos[:, None]) | (piece_ids[None, :] == piece_ids[:, None])
    return (onehot, bias_block, allowed)


def block_scores(query_block, key_heads, bias_block, allowed):
    scores = jnp.einsum("qhd,khd->hqk", query_block, key_heads, preferred_element_type=jnp.float32)
    if bias_block is not None:
        scores = jnp.where(allowed[None], scores + bias_block, NEG)
    return scores


def attend_forward(queries, key_rows, value_rows, context):
    key_heads = split_heads(key_rows)
    value_heads = split_heads(value_rows)
    query_block = split_heads(queries)
    onehot, bias_block, allowed = block_terms(context, QBLOCK, key_rows.shape[0])
    scores = block_scores(query_block, key_heads, bias_block, allowed)
    row_max = jnp.max(scores, axis=-1, keepdims=True)
    raised = jnp.exp(scores - row_max)
    row_sum = jnp.sum(raised, axis=-1, keepdims=True)
    prob_low = (raised / row_sum).astype(jnp.bfloat16)
    mixed_block = jnp.einsum(
        "hqk,khd->qhd", prob_low, value_heads, preferred_element_type=jnp.float32
    )
    mixed_parts = mixed_block.reshape(QBLOCK, HEADS * HEAD_DIM).astype(jnp.bfloat16)
    lse_parts = row_max + jnp.log(row_sum)
    return (mixed_parts, lse_parts)


def attend_backward(queries, key_rows, value_rows, grad_mixed, lse_rows, context):
    key_count = key_rows.shape[0]
    key_heads = split_heads(key_rows)
    value_heads = split_heads(value_rows)
    table_grad = jnp.zeros((BUCKETS, HEADS), jnp.float32)
    query_block = split_heads(queries)
    grad_block = split_heads(grad_mixed)
    onehot, bias_block, allowed = block_terms(context, QBLOCK, key_count)
    scores = block_scores(query_block, key_heads, bias_block, allowed)
    probs = jnp.exp(scores - lse_rows)
    prob_low = probs.astype(jnp.bfloat16)
    grad_probs = jnp.einsum(
        "qhd,khd->hqk", grad_block, value_heads, preferred_element_type=jnp.float32
    )
    inner_sum = jnp.sum(probs * grad_probs, axis=-1, keepdims=True)
    grad_scores = (probs * (grad_probs - inner_sum)).astype(jnp.bfloat16)
    query_grad = jnp.einsum(
        "hqk,khd->qhd", grad_scores, key_heads, preferred_element_type=jnp.float32
    )
    query_parts = query_grad.reshape(QBLOCK, HEADS * HEAD_DIM).astype(jnp.bfloat16)
    key_grad = jnp.einsum(
        "hqk,qhd->khd", grad_scores, query_block, preferred_element_type=jnp.float32
    )
    value_grad = jnp.einsum(
        "hqk,qhd->khd", prob_low, grad_block, preferred_element_type=jnp.float32
    )
    if onehot is not None:
        table_grad = lax.dot_general(
            onehot,
            grad_scores,
            (((1, 2), (2, 1)), ((), ())),
            preferred_element_type=jnp.float32,
        )
    key_low = key_grad.reshape(key_count, HEADS * HEAD_DIM).astype(jnp.bfloat16)
    value_low = value_grad.reshape(key_count, HEADS * HEAD_DIM).astype(jnp.bfloat16)
    return (query_parts, key_low, value_low, table_grad)


def pairs_of(size, bit):
    return [(i, i ^ bit) for i in range(size)]


def tree_gather(shard, fsdp_size):
    me_f = lax.axis_index("fsdp")
    cur = shard
    levels = fsdp_size.bit_length() - 1
    for k in range(levels):
        bit = 1 << (levels - 1 - k)
        mine = (me_f // bit) % 2
        recv = lax.ppermute(cur, "fsdp", pairs_of(fsdp_size, bit))
        cur = jnp.where(
            mine == 0, jnp.stack([cur, recv], axis=k), jnp.stack([recv, cur], axis=k)
        )
    return cur.reshape(-1, shard.shape[1])


def tree_reduce(parts, fsdp_size, replica_size, carry=None, shifts=None):
    me_f = lax.axis_index("fsdp")
    me_r = lax.axis_index("replica")
    fsdp_bits = [1 << b for b in range(fsdp_size.bit_length() - 1)]
    rep_bits = [1 << b for b in range(replica_size.bit_length() - 1)]

    def fsdp_step(cur, bit):
        mine = (me_f // bit) % 2
        cur = cur.reshape(cur.shape[0] // 2, 2, cur.shape[1], cur.shape[2])
        keep = lax.dynamic_index_in_dim(cur, mine, axis=1, keepdims=False)
        send = lax.dynamic_index_in_dim(cur, 1 - mine, axis=1, keepdims=False)
        recv = lax.ppermute(send.astype(jnp.bfloat16), "fsdp", pairs_of(fsdp_size, bit))
        return keep + recv.astype(jnp.float32)

    def replica_step(cur, bit):
        mine = (me_r // bit) % 2
        cur = cur.reshape(cur.shape[0], 2, cur.shape[1] // 2, cur.shape[2])
        keep = lax.dynamic_index_in_dim(cur, mine, axis=1, keepdims=False)
        send = lax.dynamic_index_in_dim(cur, 1 - mine, axis=1, keepdims=False)
        recv = lax.ppermute(send.astype(jnp.bfloat16), "replica", pairs_of(replica_size, bit))
        return keep + recv.astype(jnp.float32)

    def replica_back(cur, bit):
        mine = (me_r // bit) % 2
        recv = lax.ppermute(cur, "replica", pairs_of(replica_size, bit))
        low = jnp.where(mine == 0, cur, recv)
        high = jnp.where(mine == 0, recv, cur)
        return jnp.concatenate([low, high], axis=1)

    firsts = []
    for pieces in parts:
        packed = jnp.concatenate(pieces, axis=1) if len(pieces) > 1 else pieces[0]
        rows = packed.shape[0] // fsdp_size
        cur = packed.reshape(fsdp_size, rows, packed.shape[1])
        firsts.append(fsdp_step(cur, fsdp_bits[0]))
    if carry is not None:
        firsts, carry = lax.optimization_barrier((firsts, carry))
    outs = []
    for part, cur in enumerate(firsts):
        rows = cur.shape[1]
        steps = [("f", bit) for bit in fsdp_bits[1:]] + [("r", bit) for bit in rep_bits]
        shift = (shifts[part] if shifts else part) % len(steps) if steps else 0
        steps = steps[shift:] + steps[:shift]
        for kind, bit in steps:
            cur = fsdp_step(cur, bit) if kind == "f" else replica_step(cur, bit)
        rep_order = [bit for kind, bit in steps if kind == "r"]
        cur = cur.astype(jnp.bfloat16)
        for bit in reversed(rep_order):
            cur = replica_back(cur, bit)
        outs.append(cur.reshape(rows, -1))
    return jnp.concatenate(outs, axis=1), carry


def make_on_device(fsdp_size, replica_size):
    def on_device(
        hidden_in,
        encoder_states,
        output_grad,
        piece_starts,
        selfquery,
        selfkey,
        selfvalue,
        selfproj,
        crossquery,
        crosskey,
        crossvalue,
        crossproj,
        gateproj,
        upproj,
        downproj,
        gainself,
        gaincross,
        gainffn,
        reltable,
    ):
        shard_rows, width = selfquery.shape
        ff_width = gateproj.shape[1]
        table_rows = reltable.shape[0]
        self_packed = jnp.concatenate([selfquery, selfkey, selfvalue], axis=1)
        small_packed = jnp.concatenate(
            [gainself, gaincross, gainffn, reltable.reshape(-1)]
        )
        mid_packed = jnp.concatenate(
            [selfproj, crossquery, crosskey, crossvalue, crossproj], axis=1
        )
        ffn_packed = jnp.concatenate([gateproj, upproj], axis=1)
        self_full = lax.all_gather(self_packed, "fsdp", axis=0, tiled=True)
        small_full = lax.all_gather(small_packed, "fsdp", axis=0, tiled=False)
        mid_full = lax.all_gather(mid_packed, "fsdp", axis=0, tiled=True)
        ffn_full = lax.all_gather(ffn_packed, "fsdp", axis=0, tiled=True)

        gain_one = small_full[:, 0:shard_rows].reshape(-1)
        gain_two = small_full[:, shard_rows : 2 * shard_rows].reshape(-1)
        gain_three = small_full[:, 2 * shard_rows : 3 * shard_rows].reshape(-1)
        table_full = small_full[:, 3 * shard_rows :].reshape(-1, HEADS)
        self_proj = mid_full[:, 0:width]
        cross_query = mid_full[:, width : 2 * width]
        cross_kv = mid_full[:, 2 * width : 4 * width]
        cross_key = cross_kv[:, :width]
        cross_value = cross_kv[:, width:]
        cross_proj = mid_full[:, 4 * width : 5 * width]
        gate_up = ffn_full
        down_full = tree_gather(downproj, fsdp_size)

        length = hidden_in.shape[0]
        position = jnp.arange(length, dtype=jnp.int32)
        piece_ids = (
            jnp.sum((piece_starts[0][None, :] <= position[:, None]).astype(jnp.int32), axis=1) - 1
        )
        context = (table_full, piece_ids)
        resid_in = hidden_in.astype(jnp.float32)
        normed_one = rms_scale(resid_in, gain_one.astype(jnp.float32)).astype(jnp.bfloat16)
        qkv_one = product(normed_one, self_full).astype(jnp.bfloat16)
        query_one = qkv_one[:, :width]
        key_one = qkv_one[:, width : 2 * width]
        value_one = qkv_one[:, 2 * width :]
        mixed_one, lse_one = attend_forward(query_one, key_one, value_one, context)
        after_self = resid_in + product(mixed_one, self_proj)
        normed_two = rms_scale(after_self, gain_two.astype(jnp.float32)).astype(jnp.bfloat16)
        query_two = product(normed_two, cross_query).astype(jnp.bfloat16)
        kv_two = product(encoder_states, cross_kv).astype(jnp.bfloat16)
        key_two = kv_two[:, :width]
        value_two = kv_two[:, width:]
        mixed_two, lse_two = attend_forward(query_two, key_two, value_two, None)
        after_cross = after_self + product(mixed_two, cross_proj)
        normed_three = rms_scale(after_cross, gain_three.astype(jnp.float32)).astype(jnp.bfloat16)
        gate_upper = product(normed_three, gate_up)
        gate_pre = gate_upper[:, :ff_width]
        upper_pre = gate_upper[:, ff_width:]
        inner = gated(gate_pre, upper_pre).astype(jnp.bfloat16)
        layer_out = (after_cross + product(inner, down_full)).astype(jnp.bfloat16)

        def reduce_rows(packed):
            return lax.psum_scatter(
                packed.astype(jnp.bfloat16), ("fsdp", "replica"), scatter_dimension=0, tiled=True
            )

        downproj_grad = left_product(inner, output_grad)
        inner_grad = right_product(output_grad, down_full)
        gated_value, pull_gate = jax.vjp(gated, gate_pre, upper_pre)
        gate_grad, upper_grad = pull_gate(inner_grad)
        gate_upper_low = jnp.concatenate(
            [gate_grad.astype(jnp.bfloat16), upper_grad.astype(jnp.bfloat16)], axis=1
        )
        gate_up_grad = left_product(normed_three, gate_upper_low)
        ffn_packed = jnp.concatenate(
            [gate_up_grad, downproj_grad.reshape(width, ff_width)], axis=1
        ).astype(jnp.bfloat16)
        normed_grad = right_product(gate_upper_low, gate_up)
        norm_value, pull_norm = jax.vjp(rms_scale, after_cross, gain_three.astype(jnp.float32))
        back_resid, gainffn_grad = pull_norm(normed_grad)
        ffn_packed, back_resid = lax.optimization_barrier((ffn_packed, back_resid))
        ffn_part = reduce_rows(ffn_packed)
        resid_grad = output_grad.astype(jnp.float32) + back_resid
        branch_low = resid_grad.astype(jnp.bfloat16)
        crossproj_grad = left_product(mixed_two, branch_low)
        mixed_grad = right_product(branch_low, cross_proj).astype(jnp.bfloat16)
        query_back, key_back, value_back, unused_table = attend_backward(
            query_two, key_two, value_two, mixed_grad, lse_two, None
        )
        crossquery_grad = left_product(normed_two, query_back)
        kv_back = jnp.concatenate([key_back, value_back], axis=1)
        crosskv_grad = left_product(encoder_states, kv_back)
        encoder_grad = right_product(kv_back, cross_kv)
        normed_grad = right_product(query_back, cross_query)
        norm_value, pull_norm = jax.vjp(rms_scale, after_self, gain_two.astype(jnp.float32))
        back_resid, gaincross_grad = pull_norm(normed_grad)
        resid_grad = resid_grad + back_resid
        branch_low = resid_grad.astype(jnp.bfloat16)
        selfproj_grad = left_product(mixed_one, branch_low)
        mixed_grad = right_product(branch_low, self_proj).astype(jnp.bfloat16)
        query_back, key_back, value_back, reltable_grad = attend_backward(
            query_one, key_one, value_one, mixed_grad, lse_one, context
        )
        qkv_back = jnp.concatenate([query_back, key_back, value_back], axis=1)
        selfqkv_grad = left_product(normed_one, qkv_back)
        normed_grad = right_product(qkv_back, self_full)
        norm_value, pull_norm = jax.vjp(rms_scale, resid_in, gain_one.astype(jnp.float32))
        back_resid, gainself_grad = pull_norm(normed_grad)
        hidden_grad = resid_grad + back_resid

        table_block_rows = table_rows
        table_cols = jnp.pad(
            reltable_grad.reshape(fsdp_size, table_block_rows, HEADS),
            ((0, 0), (0, shard_rows - table_block_rows), (0, 0)),
        ).reshape(width, HEADS)
        extra = jnp.concatenate(
            [
                gainffn_grad[:, None],
                gaincross_grad[:, None],
                gainself_grad[:, None],
                table_cols,
                jnp.zeros((width, 128 - 3 - HEADS), jnp.float32),
            ],
            axis=1,
        )
        attn_parts = [
            [crossproj_grad, crossquery_grad],
            [crosskv_grad[:, :width]],
            [crosskv_grad[:, width:]],
            [selfproj_grad, extra],
            [selfqkv_grad[:, : 2 * width]],
            [selfqkv_grad[:, 2 * width :]],
        ]
        attn_owned, ffn_part = tree_reduce(
            attn_parts, fsdp_size, replica_size, carry=ffn_part, shifts=[0, 2, 0, 3, 1, 2]
        )
        ffn_owned = lax.all_gather(ffn_part, "replica", axis=0, tiled=True)
        cross_owned = attn_owned[:, : 4 * width]
        extra_owned = attn_owned[:, 5 * width : 5 * width + 128].astype(jnp.float32)
        self_owned = jnp.concatenate(
            [attn_owned[:, 4 * width : 5 * width], attn_owned[:, 5 * width + 128 :]], axis=1
        )

        as_f32 = lambda v: v.astype(jnp.float32)
        return (
            layer_out,
            hidden_grad,
            encoder_grad,
            as_f32(self_owned[:, width : 2 * width]),
            as_f32(self_owned[:, 2 * width : 3 * width]),
            as_f32(self_owned[:, 3 * width : 4 * width]),
            as_f32(self_owned[:, 0:width]),
            as_f32(cross_owned[:, width : 2 * width]),
            as_f32(cross_owned[:, 2 * width : 3 * width]),
            as_f32(cross_owned[:, 3 * width : 4 * width]),
            as_f32(cross_owned[:, 0:width]),
            as_f32(ffn_owned[:, 0:ff_width]),
            as_f32(ffn_owned[:, ff_width : 2 * ff_width]),
            as_f32(ffn_owned[:, 2 * ff_width :].reshape(-1, width)),
            extra_owned[:, 2],
            extra_owned[:, 1],
            extra_owned[:, 0],
            extra_owned[:table_block_rows, 3 : 3 + HEADS],
        )

    return on_device


def solution(mesh):
    placed = (
        P(("fsdp", "replica"), None),
        P(("fsdp", "replica"), None),
        P(("fsdp", "replica"), None),
        P(("fsdp", "replica"), None),
        P("fsdp", None),
        P("fsdp", None),
        P("fsdp", None),
        P("fsdp", None),
        P("fsdp", None),
        P("fsdp", None),
        P("fsdp", None),
        P("fsdp", None),
        P("fsdp", None),
        P("fsdp", None),
        P("fsdp", None),
        P("fsdp"),
        P("fsdp"),
        P("fsdp"),
        P("fsdp", None),
    )
    return jax.shard_map(
        make_on_device(mesh.shape["fsdp"], mesh.shape["replica"]),
        mesh=mesh,
        in_specs=placed,
        out_specs=(
            P(("fsdp", "replica"), None),
            P(("fsdp", "replica"), None),
            P(("fsdp", "replica"), None),
            P("fsdp", None),
            P("fsdp", None),
            P("fsdp", None),
            P("fsdp", None),
            P("fsdp", None),
            P("fsdp", None),
            P("fsdp", None),
            P("fsdp", None),
            P("fsdp", None),
            P("fsdp", None),
            P("fsdp", None),
            P("fsdp"),
            P("fsdp"),
            P("fsdp"),
            P("fsdp", None),
        ),
        check_vma=False,
    )
```
